32 devices in a mesh: ctx: 16 (over z, x, core), head: 2 (over y).
Axes of the slice: x: 2, y: 2, z: 4, core: 2. Of those that a mesh axis runs over, the one named last changes fastest.
Arguments:
- attn_q: bfloat16 [4096, 8192], P(('ctx', 'head')), may hold values from -8 to 8
- attn_k: bfloat16 [4096, 8192], P(('ctx', 'head')), may hold values from -8 to 8
- attn_v: bfloat16 [4096, 8192], P(('ctx', 'head')), may hold values from -5 to 5
- attn_dout: bfloat16 [4096, 8192], P(('ctx', 'head')), may hold values from -5 to 5
- doc_ids: int32 [4096], replicated, may hold values from 0 to 7, never falling along the last dimension, each value on 1 to 1024 neighbouring positions
Outputs:
- attn_dq: bfloat16 [4096, 8192], P('ctx', 'head')
- attn_dk: bfloat16 [4096, 8192], P('ctx', 'head')
- attn_dv: bfloat16 [4096, 8192], P('ctx', 'head')
The draws below stay inside these ranges and needn't reach their ends.
Inputs may be any that keep to these rules, and one draw needn't show every extreme that they name: `doc_ids`: document numbers never fall along the window; each document holds 1 to 1024 consecutive tokens, and one holds exactly 1024.
All inputs are finite; a program needn't handle non-finite values.
Results may differ from the reference program's by a relative error of at most 0.0088.
Values may be sent and summed in bfloat16 or wider, within the bound.
No kernel may reach another device: no remote copies, remote signals or barrier semaphores. Data moves between devices by JAX's collectives and lax.ppermute only.
A program may use at most 256 MiB of HBM per device.

```python
import math
import jax
import jax.numpy as jnp
import numpy as np
from jax import lax

HEAD_DIM = 128
HEADS = 64
REACH = 4
TOK_DEV = 256
TOKENS = 4096
MAX_DOC = 1024
DOCS = 8


def paired_rows(key):
    rows = TOKENS
    cols = HEADS * HEAD_DIM
    queries = jnp.clip(jax.random.normal(jax.random.fold_in(key, 201), (rows, cols), jnp.float32), -4.0, 4.0)
    keys = jnp.clip(jax.random.normal(jax.random.fold_in(key, 202), (rows, cols), jnp.float32), -4.0, 4.0)
    return (queries, keys)


def draw_attn_q(key, part):
    return paired_rows(key)[0].astype(jnp.bfloat16)


def draw_attn_k(key, part):
    return paired_rows(key)[1].astype(jnp.bfloat16)


def steps_of(own_key, extent, shards, low, high):
    loudness, own = 1.0, jax.random.fold_in(own_key, 6)
    for position, shards_of in shards:
        heights = jnp.exp(jax.random.uniform(jax.random.fold_in(own, position), (shards_of,), jnp.float32, low / len(shards), high / len(shards)))
        loudness = loudness * jnp.repeat(heights, extent[position] // shards_of).reshape([-1 if axis == position else 1 for axis in range(len(extent))])
    return loudness


def split_up(count, total, most, slope):
    loads = [(1 << 20) // math.isqrt(standing ** slope) + 1 for standing in range(2, count + 1)]
    surplus, holding = total - most - (count - 1), [1] * (count - 1)
    while surplus > 0:
        candidates = [i for i in range(count - 1) if holding[i] < most]
        pool, left = sum([loads[i] for i in candidates]), surplus
        for i in candidates:
            addition = min(most - holding[i], max(1, left * loads[i] // pool), surplus)
            holding[i] = holding[i] + addition
            surplus = surplus - addition
    return np.array([most] + holding)


def uneven(own_key, amount, total, bound, skew):
    if amount == 2:
        one = jax.random.randint(own_key, (), max(1, total - bound), min(bound, total - 1) + 1)
        return jnp.stack([one, total - one])
    tallies = jnp.asarray(split_up(amount, total, bound, skew), jnp.int32)
    couples = (amount - 1) // 2
    source_of, sink = tallies[1:1 + 2 * couples:2], tallies[2:2 + 2 * couples:2]
    slack = jnp.minimum(source_of - 1, bound - sink)
    passed = jax.random.randint(jax.random.fold_in(own_key, 1), (couples,), 0, 1 << 20) % (slack + 1)
    tallies = tallies.at[1:1 + 2 * couples:2].set(source_of - passed).at[2:2 + 2 * couples:2].set(sink + passed)
    return tallies[jax.random.permutation(jax.random.fold_in(own_key, 2), amount)]


def scatter_about(stream_key, shape, spread, limit, pieces=(), held_as=jnp.bfloat16):
    array = spread * jax.random.normal(stream_key, shape, jnp.float32)
    if pieces:
        array = array * steps_of(stream_key, shape, pieces, -0.22, 0.18)
    return jnp.clip(array, -limit, limit).astype(held_as)


def setup_inputs(seed: int = 0) -> dict:
    streams_of = jax.random.split(jax.random.key(seed), 6)
    return {
        "attn_q": draw_attn_q(jax.random.fold_in(streams_of[5], 71), 0),
        "attn_k": draw_attn_k(jax.random.fold_in(streams_of[5], 71), 0),
        "attn_v": scatter_about(streams_of[2], (TOKENS, HEADS * HEAD_DIM), 1.0, 5.0, ((0, 32),)),
        "attn_dout": scatter_about(streams_of[3], (TOKENS, HEADS * HEAD_DIM), 1.0, 5.0, ((0, 32),)),
        "doc_ids": jnp.searchsorted(jnp.cumsum(uneven(streams_of[4], DOCS, TOKENS, MAX_DOC, 1)), jnp.arange(TOKENS), side="right").astype(jnp.int32),
    }


masked_value = -1e30


def rounded(values):
    return lax.optimization_barrier(values.astype(jnp.bfloat16)).astype(jnp.float32)


def reference(attn_q, attn_k, attn_v, attn_dout, doc_ids):
    scale = HEAD_DIM ** -0.5
    shape3 = (TOKENS, HEADS, HEAD_DIM)
    q_all = attn_q.reshape(shape3)
    k_all = attn_k.reshape(shape3)
    v_all = attn_v.reshape(shape3)
    d_all = attn_dout.reshape(shape3)
    window = (REACH + 1) * TOK_DEV

    def step(carry, block):
        dk_acc, dv_acc = carry
        q_start = (block * TOK_DEV).astype(jnp.int32)
        k_start = jnp.maximum(q_start - REACH * TOK_DEV, 0).astype(jnp.int32)
        q_blk = lax.dynamic_slice_in_dim(q_all, q_start, TOK_DEV, 0).astype(jnp.float32)
        d_blk = lax.dynamic_slice_in_dim(d_all, q_start, TOK_DEV, 0).astype(jnp.float32)
        k_win = lax.dynamic_slice_in_dim(k_all, k_start, window, 0).astype(jnp.float32)
        v_win = lax.dynamic_slice_in_dim(v_all, k_start, window, 0).astype(jnp.float32)
        q_pos = q_start + jnp.arange(TOK_DEV, dtype=jnp.int32)
        k_pos = k_start + jnp.arange(window, dtype=jnp.int32)
        q_doc = lax.dynamic_slice_in_dim(doc_ids, q_start, TOK_DEV)
        k_doc = lax.dynamic_slice_in_dim(doc_ids, k_start, window)
        mask = (k_pos[None, :] <= q_pos[:, None]) & (k_doc[None, :] == q_doc[:, None])
        raw = jnp.einsum('qhd,khd->hqk', q_blk, k_win) * scale
        scores = jnp.where(mask[None], raw, masked_value)
        top = jnp.max(scores, axis=2, keepdims=True)
        lse = top + jnp.log(jnp.sum(jnp.exp(scores - top), axis=2, keepdims=True))
        probs = jnp.where(mask[None], jnp.exp(scores - lse), 0.0)
        probs_bf = rounded(probs)
        attn_out = jnp.einsum('hqk,khd->qhd', probs_bf, v_win)
        delta = jnp.sum(d_blk * attn_out, axis=2).T
        dprobs = jnp.einsum('qhd,khd->hqk', d_blk, v_win)
        dscores = rounded(probs * (dprobs - delta[:, :, None]))
        dq_blk = (jnp.einsum('hqk,khd->qhd', dscores, k_win) * scale).astype(jnp.bfloat16)
        dk_part = jnp.einsum('hqk,qhd->khd', dscores, q_blk) * scale
        dv_part = jnp.einsum('hqk,qhd->khd', probs_bf, d_blk)
        dk_acc = lax.dynamic_update_slice_in_dim(dk_acc, lax.dynamic_slice_in_dim(dk_acc, k_start, window, 0) + dk_part, k_start, 0)
        dv_acc = lax.dynamic_update_slice_in_dim(dv_acc, lax.dynamic_slice_in_dim(dv_acc, k_start, window, 0) + dv_part, k_start, 0)
        return (dk_acc, dv_acc), dq_blk

    zeros = jnp.zeros(shape3, jnp.float32)
    (dk_acc, dv_acc), dq_blocks = lax.scan(step, (zeros, zeros), jnp.arange(TOKENS // TOK_DEV, dtype=jnp.int32))
    width = HEADS * HEAD_DIM
    attn_dq = dq_blocks.reshape(TOKENS, width)
    attn_dk = dk_acc.astype(jnp.bfloat16).reshape(TOKENS, width)
    attn_dv = dv_acc.astype(jnp.bfloat16).reshape(TOKENS, width)
    return attn_dq, attn_dk, attn_dv
```

```python
import jax
import jax.numpy as jnp
from jax import lax
from jax.experimental import pallas as pl
from jax.experimental.pallas import tpu as pltpu
from jax.sharding import PartitionSpec as P

HEAD_DIM = 128
MAX_DOC = 1024

masked_value = -1e30


def shifted(value, axis, steps):
    count = lax.axis_size(axis)
    leading, last = (max(0, -steps), min(count, count - steps))
    return lax.ppermute(value, axis, [(source, source + steps) for source in range(leading, last)])


def _row(col, tok):
    return jnp.transpose(jnp.broadcast_to(col, (tok, 128)))[0:1, :]


def _query_side_kernel(nblk, tok, scale):
    def kernel(*refs):
        q_ref, d_ref = refs[0], refs[1]
        k_refs = refs[2:2 + nblk]
        v_refs = refs[2 + nblk:2 + 2 * nblk]
        bias_ref = refs[2 + 2 * nblk]
        dq_ref, ld_ref = refs[3 + 2 * nblk], refs[4 + 2 * nblk]
        q = q_ref[...]
        d = d_ref[...]
        logits = []
        for j in range(nblk):
            raw = lax.dot_general(q, k_refs[j][...], (((1,), (1,)), ((), ())),
                                  preferred_element_type=jnp.float32)
            logits.append(raw * scale + bias_ref[:, j * tok:(j + 1) * tok])
        top = logits[0].max(axis=1, keepdims=True)
        for j in range(1, nblk):
            top = jnp.maximum(top, logits[j].max(axis=1, keepdims=True))
        denom = jnp.exp(logits[0] - top).sum(axis=1, keepdims=True)
        for j in range(1, nblk):
            denom = denom + jnp.exp(logits[j] - top).sum(axis=1, keepdims=True)
        lse = top + jnp.log(denom)
        probs = [jnp.exp(item - lse) for item in logits]
        out = None
        for j in range(nblk):
            part = jnp.dot(probs[j].astype(jnp.bfloat16), v_refs[j][...],
                           preferred_element_type=jnp.float32)
            out = part if out is None else out + part
        delta = (d.astype(jnp.float32) * out).sum(axis=1, keepdims=True)
        dq = None
        for j in range(nblk):
            dprobs = lax.dot_general(d, v_refs[j][...], (((1,), (1,)), ((), ())),
                                     preferred_element_type=jnp.float32)
            dscores = (probs[j] * (dprobs - delta)).astype(jnp.bfloat16)
            part = jnp.dot(dscores, k_refs[j][...], preferred_element_type=jnp.float32)
            dq = part if dq is None else dq + part
        dq_ref[...] = (dq * scale).astype(dq_ref.dtype)
        ld_ref[0:1, :] = _row(lse, tok)
        ld_ref[1:2, :] = _row(delta, tok)

    return kernel


def _key_side_kernel(nblk, tok, scale):
    def kernel(*refs):
        k_ref, v_ref = refs[0], refs[1]
        q_refs = refs[2:2 + nblk]
        d_refs = refs[2 + nblk:2 + 2 * nblk]
        ld_refs = refs[2 + 2 * nblk:2 + 3 * nblk]
        bias_ref = refs[2 + 3 * nblk]
        dk_ref, dv_ref = refs[3 + 3 * nblk], refs[4 + 3 * nblk]
        k = k_ref[...]
        v = v_ref[...]
        dk = None
        dv = None
        for j in range(nblk):
            q = q_refs[j][...]
            d = d_refs[j][...]
            lse = ld_refs[j][0:1, :]
            delta = ld_refs[j][1:2, :]
            raw = lax.dot_general(k, q, (((1,), (1,)), ((), ())),
                                  preferred_element_type=jnp.float32)
            logit = raw * scale + bias_ref[:, j * tok:(j + 1) * tok]
            prob = jnp.exp(logit - lse)
            dprobs = lax.dot_general(v, d, (((1,), (1,)), ((), ())),
                                     preferred_element_type=jnp.float32)
            dscores = (prob * (dprobs - delta)).astype(jnp.bfloat16)
            part_k = jnp.dot(dscores, q, preferred_element_type=jnp.float32)
            part_v = jnp.dot(prob.astype(jnp.bfloat16), d, preferred_element_type=jnp.float32)
            dk = part_k if dk is None else dk + part_k
            dv = part_v if dv is None else dv + part_v
        dk_ref[...] = (dk * scale).astype(dk_ref.dtype)
        dv_ref[...] = dv.astype(dv_ref.dtype)

    return kernel


def per_device(attn_q, attn_k, attn_v, attn_dout, doc_ids):
    query, keys, values, dout = (
        lax.all_to_all(attn_q, "head", split_axis=1, concat_axis=0, tiled=True),
        lax.all_to_all(attn_k, "head", split_axis=1, concat_axis=0, tiled=True),
        lax.all_to_all(attn_v, "head", split_axis=1, concat_axis=0, tiled=True),
        lax.all_to_all(attn_dout, "head", split_axis=1, concat_axis=0, tiled=True),
    )
    tok = query.shape[0]
    width = query.shape[1]
    heads_local = width // HEAD_DIM
    ctx_count = lax.axis_size("ctx")
    ctx_pos = lax.axis_index("ctx")
    scale = HEAD_DIM ** (-0.5)
    reach = min(-(-(MAX_DOC - 1) // tok), ctx_count - 1)
    nblk = reach + 1
    row_ids = jnp.arange(tok, dtype=jnp.int32)

    def block_info(owner):
        start = jnp.clip(owner * tok, 0, tok * (ctx_count - 1))
        docs = lax.dynamic_slice_in_dim(doc_ids, start, tok)
        valid = (owner >= 0) & (owner < ctx_count)
        return (owner * tok + row_ids, docs, valid)

    def allowed(q_info, k_info):
        causal = k_info[0][None, :] <= q_info[0][:, None]
        same_doc = k_info[1][None, :] == q_info[1][:, None]
        return causal & same_doc & q_info[2] & k_info[2]

    def bias_of(mask):
        return jnp.where(mask, 0.0, masked_value).astype(jnp.float32)

    own = block_info(ctx_pos)
    key_list, value_list, q_masks = [], [], []
    for shift in range(reach, 0, -1):
        far_k, far_v = shifted((keys, values), "ctx", shift)
        key_list.append(far_k)
        value_list.append(far_v)
        q_masks.append(allowed(own, block_info(ctx_pos - shift)))
    key_list.append(keys)
    value_list.append(values)
    q_masks.append(allowed(own, own))
    q_bias = bias_of(jnp.concatenate(q_masks, axis=1))

    query_list, dout_list, k_masks = [query], [dout], [allowed(own, own).T]
    for shift in range(1, reach + 1):
        far_q, far_d = shifted((query, dout), "ctx", -shift)
        query_list.append(far_q)
        dout_list.append(far_d)
        k_masks.append(allowed(block_info(ctx_pos + shift), own).T)
    k_bias = bias_of(jnp.concatenate(k_masks, axis=1))

    col_spec = pl.BlockSpec((tok, HEAD_DIM), lambda h: (0, h))
    bias_spec = pl.BlockSpec((tok, nblk * tok), lambda h: (0, 0))
    ld_spec = pl.BlockSpec((None, 2, tok), lambda h: (h, 0, 0))
    params = pltpu.CompilerParams(dimension_semantics=("arbitrary",))

    dq, ld = pl.pallas_call(
        _query_side_kernel(nblk, tok, scale),
        out_shape=(
            jax.ShapeDtypeStruct((tok, width), jnp.bfloat16),
            jax.ShapeDtypeStruct((heads_local, 2, tok), jnp.float32),
        ),
        grid=(heads_local,),
        in_specs=[col_spec] * (2 + 2 * nblk) + [bias_spec],
        out_specs=(col_spec, ld_spec),
        compiler_params=params,
        name="attn_query_side",
    )(query, dout, *key_list, *value_list, q_bias)

    ld_list = [ld]
    for shift in range(1, reach + 1):
        ld_list.append(shifted(ld, "ctx", -shift))

    dk, dv = pl.pallas_call(
        _key_side_kernel(nblk, tok, scale),
        out_shape=(
            jax.ShapeDtypeStruct((tok, width), jnp.bfloat16),
            jax.ShapeDtypeStruct((tok, width), jnp.bfloat16),
        ),
        grid=(heads_local,),
        in_specs=[col_spec] * (2 + 2 * nblk) + [ld_spec] * nblk + [bias_spec],
        out_specs=(col_spec, col_spec),
        compiler_params=params,
        name="attn_key_side",
    )(keys, values, *query_list, *dout_list, *ld_list, k_bias)
    return (dq, dk, dv)


def solution(mesh):
    return jax.shard_map(
        per_device,
        mesh=mesh,
        in_specs=(
            P(("ctx", "head"), None),
            P(("ctx", "head"), None),
            P(("ctx", "head"), None),
            P(("ctx", "head"), None),
            P(),
        ),
        out_specs=(P("ctx", "head"), P("ctx", "head"), P("ctx", "head")),
        check_vma=False,
    )
```

```python
import jax
import jax.numpy as jnp
import numpy as np
from jax import lax
from jax.experimental import pallas as pl
from jax.experimental.pallas import tpu as pltpu
from jax.sharding import Mesh
from jax.sharding import PartitionSpec as P

HEAD_DIM = 128
MAX_DOC = 1024
PLANE_TOKENS = 1024
TILE = 256

masked_value = -1e30


def shifted(value, axis, steps):
    count = lax.axis_size(axis)
    leading, last = (max(0, -steps), min(count, count - steps))
    return lax.ppermute(value, axis, [(source, source + steps) for source in range(leading, last)])


def _row(col, tok):
    return jnp.transpose(jnp.broadcast_to(col, (tok, 128)))[0:1, :]


def _query_side_kernel(nblk, scale):
    def kernel(*refs):
        q_ref, d_ref = refs[0], refs[1]
        k_refs = refs[2:2 + nblk]
        v_refs = refs[2 + nblk:2 + 2 * nblk]
        bias_ref = refs[2 + 2 * nblk]
        dq_ref, ld_ref = refs[3 + 2 * nblk], refs[4 + 2 * nblk]
        q = q_ref[...]
        d = d_ref[...]
        logits = []
        for j in range(nblk):
            raw = lax.dot_general(q, k_refs[j][...], (((1,), (1,)), ((), ())),
                                  preferred_element_type=jnp.float32)
            logits.append(raw * scale + bias_ref[:, j * TILE:(j + 1) * TILE])
        top = logits[0].max(axis=1, keepdims=True)
        for j in range(1, nblk):
            top = jnp.maximum(top, logits[j].max(axis=1, keepdims=True))
        denom = jnp.exp(logits[0] - top).sum(axis=1, keepdims=True)
        for j in range(1, nblk):
            denom = denom + jnp.exp(logits[j] - top).sum(axis=1, keepdims=True)
        lse = top + jnp.log(denom)
        probs = [jnp.exp(item - lse) for item in logits]
        out = None
        for j in range(nblk):
            part = jnp.dot(probs[j].astype(jnp.bfloat16), v_refs[j][...],
                           preferred_element_type=jnp.float32)
            out = part if out is None else out + part
        delta = (d.astype(jnp.float32) * out).sum(axis=1, keepdims=True)
        dq = None
        for j in range(nblk):
            dprobs = lax.dot_general(d, v_refs[j][...], (((1,), (1,)), ((), ())),
                                     preferred_element_type=jnp.float32)
            dscores = (probs[j] * (dprobs - delta)).astype(jnp.bfloat16)
            part = jnp.dot(dscores, k_refs[j][...], preferred_element_type=jnp.float32)
            dq = part if dq is None else dq + part
        dq_ref[...] = (dq * scale).astype(dq_ref.dtype)
        ld_ref[0:1, :] = _row(lse, TILE)
        ld_ref[1:2, :] = _row(delta, TILE)

    return kernel


def _key_side_kernel(nblk, scale):
    def kernel(*refs):
        k_ref, v_ref = refs[0], refs[1]
        q_refs = refs[2:2 + nblk]
        d_refs = refs[2 + nblk:2 + 2 * nblk]
        ld_refs = refs[2 + 2 * nblk:2 + 3 * nblk]
        bias_ref = refs[2 + 3 * nblk]
        dk_ref, dv_ref = refs[3 + 3 * nblk], refs[4 + 3 * nblk]
        k = k_ref[...]
        v = v_ref[...]
        dk = None
        dv = None
        for j in range(nblk):
            q = q_refs[j][...]
            d = d_refs[j][...]
            lse = ld_refs[j][0:1, :]
            delta = ld_refs[j][1:2, :]
            raw = lax.dot_general(k, q, (((1,), (1,)), ((), ())),
                                  preferred_element_type=jnp.float32)
            logit = raw * scale + bias_ref[:, j * TILE:(j + 1) * TILE]
            prob = jnp.exp(logit - lse)
            dprobs = lax.dot_general(v, d, (((1,), (1,)), ((), ())),
                                     preferred_element_type=jnp.float32)
            dscores = (prob * (dprobs - delta)).astype(jnp.bfloat16)
            part_k = jnp.dot(dscores, q, preferred_element_type=jnp.float32)
            part_v = jnp.dot(prob.astype(jnp.bfloat16), d, preferred_element_type=jnp.float32)
            dk = part_k if dk is None else dk + part_k
            dv = part_v if dv is None else dv + part_v
        dk_ref[...] = (dk * scale).astype(dk_ref.dtype)
        dv_ref[...] = dv.astype(dv_ref.dtype)

    return kernel


def _plan(tok_in, ctx_n, head_n):
    clo_n = 1
    while (clo_n * 2 <= ctx_n and ctx_n % (clo_n * 2) == 0
           and tok_in * clo_n * head_n < PLANE_TOKENS):
        clo_n *= 2
    return clo_n


def _per_device(clo_n, attn_q, attn_k, attn_v, attn_dout, doc_ids):
    tok_in, full_width = attn_q.shape
    head_n = lax.axis_size("head")
    chi_n = lax.axis_size("chi")
    group = clo_n * head_n
    width = full_width // group
    heads_p = width // HEAD_DIM
    plane = tok_in * group
    n_tok = doc_ids.shape[0]
    scale = HEAD_DIM ** (-0.5)
    reach = min(-(-(MAX_DOC - 1) // plane), chi_n - 1)
    tile_reach = -(-(MAX_DOC - 1) // TILE)
    nblk = tile_reach + 1
    n_tiles = plane // TILE
    chi = lax.axis_index("chi")
    plane_start = chi * plane

    def to_plane(x):
        x = x.reshape(tok_in, head_n, clo_n, width).transpose(0, 2, 1, 3).reshape(tok_in, full_width)
        return lax.all_to_all(x, ("clo", "head"), split_axis=1, concat_axis=0, tiled=True)

    keys = to_plane(attn_k)
    values = to_plane(attn_v)
    query = to_plane(attn_q)
    dout = to_plane(attn_dout)

    k_parts, v_parts = [], []
    for shift in range(reach, 0, -1):
        far_k, far_v = shifted((keys, values), "chi", shift)
        k_parts.append(far_k)
        v_parts.append(far_v)
    k_win = jnp.concatenate(k_parts + [keys], axis=0)
    v_win = jnp.concatenate(v_parts + [values], axis=0)

    q_parts, d_parts = [], []
    for shift in range(1, reach + 1):
        far_q, far_d = shifted((query, dout), "chi", -shift)
        q_parts.append(far_q)
        d_parts.append(far_d)
    q_win = jnp.concatenate([query] + q_parts, axis=0)
    d_win = jnp.concatenate([dout] + d_parts, axis=0)

    pad = (reach + 1) * plane
    docs_pad = jnp.concatenate([
        jnp.full((pad,), -1, jnp.int32), doc_ids.astype(jnp.int32), jnp.full((pad,), -1, jnp.int32)])
    span = nblk * TILE
    cols = jnp.arange(span, dtype=jnp.int32)
    rows = jnp.arange(TILE, dtype=jnp.int32)
    q_bias, k_bias = [], []
    for i in range(n_tiles):
        t_start = plane_start + i * TILE
        own_doc = lax.dynamic_slice_in_dim(docs_pad, t_start + pad, TILE)
        own_pos = t_start + rows
        k_start = t_start - tile_reach * TILE
        k_doc = lax.dynamic_slice_in_dim(docs_pad, k_start + pad, span)
        k_pos = k_start + cols
        mask = (k_pos[None, :] <= own_pos[:, None]) & (k_doc[None, :] == own_doc[:, None])
        q_bias.append(jnp.where(mask, 0.0, masked_value).astype(jnp.float32))
        q_doc = lax.dynamic_slice_in_dim(docs_pad, t_start + pad, span)
        q_pos = t_start + cols
        mask = (own_pos[:, None] <= q_pos[None, :]) & (own_doc[:, None] == q_doc[None, :])
        k_bias.append(jnp.where(mask, 0.0, masked_value).astype(jnp.float32))
    q_bias = jnp.concatenate(q_bias, axis=0)
    k_bias = jnp.concatenate(k_bias, axis=0)

    own_spec = pl.BlockSpec((TILE, HEAD_DIM), lambda i, h: (i, h))
    base = reach * n_tiles - tile_reach

    def kwin_spec(j):
        return pl.BlockSpec((TILE, HEAD_DIM), lambda i, h: (base + i + j, h))

    def qwin_spec(j):
        return pl.BlockSpec((TILE, HEAD_DIM), lambda i, h: (i + j, h))

    def ldwin_spec(j):
        return pl.BlockSpec((None, 2, TILE), lambda i, h: (h, 0, i + j))

    bias_spec = pl.BlockSpec((TILE, span), lambda i, h: (i, 0))
    ld_spec = pl.BlockSpec((None, 2, TILE), lambda i, h: (h, 0, i))
    params = pltpu.CompilerParams(dimension_semantics=("arbitrary", "arbitrary"))
    grid = (n_tiles, heads_p)

    dq, ld = pl.pallas_call(
        _query_side_kernel(nblk, scale),
        out_shape=(
            jax.ShapeDtypeStruct((plane, width), jnp.bfloat16),
            jax.ShapeDtypeStruct((heads_p, 2, plane), jnp.float32),
        ),
        grid=grid,
        in_specs=[own_spec, own_spec] + [kwin_spec(j) for j in range(nblk)] * 2 + [bias_spec],
        out_specs=(own_spec, ld_spec),
        compiler_params=params,
        name="attn_query_side",
    )(query, dout, *([k_win] * nblk), *([v_win] * nblk), q_bias)

    ld_parts = [ld]
    for shift in range(1, reach + 1):
        ld_parts.append(shifted(ld, "chi", -shift))
    ld_win = jnp.concatenate(ld_parts, axis=2)

    dk, dv = pl.pallas_call(
        _key_side_kernel(nblk, scale),
        out_shape=(
            jax.ShapeDtypeStruct((plane, width), jnp.bfloat16),
            jax.ShapeDtypeStruct((plane, width), jnp.bfloat16),
        ),
        grid=grid,
        in_specs=[own_spec, own_spec] + [qwin_spec(j) for j in range(nblk)] * 2
        + [ldwin_spec(j) for j in range(nblk)] + [bias_spec],
        out_specs=(own_spec, own_spec),
        compiler_params=params,
        name="attn_key_side",
    )(keys, values, *([q_win] * nblk), *([d_win] * nblk), *([ld_win] * nblk), k_bias)

    def from_plane(x):
        return lax.all_to_all(x, "clo", split_axis=0, concat_axis=1, tiled=True)

    return (from_plane(dq), from_plane(dk), from_plane(dv))


def solution(mesh):
    ctx_n, head_n = mesh.devices.shape
    def fn(attn_q, attn_k, attn_v, attn_dout, doc_ids):
        tok_in = attn_q.shape[0] // (ctx_n * head_n)
        clo_n = _plan(tok_in, ctx_n, head_n)
        chi_n = ctx_n // clo_n
        sub = Mesh(np.asarray(mesh.devices).reshape(chi_n, clo_n, head_n), ("chi", "clo", "head"))
        inner = jax.shard_map(
            lambda *a: _per_device(clo_n, *a),
            mesh=sub,
            in_specs=(
                P(("chi", "clo", "head"), None),
                P(("chi", "clo", "head"), None),
                P(("chi", "clo", "head"), None),
                P(("chi", "clo", "head"), None),
                P(),
            ),
            out_specs=(P(("chi", "clo"), "head"), P(("chi", "clo"), "head"), P(("chi", "clo"), "head")),
            check_vma=False,
        )
        return inner(attn_q, attn_k, attn_v, attn_dout, doc_ids)
    return fn
```

```python
import jax
import jax.numpy as jnp
import numpy as np
from jax import lax
from jax.experimental import pallas as pl
from jax.experimental.pallas import tpu as pltpu
from jax.sharding import Mesh
from jax.sharding import PartitionSpec as P

HEAD_DIM = 128
MAX_DOC = 1024
PLANE_TOKENS = 1024
TILE = 256

masked_value = -1e30


def shifted(value, axis, steps):
    count = lax.axis_size(axis)
    leading, last = (max(0, -steps), min(count, count - steps))
    return lax.ppermute(value, axis, [(source, source + steps) for source in range(leading, last)])


def _row(col, tok):
    return jnp.transpose(jnp.broadcast_to(col, (tok, 128)))[0:1, :]


def _query_side_kernel(reach, n_tiles, tile_reach, scale):
    nblk = tile_reach + 1
    npl = reach + 1

    def kernel(flags_ref, *refs):
        q_ref, d_ref = refs[0], refs[1]
        k_refs = refs[2:2 + npl]
        v_refs = refs[2 + npl:2 + 2 * npl]
        bias_ref = refs[2 + 2 * npl]
        dq_ref, ld_ref = refs[3 + 2 * npl], refs[4 + 2 * npl]
        s_scr, m_scr, l_scr, o_scr = refs[5 + 2 * npl:]

        def block(i, j):
            b = reach * n_tiles + i - tile_reach + j
            rows = pl.ds((b % n_tiles) * TILE, TILE)
            return k_refs[b // n_tiles], v_refs[b // n_tiles], rows

        for i in range(n_tiles):
            own_rows = pl.ds(i * TILE, TILE)
            q = q_ref[own_rows, :]
            d = d_ref[own_rows, :]

            def on(j):
                return flags_ref[i * nblk + j] != 0

            def logit(j):
                k_ref, _, rows = block(i, j)
                raw = lax.dot_general(q, k_ref[rows, :], (((1,), (1,)), ((), ())),
                                      preferred_element_type=jnp.float32)
                return raw * scale + bias_ref[own_rows, j * TILE:(j + 1) * TILE]

            s = logit(tile_reach)
            s_scr[tile_reach] = s
            m_scr[...] = s.max(axis=1, keepdims=True)
            for j in range(tile_reach):
                @pl.when(on(j))
                def _():
                    s = logit(j)
                    s_scr[j] = s
                    m_scr[...] = jnp.maximum(m_scr[...], s.max(axis=1, keepdims=True))
            top = m_scr[...]
            l_scr[...] = jnp.exp(s_scr[tile_reach] - top).sum(axis=1, keepdims=True)
            for j in range(tile_reach):
                @pl.when(on(j))
                def _():
                    l_scr[...] += jnp.exp(s_scr[j] - top).sum(axis=1, keepdims=True)
            lse = top + jnp.log(l_scr[...])

            def prob_out(j, first):
                _, v_ref, rows = block(i, j)
                p = jnp.exp(s_scr[j] - lse)
                s_scr[j] = p
                part = jnp.dot(p.astype(jnp.bfloat16), v_ref[rows, :],
                               preferred_element_type=jnp.float32)
                if first:
                    o_scr[...] = part
                else:
                    o_scr[...] += part

            prob_out(tile_reach, True)
            for j in range(tile_reach):
                pl.when(on(j))(lambda j=j: prob_out(j, False))
            delta = (d.astype(jnp.float32) * o_scr[...]).sum(axis=1, keepdims=True)

            def grad(j, first):
                k_ref, v_ref, rows = block(i, j)
                dprobs = lax.dot_general(d, v_ref[rows, :], (((1,), (1,)), ((), ())),
                                         preferred_element_type=jnp.float32)
                dscores = (s_scr[j] * (dprobs - delta)).astype(jnp.bfloat16)
                part = jnp.dot(dscores, k_ref[rows, :], preferred_element_type=jnp.float32)
                if first:
                    o_scr[...] = part
                else:
                    o_scr[...] += part

            grad(tile_reach, True)
            for j in range(tile_reach):
                pl.when(on(j))(lambda j=j: grad(j, False))
            dq_ref[own_rows, :] = (o_scr[...] * scale).astype(dq_ref.dtype)
            ld_ref[0:1, i * TILE:(i + 1) * TILE] = _row(lse, TILE)
            ld_ref[1:2, i * TILE:(i + 1) * TILE] = _row(delta, TILE)

    return kernel


def _key_side_kernel(reach, n_tiles, tile_reach, scale):
    nblk = tile_reach + 1
    npl = reach + 1

    def kernel(flags_ref, *refs):
        k_ref, v_ref = refs[0], refs[1]
        q_refs = refs[2:2 + npl]
        d_refs = refs[2 + npl:2 + 2 * npl]
        ld_refs = refs[2 + 2 * npl:2 + 3 * npl]
        bias_ref = refs[2 + 3 * npl]
        dk_ref, dv_ref = refs[3 + 3 * npl], refs[4 + 3 * npl]
        dk_scr, dv_scr = refs[5 + 3 * npl:]

        for i in range(n_tiles):
            own_rows = pl.ds(i * TILE, TILE)
            k = k_ref[own_rows, :]
            v = v_ref[own_rows, :]

            def step(j, first):
                b = i + j
                p_i, t = b // n_tiles, b % n_tiles
                rows = pl.ds(t * TILE, TILE)
                q = q_refs[p_i][rows, :]
                d = d_refs[p_i][rows, :]
                lse = ld_refs[p_i][0:1, t * TILE:(t + 1) * TILE]
                delta = ld_refs[p_i][1:2, t * TILE:(t + 1) * TILE]
                raw = lax.dot_general(k, q, (((1,), (1,)), ((), ())),
                                      preferred_element_type=jnp.float32)
                logit = raw * scale + bias_ref[own_rows, j * TILE:(j + 1) * TILE]
                prob = jnp.exp(logit - lse)
                dprobs = lax.dot_general(v, d, (((1,), (1,)), ((), ())),
                                         preferred_element_type=jnp.float32)
                dscores = (prob * (dprobs - delta)).astype(jnp.bfloat16)
                part_k = jnp.dot(dscores, q, preferred_element_type=jnp.float32)
                part_v = jnp.dot(prob.astype(jnp.bfloat16), d, preferred_element_type=jnp.float32)
                if first:
                    dk_scr[...] = part_k
                    dv_scr[...] = part_v
                else:
                    dk_scr[...] += part_k
                    dv_scr[...] += part_v

            step(0, True)
            for j in range(1, nblk):
                pl.when(flags_ref[i * nblk + j] != 0)(lambda j=j: step(j, False))
            dk_ref[own_rows, :] = (dk_scr[...] * scale).astype(dk_ref.dtype)
            dv_ref[own_rows, :] = dv_scr[...].astype(dv_ref.dtype)

    return kernel


def _plan(tok_in, ctx_n, head_n):
    clo_n = 1
    while (clo_n * 2 <= ctx_n and ctx_n % (clo_n * 2) == 0
           and tok_in * clo_n * head_n < PLANE_TOKENS):
        clo_n *= 2
    return clo_n


def _per_device(clo_n, attn_q, attn_k, attn_v, attn_dout, doc_ids):
    tok_in, full_width = attn_q.shape
    head_n = lax.axis_size("head")
    chi_n = lax.axis_size("chi")
    group = clo_n * head_n
    width = full_width // group
    heads_p = width // HEAD_DIM
    plane = tok_in * group
    n_tok = doc_ids.shape[0]
    scale = HEAD_DIM ** (-0.5)
    reach = min(-(-(MAX_DOC - 1) // plane), chi_n - 1)
    tile_reach = -(-(MAX_DOC - 1) // TILE)
    nblk = tile_reach + 1
    n_tiles = plane // TILE
    chi = lax.axis_index("chi")
    plane_start = chi * plane

    def to_plane(x):
        x = x.reshape(tok_in, head_n, clo_n, width).transpose(0, 2, 1, 3).reshape(tok_in, full_width)
        return lax.all_to_all(x, ("clo", "head"), split_axis=1, concat_axis=0, tiled=True)

    keys = to_plane(attn_k)
    values = to_plane(attn_v)
    query = to_plane(attn_q)
    dout = to_plane(attn_dout)

    k_parts, v_parts = [], []
    for shift in range(reach, 0, -1):
        far_k, far_v = shifted((keys, values), "chi", shift)
        k_parts.append(far_k)
        v_parts.append(far_v)
    k_parts.append(keys)
    v_parts.append(values)

    q_parts, d_parts = [query], [dout]
    for shift in range(1, reach + 1):
        far_q, far_d = shifted((query, dout), "chi", -shift)
        q_parts.append(far_q)
        d_parts.append(far_d)

    pad = (reach + 1) * plane
    docs_pad = jnp.concatenate([
        jnp.full((pad,), -1, jnp.int32), doc_ids.astype(jnp.int32), jnp.full((pad,), -1, jnp.int32)])
    span = nblk * TILE
    cols = jnp.arange(span, dtype=jnp.int32)
    rows = jnp.arange(TILE, dtype=jnp.int32)
    q_bias, k_bias, q_flags, k_flags = [], [], [], []
    for i in range(n_tiles):
        t_start = plane_start + i * TILE
        own_doc = lax.dynamic_slice_in_dim(docs_pad, t_start + pad, TILE)
        own_pos = t_start + rows
        k_start = t_start - tile_reach * TILE
        k_doc = lax.dynamic_slice_in_dim(docs_pad, k_start + pad, span)
        k_pos = k_start + cols
        mask = (k_pos[None, :] <= own_pos[:, None]) & (k_doc[None, :] == own_doc[:, None])
        q_bias.append(jnp.where(mask, 0.0, masked_value).astype(jnp.float32))
        q_flags.append(mask.reshape(TILE, nblk, TILE).any(axis=(0, 2)))
        q_doc = lax.dynamic_slice_in_dim(docs_pad, t_start + pad, span)
        q_pos = t_start + cols
        mask = (own_pos[:, None] <= q_pos[None, :]) & (own_doc[:, None] == q_doc[None, :])
        k_bias.append(jnp.where(mask, 0.0, masked_value).astype(jnp.float32))
        k_flags.append(mask.reshape(TILE, nblk, TILE).any(axis=(0, 2)))
    q_bias = jnp.concatenate(q_bias, axis=0)
    k_bias = jnp.concatenate(k_bias, axis=0)
    q_flags = jnp.concatenate(q_flags).astype(jnp.int32)
    k_flags = jnp.concatenate(k_flags).astype(jnp.int32)

    plane_spec = pl.BlockSpec((plane, HEAD_DIM), lambda h, f: (0, h))
    ld_spec = pl.BlockSpec((None, 2, plane), lambda h, f: (h, 0, 0))
    bias_spec = pl.BlockSpec((plane, span), lambda h, f: (0, 0))
    params = pltpu.CompilerParams(dimension_semantics=("arbitrary",))
    npl = reach + 1

    dq, ld = pl.pallas_call(
        _query_side_kernel(reach, n_tiles, tile_reach, scale),
        out_shape=(
            jax.ShapeDtypeStruct((plane, width), jnp.bfloat16),
            jax.ShapeDtypeStruct((heads_p, 2, plane), jnp.float32),
        ),
        grid_spec=pltpu.PrefetchScalarGridSpec(
            num_scalar_prefetch=1,
            grid=(heads_p,),
            in_specs=[plane_spec] * (2 + 2 * npl) + [bias_spec],
            out_specs=(plane_spec, ld_spec),
            scratch_shapes=[
                pltpu.VMEM((nblk, TILE, TILE), jnp.float32),
                pltpu.VMEM((TILE, 1), jnp.float32),
                pltpu.VMEM((TILE, 1), jnp.float32),
                pltpu.VMEM((TILE, HEAD_DIM), jnp.float32),
            ],
        ),
        compiler_params=params,
        name="attn_query_side",
    )(q_flags, query, dout, *k_parts, *v_parts, q_bias)

    ld_parts = [ld]
    for shift in range(1, reach + 1):
        ld_parts.append(shifted(ld, "chi", -shift))

    dk, dv = pl.pallas_call(
        _key_side_kernel(reach, n_tiles, tile_reach, scale),
        out_shape=(
            jax.ShapeDtypeStruct((plane, width), jnp.bfloat16),
            jax.ShapeDtypeStruct((plane, width), jnp.bfloat16),
        ),
        grid_spec=pltpu.PrefetchScalarGridSpec(
            num_scalar_prefetch=1,
            grid=(heads_p,),
            in_specs=[plane_spec] * (2 + 2 * npl) + [ld_spec] * npl + [bias_spec],
            out_specs=(plane_spec, plane_spec),
            scratch_shapes=[
                pltpu.VMEM((TILE, HEAD_DIM), jnp.float32),
                pltpu.VMEM((TILE, HEAD_DIM), jnp.float32),
            ],
        ),
        compiler_params=params,
        name="attn_key_side",
    )(k_flags, keys, values, *q_parts, *d_parts, *ld_parts, k_bias)

    def from_plane(x):
        return lax.all_to_all(x, "clo", split_axis=0, concat_axis=1, tiled=True)

    return (from_plane(dq), from_plane(dk), from_plane(dv))


def solution(mesh):
    ctx_n, head_n = mesh.devices.shape
    def fn(attn_q, attn_k, attn_v, attn_dout, doc_ids):
        tok_in = attn_q.shape[0] // (ctx_n * head_n)
        clo_n = _plan(tok_in, ctx_n, head_n)
        chi_n = ctx_n // clo_n
        sub = Mesh(np.asarray(mesh.devices).reshape(chi_n, clo_n, head_n), ("chi", "clo", "head"))
        inner = jax.shard_map(
            lambda *a: _per_device(clo_n, *a),
            mesh=sub,
            in_specs=(
                P(("chi", "clo", "head"), None),
                P(("chi", "clo", "head"), None),
                P(("chi", "clo", "head"), None),
                P(("chi", "clo", "head"), None),
                P(),
            ),
            out_specs=(P(("chi", "clo"), "head"), P(("chi", "clo"), "head"), P(("chi", "clo"), "head")),
            check_vma=False,
        )
        return inner(attn_q, attn_k, attn_v, attn_dout, doc_ids)
    return fn
```

```python
import jax
import jax.numpy as jnp
import numpy as np
from jax import lax
from jax.experimental import pallas as pl
from jax.experimental.pallas import tpu as pltpu
from jax.sharding import Mesh
from jax.sharding import PartitionSpec as P

HEAD_DIM = 128
MAX_DOC = 1024
PLANE_TOKENS = 1024
TILE = 256

masked_value = -1e30


def shifted(value, axis, steps):
    count = lax.axis_size(axis)
    leading, last = (max(0, -steps), min(count, count - steps))
    return lax.ppermute(value, axis, [(source, source + steps) for source in range(leading, last)])


def _row(col, tok):
    return jnp.transpose(jnp.broadcast_to(col, (tok, 128)))[0:1, :]


def _pick(refs, plane_idx):
    value = refs[-1][...]
    for p in range(len(refs) - 2, -1, -1):
        value = jnp.where(plane_idx == p, refs[p][...], value)
    return value


def _query_side_kernel(nblk, npl, base, n_tiles, scale):
    def kernel(*refs):
        q_ref, d_ref = refs[0], refs[1]
        nref = nblk * npl
        kp_refs = refs[2:2 + nref]
        vp_refs = refs[2 + nref:2 + 2 * nref]
        bias_ref = refs[2 + 2 * nref]
        dq_ref, ld_ref = refs[3 + 2 * nref], refs[4 + 2 * nref]
        tile = pl.program_id(0)
        k_blocks, v_blocks = [], []
        for j in range(nblk):
            plane_idx = (base + tile + j) // n_tiles
            k_blocks.append(_pick(kp_refs[j * npl:(j + 1) * npl], plane_idx))
            v_blocks.append(_pick(vp_refs[j * npl:(j + 1) * npl], plane_idx))
        q = q_ref[...]
        d = d_ref[...]
        logits = []
        for j in range(nblk):
            raw = lax.dot_general(q, k_blocks[j], (((1,), (1,)), ((), ())),
                                  preferred_element_type=jnp.float32)
            logits.append(raw * scale + bias_ref[:, j * TILE:(j + 1) * TILE])
        top = logits[0].max(axis=1, keepdims=True)
        for j in range(1, nblk):
            top = jnp.maximum(top, logits[j].max(axis=1, keepdims=True))
        denom = jnp.exp(logits[0] - top).sum(axis=1, keepdims=True)
        for j in range(1, nblk):
            denom = denom + jnp.exp(logits[j] - top).sum(axis=1, keepdims=True)
        lse = top + jnp.log(denom)
        probs = [jnp.exp(item - lse) for item in logits]
        out = None
        for j in range(nblk):
            part = jnp.dot(probs[j].astype(jnp.bfloat16), v_blocks[j],
                           preferred_element_type=jnp.float32)
            out = part if out is None else out + part
        delta = (d.astype(jnp.float32) * out).sum(axis=1, keepdims=True)
        dq = None
        for j in range(nblk):
            dprobs = lax.dot_general(d, v_blocks[j], (((1,), (1,)), ((), ())),
                                     preferred_element_type=jnp.float32)
            dscores = (probs[j] * (dprobs - delta)).astype(jnp.bfloat16)
            part = jnp.dot(dscores, k_blocks[j], preferred_element_type=jnp.float32)
            dq = part if dq is None else dq + part
        dq_ref[...] = (dq * scale).astype(dq_ref.dtype)
        ld_ref[0:1, :] = _row(lse, TILE)
        ld_ref[1:2, :] = _row(delta, TILE)

    return kernel


def _key_side_kernel(nblk, npl, n_tiles, scale):
    def kernel(*refs):
        k_ref, v_ref = refs[0], refs[1]
        nref = nblk * npl
        qp_refs = refs[2:2 + nref]
        dp_refs = refs[2 + nref:2 + 2 * nref]
        lp_refs = refs[2 + 2 * nref:2 + 3 * nref]
        bias_ref = refs[2 + 3 * nref]
        out_ref = refs[3 + 3 * nref]
        tile = pl.program_id(0)
        k = k_ref[...]
        v = v_ref[...]
        dk = None
        dv = None
        for j in range(nblk):
            plane_idx = (tile + j) // n_tiles
            q = _pick(qp_refs[j * npl:(j + 1) * npl], plane_idx)
            d = _pick(dp_refs[j * npl:(j + 1) * npl], plane_idx)
            ld = _pick(lp_refs[j * npl:(j + 1) * npl], plane_idx)
            lse = ld[0:1, :]
            delta = ld[1:2, :]
            raw = lax.dot_general(k, q, (((1,), (1,)), ((), ())),
                                  preferred_element_type=jnp.float32)
            logit = raw * scale + bias_ref[:, j * TILE:(j + 1) * TILE]
            prob = jnp.exp(logit - lse)
            dprobs = lax.dot_general(v, d, (((1,), (1,)), ((), ())),
                                     preferred_element_type=jnp.float32)
            dscores = (prob * (dprobs - delta)).astype(jnp.bfloat16)
            part_k = jnp.dot(dscores, q, preferred_element_type=jnp.float32)
            part_v = jnp.dot(prob.astype(jnp.bfloat16), d, preferred_element_type=jnp.float32)
            dk = part_k if dk is None else dk + part_k
            dv = part_v if dv is None else dv + part_v
        out_ref[0] = (dk * scale).astype(out_ref.dtype)
        out_ref[1] = dv.astype(out_ref.dtype)

    return kernel


def _plan(tok_in, ctx_n, head_n):
    clo_n = 1
    while (clo_n * 2 <= ctx_n and ctx_n % (clo_n * 2) == 0
           and tok_in * clo_n * head_n < PLANE_TOKENS):
        clo_n *= 2
    return clo_n


def _per_device(clo_n, attn_q, attn_k, attn_v, attn_dout, doc_ids):
    tok_in, full_width = attn_q.shape
    head_n = lax.axis_size("head")
    chi_n = lax.axis_size("chi")
    group = clo_n * head_n
    width = full_width // group
    heads_p = width // HEAD_DIM
    plane = tok_in * group
    n_tok = doc_ids.shape[0]
    scale = HEAD_DIM ** (-0.5)
    reach = min(-(-(MAX_DOC - 1) // plane), chi_n - 1)
    tile_reach = -(-(MAX_DOC - 1) // TILE)
    nblk = tile_reach + 1
    n_tiles = plane // TILE
    chi = lax.axis_index("chi")
    plane_start = chi * plane

    def to_plane(a, b):
        x = jnp.stack([a, b]).reshape(2, tok_in, head_n, clo_n, width)
        x = x.transpose(0, 1, 3, 2, 4).reshape(2, tok_in, full_width)
        return lax.all_to_all(x, ("clo", "head"), split_axis=2, concat_axis=1, tiled=True)

    kv = to_plane(attn_k, attn_v)
    kv_parts = [shifted(kv, "chi", shift) for shift in range(reach, 0, -1)] + [kv]
    qd = to_plane(attn_q, attn_dout)
    qd_parts = [qd] + [shifted(qd, "chi", -shift) for shift in range(1, reach + 1)]

    pad = (reach + 1) * plane
    docs_pad = jnp.concatenate([
        jnp.full((pad,), -1, jnp.int32), doc_ids.astype(jnp.int32), jnp.full((pad,), -1, jnp.int32)])
    span = nblk * TILE
    cols = jnp.arange(span, dtype=jnp.int32)
    rows = jnp.arange(TILE, dtype=jnp.int32)
    q_bias, k_bias = [], []
    for i in range(n_tiles):
        t_start = plane_start + i * TILE
        own_doc = lax.dynamic_slice_in_dim(docs_pad, t_start + pad, TILE)
        own_pos = t_start + rows
        k_start = t_start - tile_reach * TILE
        k_doc = lax.dynamic_slice_in_dim(docs_pad, k_start + pad, span)
        k_pos = k_start + cols
        mask = (k_pos[None, :] <= own_pos[:, None]) & (k_doc[None, :] == own_doc[:, None])
        q_bias.append(jnp.where(mask, 0.0, masked_value).astype(jnp.float32))
        q_doc = lax.dynamic_slice_in_dim(docs_pad, t_start + pad, span)
        q_pos = t_start + cols
        mask = (own_pos[:, None] <= q_pos[None, :]) & (own_doc[:, None] == q_doc[None, :])
        k_bias.append(jnp.where(mask, 0.0, masked_value).astype(jnp.float32))
    q_bias = jnp.concatenate(q_bias, axis=0)
    k_bias = jnp.concatenate(k_bias, axis=0)

    def own_spec(w):
        return pl.BlockSpec((None, TILE, HEAD_DIM), lambda i, h: (w, i, h))

    base = reach * n_tiles - tile_reach
    npl = reach + 1

    def clamp_tile(b, p):
        return jnp.clip(b - p * n_tiles, 0, n_tiles - 1)

    def win_specs(w, shift):
        return [pl.BlockSpec((None, TILE, HEAD_DIM),
                             lambda i, h, p=p, j=j: (w, clamp_tile(shift + i + j, p), h))
                for j in range(nblk) for p in range(npl)]

    ld_win_specs = [pl.BlockSpec((None, 2, TILE), lambda i, h, p=p, j=j: (h, 0, clamp_tile(i + j, p)))
                    for j in range(nblk) for p in range(npl)]
    bias_spec = pl.BlockSpec((TILE, span), lambda i, h: (i, 0))
    ld_spec = pl.BlockSpec((None, 2, TILE), lambda i, h: (h, 0, i))
    params = pltpu.CompilerParams(dimension_semantics=("arbitrary", "arbitrary"))
    grid = (n_tiles, heads_p)

    dq, ld = pl.pallas_call(
        _query_side_kernel(nblk, npl, base, n_tiles, scale),
        out_shape=(
            jax.ShapeDtypeStruct((plane, width), jnp.bfloat16),
            jax.ShapeDtypeStruct((heads_p, 2, plane), jnp.float32),
        ),
        grid=grid,
        in_specs=[own_spec(0), own_spec(1)] + win_specs(0, base) + win_specs(1, base) + [bias_spec],
        out_specs=(pl.BlockSpec((TILE, HEAD_DIM), lambda i, h: (i, h)), ld_spec),
        compiler_params=params,
        name="attn_query_side",
    )(qd, qd, *(kv_parts * nblk), *(kv_parts * nblk), q_bias)

    ld_parts = [ld] + [shifted(ld, "chi", -shift) for shift in range(1, reach + 1)]

    dkv = pl.pallas_call(
        _key_side_kernel(nblk, npl, n_tiles, scale),
        out_shape=jax.ShapeDtypeStruct((2, plane, width), jnp.bfloat16),
        grid=grid,
        in_specs=[own_spec(0), own_spec(1)] + win_specs(0, 0) + win_specs(1, 0) + ld_win_specs + [bias_spec],
        out_specs=pl.BlockSpec((2, TILE, HEAD_DIM), lambda i, h: (0, i, h)),
        compiler_params=params,
        name="attn_key_side",
    )(kv, kv, *(qd_parts * nblk), *(qd_parts * nblk), *(ld_parts * nblk), k_bias)

    dq = lax.all_to_all(dq, "clo", split_axis=0, concat_axis=1, tiled=True)
    dkv = lax.all_to_all(dkv, "clo", split_axis=1, concat_axis=2, tiled=True)
    return (dq, dkv[0], dkv[1])


def solution(mesh):
    ctx_n, head_n = mesh.devices.shape
    def fn(attn_q, attn_k, attn_v, attn_dout, doc_ids):
        tok_in = attn_q.shape[0] // (ctx_n * head_n)
        clo_n = _plan(tok_in, ctx_n, head_n)
        chi_n = ctx_n // clo_n
        sub = Mesh(np.asarray(mesh.devices).reshape(chi_n, clo_n, head_n), ("chi", "clo", "head"))
        inner = jax.shard_map(
            lambda *a: _per_device(clo_n, *a),
            mesh=sub,
            in_specs=(
                P(("chi", "clo", "head"), None),
                P(("chi", "clo", "head"), None),
                P(("chi", "clo", "head"), None),
                P(("chi", "clo", "head"), None),
                P(),
            ),
            out_specs=(P(("chi", "clo"), "head"), P(("chi", "clo"), "head"), P(("chi", "clo"), "head")),
            check_vma=False,
        )
        return inner(attn_q, attn_k, attn_v, attn_dout, doc_ids)
    return fn
```

```python
import jax
import jax.numpy as jnp
import numpy as np
from jax import lax
from jax.experimental import pallas as pl
from jax.experimental.pallas import tpu as pltpu
from jax.sharding import Mesh
from jax.sharding import PartitionSpec as P

HEAD_DIM = 128
MAX_DOC = 1024
PLANE_TOKENS = 1024
TILE = 256

masked_value = -1e30


def shifted(value, axis, steps):
    count = lax.axis_size(axis)
    leading, last = (max(0, -steps), min(count, count - steps))
    return lax.ppermute(value, axis, [(source, source + steps) for source in range(leading, last)])


def _row(col, tok):
    return jnp.transpose(jnp.broadcast_to(col, (tok, 128)))[0:1, :]


def _query_side_kernel(nblk, scale):
    def kernel(*refs):
        q_ref, d_ref = refs[0], refs[1]
        k_refs = refs[2:2 + nblk]
        v_refs = refs[2 + nblk:2 + 2 * nblk]
        bias_ref = refs[2 + 2 * nblk]
        dq_ref, ld_ref = refs[3 + 2 * nblk], refs[4 + 2 * nblk]
        q = q_ref[...]
        d = d_ref[...]
        logits = []
        for j in range(nblk):
            raw = lax.dot_general(q, k_refs[j][...], (((1,), (1,)), ((), ())),
                                  preferred_element_type=jnp.float32)
            logits.append(raw * scale + bias_ref[:, j * TILE:(j + 1) * TILE])
        top = logits[0].max(axis=1, keepdims=True)
        for j in range(1, nblk):
            top = jnp.maximum(top, logits[j].max(axis=1, keepdims=True))
        denom = jnp.exp(logits[0] - top).sum(axis=1, keepdims=True)
        for j in range(1, nblk):
            denom = denom + jnp.exp(logits[j] - top).sum(axis=1, keepdims=True)
        lse = top + jnp.log(denom)
        probs = [jnp.exp(item - lse) for item in logits]
        out = None
        for j in range(nblk):
            part = jnp.dot(probs[j].astype(jnp.bfloat16), v_refs[j][...],
                           preferred_element_type=jnp.float32)
            out = part if out is None else out + part
        delta = (d.astype(jnp.float32) * out).sum(axis=1, keepdims=True)
        dq = None
        for j in range(nblk):
            dprobs = lax.dot_general(d, v_refs[j][...], (((1,), (1,)), ((), ())),
                                     preferred_element_type=jnp.float32)
            dscores = (probs[j] * (dprobs - delta)).astype(jnp.bfloat16)
            part = jnp.dot(dscores, k_refs[j][...], preferred_element_type=jnp.float32)
            dq = part if dq is None else dq + part
        dq_ref[...] = (dq * scale).astype(dq_ref.dtype)
        ld_ref[0:1, :] = _row(lse, TILE)
        ld_ref[1:2, :] = _row(delta, TILE)

    return kernel


def _key_side_kernel(nblk, scale):
    def kernel(*refs):
        k_ref, v_ref = refs[0], refs[1]
        q_refs = refs[2:2 + nblk]
        d_refs = refs[2 + nblk:2 + 2 * nblk]
        ld_refs = refs[2 + 2 * nblk:2 + 3 * nblk]
        bias_ref = refs[2 + 3 * nblk]
        dk_ref, dv_ref = refs[3 + 3 * nblk], refs[4 + 3 * nblk]
        k = k_ref[...]
        v = v_ref[...]
        dk = None
        dv = None
        for j in range(nblk):
            q = q_refs[j][...]
            d = d_refs[j][...]
            lse = ld_refs[j][0:1, :]
            delta = ld_refs[j][1:2, :]
            raw = lax.dot_general(k, q, (((1,), (1,)), ((), ())),
                                  preferred_element_type=jnp.float32)
            logit = raw * scale + bias_ref[:, j * TILE:(j + 1) * TILE]
            prob = jnp.exp(logit - lse)
            dprobs = lax.dot_general(v, d, (((1,), (1,)), ((), ())),
                                     preferred_element_type=jnp.float32)
            dscores = (prob * (dprobs - delta)).astype(jnp.bfloat16)
            part_k = jnp.dot(dscores, q, preferred_element_type=jnp.float32)
            part_v = jnp.dot(prob.astype(jnp.bfloat16), d, preferred_element_type=jnp.float32)
            dk = part_k if dk is None else dk + part_k
            dv = part_v if dv is None else dv + part_v
        dk_ref[...] = (dk * scale).astype(dk_ref.dtype)
        dv_ref[...] = dv.astype(dv_ref.dtype)

    return kernel


def _plan(tok_in, ctx_n, head_n):
    clo_n = 1
    while (clo_n * 2 <= ctx_n and ctx_n % (clo_n * 2) == 0
           and tok_in * clo_n * head_n < PLANE_TOKENS):
        clo_n *= 2
    return clo_n


def _per_device(clo_n, attn_q, attn_k, attn_v, attn_dout, doc_ids):
    tok_in, full_width = attn_q.shape
    head_n = lax.axis_size("head")
    chi_n = lax.axis_size("chi")
    group = clo_n * head_n
    width = full_width // group
    heads_p = width // HEAD_DIM
    plane = tok_in * group
    n_tok = doc_ids.shape[0]
    scale = HEAD_DIM ** (-0.5)
    reach = min(-(-(MAX_DOC - 1) // plane), chi_n - 1)
    tile_reach = -(-(MAX_DOC - 1) // TILE)
    nblk = tile_reach + 1
    n_tiles = plane // TILE
    chi = lax.axis_index("chi")
    plane_start = chi * plane

    def to_plane(a, b):
        a = a.reshape(tok_in, head_n, clo_n, 1, width)
        b = b.reshape(tok_in, head_n, clo_n, 1, width)
        x = jnp.concatenate([a, b], axis=3).transpose(0, 2, 1, 3, 4).reshape(tok_in, 2 * full_width)
        return lax.all_to_all(x, ("clo", "head"), split_axis=1, concat_axis=0, tiled=True)

    kv = to_plane(attn_k, attn_v)
    kv_win = jnp.concatenate([shifted(kv, "chi", shift) for shift in range(reach, 0, -1)] + [kv], axis=0)
    qd = to_plane(attn_q, attn_dout)
    qd_win = jnp.concatenate([qd] + [shifted(qd, "chi", -shift) for shift in range(1, reach + 1)], axis=0)

    pad = (reach + 1) * plane
    docs_pad = jnp.concatenate([
        jnp.full((pad,), -1, jnp.int32), doc_ids.astype(jnp.int32), jnp.full((pad,), -1, jnp.int32)])
    span = nblk * TILE
    cols = jnp.arange(span, dtype=jnp.int32)
    rows = jnp.arange(TILE, dtype=jnp.int32)
    q_bias, k_bias = [], []
    for i in range(n_tiles):
        t_start = plane_start + i * TILE
        own_doc = lax.dynamic_slice_in_dim(docs_pad, t_start + pad, TILE)
        own_pos = t_start + rows
        k_start = t_start - tile_reach * TILE
        k_doc = lax.dynamic_slice_in_dim(docs_pad, k_start + pad, span)
        k_pos = k_start + cols
        mask = (k_pos[None, :] <= own_pos[:, None]) & (k_doc[None, :] == own_doc[:, None])
        q_bias.append(jnp.where(mask, 0.0, masked_value).astype(jnp.float32))
        q_doc = lax.dynamic_slice_in_dim(docs_pad, t_start + pad, span)
        q_pos = t_start + cols
        mask = (own_pos[:, None] <= q_pos[None, :]) & (own_doc[:, None] == q_doc[None, :])
        k_bias.append(jnp.where(mask, 0.0, masked_value).astype(jnp.float32))
    q_bias = jnp.concatenate(q_bias, axis=0)
    k_bias = jnp.concatenate(k_bias, axis=0)

    own_spec = pl.BlockSpec((TILE, HEAD_DIM), lambda i, h: (i, h))
    base = reach * n_tiles - tile_reach

    def col_spec(off):
        return pl.BlockSpec((TILE, HEAD_DIM), lambda i, h: (i, h + off))

    def kwin_spec(j, off):
        return pl.BlockSpec((TILE, HEAD_DIM), lambda i, h: (base + i + j, h + off))

    def qwin_spec(j, off):
        return pl.BlockSpec((TILE, HEAD_DIM), lambda i, h: (i + j, h + off))

    def ldwin_spec(j):
        return pl.BlockSpec((None, 2, TILE), lambda i, h: (h, 0, i + j))

    bias_spec = pl.BlockSpec((TILE, span), lambda i, h: (i, 0))
    ld_spec = pl.BlockSpec((None, 2, TILE), lambda i, h: (h, 0, i))
    params = pltpu.CompilerParams(dimension_semantics=("arbitrary", "arbitrary"))
    grid = (n_tiles, heads_p)

    dq, ld = pl.pallas_call(
        _query_side_kernel(nblk, scale),
        out_shape=(
            jax.ShapeDtypeStruct((plane, width), jnp.bfloat16),
            jax.ShapeDtypeStruct((heads_p, 2, plane), jnp.float32),
        ),
        grid=grid,
        in_specs=[col_spec(0), col_spec(heads_p)] + [kwin_spec(j, 0) for j in range(nblk)]
        + [kwin_spec(j, heads_p) for j in range(nblk)] + [bias_spec],
        out_specs=(own_spec, ld_spec),
        compiler_params=params,
        name="attn_query_side",
    )(qd, qd, *([kv_win] * (2 * nblk)), q_bias)

    ld_parts = [ld]
    for shift in range(1, reach + 1):
        ld_parts.append(shifted(ld, "chi", -shift))
    ld_win = jnp.concatenate(ld_parts, axis=2)

    dk, dv = pl.pallas_call(
        _key_side_kernel(nblk, scale),
        out_shape=(
            jax.ShapeDtypeStruct((plane, width), jnp.bfloat16),
            jax.ShapeDtypeStruct((plane, width), jnp.bfloat16),
        ),
        grid=grid,
        in_specs=[col_spec(0), col_spec(heads_p)] + [qwin_spec(j, 0) for j in range(nblk)]
        + [qwin_spec(j, heads_p) for j in range(nblk)] + [ldwin_spec(j) for j in range(nblk)] + [bias_spec],
        out_specs=(own_spec, own_spec),
        compiler_params=params,
        name="attn_key_side",
    )(kv, kv, *([qd_win] * (2 * nblk)), *([ld_win] * nblk), k_bias)

    def from_plane(x):
        return lax.all_to_all(x, "clo", split_axis=0, concat_axis=1, tiled=True)

    return (from_plane(dq), from_plane(dk), from_plane(dv))


def solution(mesh):
    ctx_n, head_n = mesh.devices.shape
    def fn(attn_q, attn_k, attn_v, attn_dout, doc_ids):
        tok_in = attn_q.shape[0] // (ctx_n * head_n)
        clo_n = _plan(tok_in, ctx_n, head_n)
        chi_n = ctx_n // clo_n
        sub = Mesh(np.asarray(mesh.devices).reshape(chi_n, clo_n, head_n), ("chi", "clo", "head"))
        inner = jax.shard_map(
            lambda *a: _per_device(clo_n, *a),
            mesh=sub,
            in_specs=(
                P(("chi", "clo", "head"), None),
                P(("chi", "clo", "head"), None),
                P(("chi", "clo", "head"), None),
                P(("chi", "clo", "head"), None),
                P(),
            ),
            out_specs=(P(("chi", "clo"), "head"), P(("chi", "clo"), "head"), P(("chi", "clo"), "head")),
            check_vma=False,
        )
        return inner(attn_q, attn_k, attn_v, attn_dout, doc_ids)
    return fn
```

```python
import jax
import jax.numpy as jnp
import numpy as np
from jax import lax
from jax.experimental import pallas as pl
from jax.experimental.pallas import tpu as pltpu
from jax.sharding import Mesh
from jax.sharding import PartitionSpec as P

HEAD_DIM = 128
MAX_DOC = 1024
PLANE_TOKENS = 1024
TILE = 256
HALO_ROWS = 256

masked_value = -1e30


def shifted(value, axis, steps):
    count = lax.axis_size(axis)
    leading, last = (max(0, -steps), min(count, count - steps))
    return lax.ppermute(value, axis, [(source, source + steps) for source in range(leading, last)])


def _row(col, tok):
    return jnp.transpose(jnp.broadcast_to(col, (tok, 128)))[0:1, :]


def _query_side_kernel(nblk, scale):
    def kernel(*refs):
        q_ref, d_ref = refs[0], refs[1]
        k_refs = refs[2:2 + nblk]
        v_refs = refs[2 + nblk:2 + 2 * nblk]
        bias_ref = refs[2 + 2 * nblk]
        dq_ref, ld_ref = refs[3 + 2 * nblk], refs[4 + 2 * nblk]
        q = q_ref[...]
        d = d_ref[...]
        logits = []
        for j in range(nblk):
            raw = lax.dot_general(q, k_refs[j][...], (((1,), (1,)), ((), ())),
                                  preferred_element_type=jnp.float32)
            logits.append(raw * scale + bias_ref[:, j * TILE:(j + 1) * TILE])
        top = logits[0].max(axis=1, keepdims=True)
        for j in range(1, nblk):
            top = jnp.maximum(top, logits[j].max(axis=1, keepdims=True))
        denom = jnp.exp(logits[0] - top).sum(axis=1, keepdims=True)
        for j in range(1, nblk):
            denom = denom + jnp.exp(logits[j] - top).sum(axis=1, keepdims=True)
        lse = top + jnp.log(denom)
        probs = [jnp.exp(item - lse) for item in logits]
        out = None
        for j in range(nblk):
            part = jnp.dot(probs[j].astype(jnp.bfloat16), v_refs[j][...],
                           preferred_element_type=jnp.float32)
            out = part if out is None else out + part
        delta = (d.astype(jnp.float32) * out).sum(axis=1, keepdims=True)
        dq = None
        for j in range(nblk):
            dprobs = lax.dot_general(d, v_refs[j][...], (((1,), (1,)), ((), ())),
                                     preferred_element_type=jnp.float32)
            dscores = (probs[j] * (dprobs - delta)).astype(jnp.bfloat16)
            part = jnp.dot(dscores, k_refs[j][...], preferred_element_type=jnp.float32)
            dq = part if dq is None else dq + part
        dq_ref[...] = (dq * scale).astype(dq_ref.dtype)
        ld_ref[0:1, :] = _row(lse, TILE)
        ld_ref[1:2, :] = _row(delta, TILE)

    return kernel


def _key_side_kernel(nblk, scale):
    def kernel(*refs):
        k_ref, v_ref = refs[0], refs[1]
        q_refs = refs[2:2 + nblk]
        d_refs = refs[2 + nblk:2 + 2 * nblk]
        ld_refs = refs[2 + 2 * nblk:2 + 3 * nblk]
        bias_ref = refs[2 + 3 * nblk]
        dk_ref, dv_ref = refs[3 + 3 * nblk], refs[4 + 3 * nblk]
        k = k_ref[...]
        v = v_ref[...]
        dk = None
        dv = None
        for j in range(nblk):
            q = q_refs[j][...]
            d = d_refs[j][...]
            lse = ld_refs[j][0:1, :]
            delta = ld_refs[j][1:2, :]
            raw = lax.dot_general(k, q, (((1,), (1,)), ((), ())),
                                  preferred_element_type=jnp.float32)
            logit = raw * scale + bias_ref[:, j * TILE:(j + 1) * TILE]
            prob = jnp.exp(logit - lse)
            dprobs = lax.dot_general(v, d, (((1,), (1,)), ((), ())),
                                     preferred_element_type=jnp.float32)
            dscores = (prob * (dprobs - delta)).astype(jnp.bfloat16)
            part_k = jnp.dot(dscores, q, preferred_element_type=jnp.float32)
            part_v = jnp.dot(prob.astype(jnp.bfloat16), d, preferred_element_type=jnp.float32)
            dk = part_k if dk is None else dk + part_k
            dv = part_v if dv is None else dv + part_v
        dk_ref[...] = (dk * scale).astype(dk_ref.dtype)
        dv_ref[...] = dv.astype(dv_ref.dtype)

    return kernel


def _halo_and(x, need, steps, tail, other, args):
    rows, cols = x.shape
    count = rows // HALO_ROWS

    def branch(n):
        def run(x, *args):
            extra = other(*args)
            if n == 0:
                return jnp.zeros_like(x), extra
            part = x[rows - n * HALO_ROWS:] if tail else x[:n * HALO_ROWS]
            got = shifted(part, "chi", steps)
            fill = jnp.zeros((rows - n * HALO_ROWS, cols), x.dtype)
            return jnp.concatenate([fill, got] if tail else [got, fill], axis=0), extra
        return run

    index = jnp.clip((need + HALO_ROWS - 1) // HALO_ROWS, 0, count)
    return lax.switch(index, [branch(n) for n in range(count + 1)], x, *args)


def _plan(tok_in, ctx_n, head_n):
    clo_n = 1
    while (clo_n * 2 <= ctx_n and ctx_n % (clo_n * 2) == 0
           and tok_in * clo_n * head_n < PLANE_TOKENS):
        clo_n *= 2
    return clo_n


def _per_device(clo_n, attn_q, attn_k, attn_v, attn_dout, doc_ids):
    tok_in, full_width = attn_q.shape
    head_n = lax.axis_size("head")
    chi_n = lax.axis_size("chi")
    group = clo_n * head_n
    width = full_width // group
    heads_p = width // HEAD_DIM
    plane = tok_in * group
    n_tok = doc_ids.shape[0]
    scale = HEAD_DIM ** (-0.5)
    reach = min(-(-(MAX_DOC - 1) // plane), chi_n - 1)
    tile_reach = -(-(MAX_DOC - 1) // TILE)
    nblk = tile_reach + 1
    n_tiles = plane // TILE
    chi = lax.axis_index("chi")
    plane_start = chi * plane

    def to_plane(a, b):
        a = a.reshape(tok_in, head_n, clo_n, 1, width)
        b = b.reshape(tok_in, head_n, clo_n, 1, width)
        x = jnp.concatenate([a, b], axis=3).transpose(0, 2, 1, 3, 4).reshape(tok_in, 2 * full_width)
        return lax.all_to_all(x, ("clo", "head"), split_axis=1, concat_axis=0, tiled=True)

    kv = to_plane(attn_k, attn_v)
    if reach == 1:
        edges = jnp.arange(1, chi_n, dtype=jnp.int32) * plane
        before = edges - jnp.sum(doc_ids[None, :] < doc_ids[edges][:, None], axis=1)
        kv_prev, qd = _halo_and(kv, jnp.max(before), 1, True, to_plane, (attn_q, attn_dout))
        kv_win = jnp.concatenate([kv_prev, kv], axis=0)
        qd_win = jnp.concatenate([qd, shifted(qd, "chi", -1)], axis=0)
    else:
        qd = to_plane(attn_q, attn_dout)
        kv_win = jnp.concatenate([shifted(kv, "chi", shift) for shift in range(reach, 0, -1)] + [kv], axis=0)
        qd_win = jnp.concatenate([qd] + [shifted(qd, "chi", -shift) for shift in range(1, reach + 1)], axis=0)

    pad = (reach + 1) * plane
    docs_pad = jnp.concatenate([
        jnp.full((pad,), -1, jnp.int32), doc_ids.astype(jnp.int32), jnp.full((pad,), -1, jnp.int32)])
    span = nblk * TILE
    cols = jnp.arange(span, dtype=jnp.int32)
    rows = jnp.arange(TILE, dtype=jnp.int32)
    q_bias, k_bias = [], []
    for i in range(n_tiles):
        t_start = plane_start + i * TILE
        own_doc = lax.dynamic_slice_in_dim(docs_pad, t_start + pad, TILE)
        own_pos = t_start + rows
        k_start = t_start - tile_reach * TILE
        k_doc = lax.dynamic_slice_in_dim(docs_pad, k_start + pad, span)
        k_pos = k_start + cols
        mask = (k_pos[None, :] <= own_pos[:, None]) & (k_doc[None, :] == own_doc[:, None])
        q_bias.append(jnp.where(mask, 0.0, masked_value).astype(jnp.float32))
        q_doc = lax.dynamic_slice_in_dim(docs_pad, t_start + pad, span)
        q_pos = t_start + cols
        mask = (own_pos[:, None] <= q_pos[None, :]) & (own_doc[:, None] == q_doc[None, :])
        k_bias.append(jnp.where(mask, 0.0, masked_value).astype(jnp.float32))
    q_bias = jnp.concatenate(q_bias, axis=0)
    k_bias = jnp.concatenate(k_bias, axis=0)

    own_spec = pl.BlockSpec((TILE, HEAD_DIM), lambda i, h: (i, h))
    base = reach * n_tiles - tile_reach

    def col_spec(off):
        return pl.BlockSpec((TILE, HEAD_DIM), lambda i, h: (i, h + off))

    def kwin_spec(j, off):
        return pl.BlockSpec((TILE, HEAD_DIM), lambda i, h: (base + i + j, h + off))

    def qwin_spec(j, off):
        return pl.BlockSpec((TILE, HEAD_DIM), lambda i, h: (i + j, h + off))

    def ldwin_spec(j):
        return pl.BlockSpec((None, 2, TILE), lambda i, h: (h, 0, i + j))

    bias_spec = pl.BlockSpec((TILE, span), lambda i, h: (i, 0))
    ld_spec = pl.BlockSpec((None, 2, TILE), lambda i, h: (h, 0, i))
    params = pltpu.CompilerParams(dimension_semantics=("arbitrary", "arbitrary"))
    grid = (n_tiles, heads_p)

    dq, ld = pl.pallas_call(
        _query_side_kernel(nblk, scale),
        out_shape=(
            jax.ShapeDtypeStruct((plane, width), jnp.bfloat16),
            jax.ShapeDtypeStruct((heads_p, 2, plane), jnp.float32),
        ),
        grid=grid,
        in_specs=[col_spec(0), col_spec(heads_p)] + [kwin_spec(j, 0) for j in range(nblk)]
        + [kwin_spec(j, heads_p) for j in range(nblk)] + [bias_spec],
        out_specs=(own_spec, ld_spec),
        compiler_params=params,
        name="attn_query_side",
    )(qd, qd, *([kv_win] * (2 * nblk)), q_bias)

    ld_parts = [ld]
    for shift in range(1, reach + 1):
        ld_parts.append(shifted(ld, "chi", -shift))
    ld_win = jnp.concatenate(ld_parts, axis=2)

    dk, dv = pl.pallas_call(
        _key_side_kernel(nblk, scale),
        out_shape=(
            jax.ShapeDtypeStruct((plane, width), jnp.bfloat16),
            jax.ShapeDtypeStruct((plane, width), jnp.bfloat16),
        ),
        grid=grid,
        in_specs=[col_spec(0), col_spec(heads_p)] + [qwin_spec(j, 0) for j in range(nblk)]
        + [qwin_spec(j, heads_p) for j in range(nblk)] + [ldwin_spec(j) for j in range(nblk)] + [bias_spec],
        out_specs=(own_spec, own_spec),
        compiler_params=params,
        name="attn_key_side",
    )(kv, kv, *([qd_win] * (2 * nblk)), *([ld_win] * nblk), k_bias)

    def from_plane(x):
        return lax.all_to_all(x, "clo", split_axis=0, concat_axis=1, tiled=True)

    return (from_plane(dq), from_plane(dk), from_plane(dv))


def solution(mesh):
    ctx_n, head_n = mesh.devices.shape
    def fn(attn_q, attn_k, attn_v, attn_dout, doc_ids):
        tok_in = attn_q.shape[0] // (ctx_n * head_n)
        clo_n = _plan(tok_in, ctx_n, head_n)
        chi_n = ctx_n // clo_n
        sub = Mesh(np.asarray(mesh.devices).reshape(chi_n, clo_n, head_n), ("chi", "clo", "head"))
        inner = jax.shard_map(
            lambda *a: _per_device(clo_n, *a),
            mesh=sub,
            in_specs=(
                P(("chi", "clo", "head"), None),
                P(("chi", "clo", "head"), None),
                P(("chi", "clo", "head"), None),
                P(("chi", "clo", "head"), None),
                P(),
            ),
            out_specs=(P(("chi", "clo"), "head"), P(("chi", "clo"), "head"), P(("chi", "clo"), "head")),
            check_vma=False,
        )
        return inner(attn_q, attn_k, attn_v, attn_dout, doc_ids)
    return fn
```

```python
import jax
import jax.numpy as jnp
import numpy as np
from jax import lax
from jax.experimental import pallas as pl
from jax.experimental.pallas import tpu as pltpu
from jax.sharding import Mesh
from jax.sharding import PartitionSpec as P

HEAD_DIM = 128
MAX_DOC = 1024
PLANE_TOKENS = 1024
TILE = 256

masked_value = -1e30


def shifted(value, axis, steps):
    count = lax.axis_size(axis)
    leading, last = (max(0, -steps), min(count, count - steps))
    return lax.ppermute(value, axis, [(source, source + steps) for source in range(leading, last)])


def _row(col, tok):
    return jnp.transpose(jnp.broadcast_to(col, (tok, 128)))[0:1, :]


def _query_side_kernel(nblk, scale):
    def kernel(*refs):
        q_ref, d_ref = refs[0], refs[1]
        k_refs = refs[2:2 + nblk]
        v_refs = refs[2 + nblk:2 + 2 * nblk]
        bias_ref = refs[2 + 2 * nblk]
        dq_ref, ld_ref = refs[3 + 2 * nblk], refs[4 + 2 * nblk]
        q = q_ref[...]
        d = d_ref[...]
        logits = []
        for j in range(nblk):
            raw = lax.dot_general(q, k_refs[j][...], (((1,), (1,)), ((), ())),
                                  preferred_element_type=jnp.float32)
            logits.append(raw * scale + bias_ref[:, j * TILE:(j + 1) * TILE])
        top = logits[0].max(axis=1, keepdims=True)
        for j in range(1, nblk):
            top = jnp.maximum(top, logits[j].max(axis=1, keepdims=True))
        denom = jnp.exp(logits[0] - top).sum(axis=1, keepdims=True)
        for j in range(1, nblk):
            denom = denom + jnp.exp(logits[j] - top).sum(axis=1, keepdims=True)
        lse = top + jnp.log(denom)
        probs = [jnp.exp(item - lse) for item in logits]
        out = None
        for j in range(nblk):
            part = jnp.dot(probs[j].astype(jnp.bfloat16), v_refs[j][...],
                           preferred_element_type=jnp.float32)
            out = part if out is None else out + part
        delta = (d.astype(jnp.float32) * out).sum(axis=1, keepdims=True)
        dq = None
        for j in range(nblk):
            dprobs = lax.dot_general(d, v_refs[j][...], (((1,), (1,)), ((), ())),
                                     preferred_element_type=jnp.float32)
            dscores = (probs[j] * (dprobs - delta)).astype(jnp.bfloat16)
            part = jnp.dot(dscores, k_refs[j][...], preferred_element_type=jnp.float32)
            dq = part if dq is None else dq + part
        dq_ref[...] = (dq * scale).astype(dq_ref.dtype)
        ld_ref[0:1, :] = _row(lse, TILE)
        ld_ref[1:2, :] = _row(delta, TILE)

    return kernel


def _key_side_kernel(nblk, scale):
    def kernel(*refs):
        k_ref, v_ref = refs[0], refs[1]
        q_refs = refs[2:2 + nblk]
        d_refs = refs[2 + nblk:2 + 2 * nblk]
        ld_refs = refs[2 + 2 * nblk:2 + 3 * nblk]
        bias_ref = refs[2 + 3 * nblk]
        out_ref = refs[3 + 3 * nblk]
        k = k_ref[...]
        v = v_ref[...]
        dk = None
        dv = None
        for j in range(nblk):
            q = q_refs[j][...]
            d = d_refs[j][...]
            lse = ld_refs[j][0:1, :]
            delta = ld_refs[j][1:2, :]
            raw = lax.dot_general(k, q, (((1,), (1,)), ((), ())),
                                  preferred_element_type=jnp.float32)
            logit = raw * scale + bias_ref[:, j * TILE:(j + 1) * TILE]
            prob = jnp.exp(logit - lse)
            dprobs = lax.dot_general(v, d, (((1,), (1,)), ((), ())),
                                     preferred_element_type=jnp.float32)
            dscores = (prob * (dprobs - delta)).astype(jnp.bfloat16)
            part_k = jnp.dot(dscores, q, preferred_element_type=jnp.float32)
            part_v = jnp.dot(prob.astype(jnp.bfloat16), d, preferred_element_type=jnp.float32)
            dk = part_k if dk is None else dk + part_k
            dv = part_v if dv is None else dv + part_v
        out_ref[:, 0:HEAD_DIM] = (dk * scale).astype(out_ref.dtype)
        out_ref[:, HEAD_DIM:2 * HEAD_DIM] = dv.astype(out_ref.dtype)

    return kernel


def _plan(tok_in, ctx_n, head_n):
    clo_n = 1
    while (clo_n * 2 <= ctx_n and ctx_n % (clo_n * 2) == 0
           and tok_in * clo_n * head_n < PLANE_TOKENS):
        clo_n *= 2
    return clo_n


def _per_device(clo_n, attn_q, attn_k, attn_v, attn_dout, doc_ids):
    tok_in, full_width = attn_q.shape
    head_n = lax.axis_size("head")
    chi_n = lax.axis_size("chi")
    group = clo_n * head_n
    width = full_width // group
    heads_p = width // HEAD_DIM
    plane = tok_in * group
    n_tok = doc_ids.shape[0]
    scale = HEAD_DIM ** (-0.5)
    reach = min(-(-(MAX_DOC - 1) // plane), chi_n - 1)
    tile_reach = -(-(MAX_DOC - 1) // TILE)
    nblk = tile_reach + 1
    n_tiles = plane // TILE
    chi = lax.axis_index("chi")
    plane_start = chi * plane

    def to_plane(a, b):
        a = a.reshape(tok_in, head_n, clo_n, 1, width)
        b = b.reshape(tok_in, head_n, clo_n, 1, width)
        x = jnp.concatenate([a, b], axis=3).transpose(0, 2, 1, 3, 4).reshape(tok_in, 2 * full_width)
        return lax.all_to_all(x, ("clo", "head"), split_axis=1, concat_axis=0, tiled=True)

    kv = to_plane(attn_k, attn_v)
    kv_win = jnp.concatenate([shifted(kv, "chi", shift) for shift in range(reach, 0, -1)] + [kv], axis=0)
    qd = to_plane(attn_q, attn_dout)
    qd_win = jnp.concatenate([qd] + [shifted(qd, "chi", -shift) for shift in range(1, reach + 1)], axis=0)

    pad = (reach + 1) * plane
    docs_pad = jnp.concatenate([
        jnp.full((pad,), -1, jnp.int32), doc_ids.astype(jnp.int32), jnp.full((pad,), -1, jnp.int32)])
    span = nblk * TILE
    cols = jnp.arange(span, dtype=jnp.int32)
    rows = jnp.arange(TILE, dtype=jnp.int32)
    q_bias, k_bias = [], []
    for i in range(n_tiles):
        t_start = plane_start + i * TILE
        own_doc = lax.dynamic_slice_in_dim(docs_pad, t_start + pad, TILE)
        own_pos = t_start + rows
        k_start = t_start - tile_reach * TILE
        k_doc = lax.dynamic_slice_in_dim(docs_pad, k_start + pad, span)
        k_pos = k_start + cols
        mask = (k_pos[None, :] <= own_pos[:, None]) & (k_doc[None, :] == own_doc[:, None])
        q_bias.append(jnp.where(mask, 0.0, masked_value).astype(jnp.float32))
        q_doc = lax.dynamic_slice_in_dim(docs_pad, t_start + pad, span)
        q_pos = t_start + cols
        mask = (own_pos[:, None] <= q_pos[None, :]) & (own_doc[:, None] == q_doc[None, :])
        k_bias.append(jnp.where(mask, 0.0, masked_value).astype(jnp.float32))
    q_bias = jnp.concatenate(q_bias, axis=0)
    k_bias = jnp.concatenate(k_bias, axis=0)

    own_spec = pl.BlockSpec((TILE, HEAD_DIM), lambda i, h: (i, h))
    base = reach * n_tiles - tile_reach

    def col_spec(off):
        return pl.BlockSpec((TILE, HEAD_DIM), lambda i, h: (i, h + off))

    def kwin_spec(j, off):
        return pl.BlockSpec((TILE, HEAD_DIM), lambda i, h: (base + i + j, h + off))

    def qwin_spec(j, off):
        return pl.BlockSpec((TILE, HEAD_DIM), lambda i, h: (i + j, h + off))

    def ldwin_spec(j):
        return pl.BlockSpec((None, 2, TILE), lambda i, h: (h, 0, i + j))

    bias_spec = pl.BlockSpec((TILE, span), lambda i, h: (i, 0))
    ld_spec = pl.BlockSpec((None, 2, TILE), lambda i, h: (h, 0, i))
    params = pltpu.CompilerParams(dimension_semantics=("arbitrary", "arbitrary"))
    grid = (n_tiles, heads_p)

    dq, ld = pl.pallas_call(
        _query_side_kernel(nblk, scale),
        out_shape=(
            jax.ShapeDtypeStruct((plane, width), jnp.bfloat16),
            jax.ShapeDtypeStruct((heads_p, 2, plane), jnp.float32),
        ),
        grid=grid,
        in_specs=[col_spec(0), col_spec(heads_p)] + [kwin_spec(j, 0) for j in range(nblk)]
        + [kwin_spec(j, heads_p) for j in range(nblk)] + [bias_spec],
        out_specs=(own_spec, ld_spec),
        compiler_params=params,
        name="attn_query_side",
    )(qd, qd, *([kv_win] * (2 * nblk)), q_bias)

    ld_parts = [ld]
    for shift in range(1, reach + 1):
        ld_parts.append(shifted(ld, "chi", -shift))
    ld_win = jnp.concatenate(ld_parts, axis=2)

    def from_plane(x):
        return lax.all_to_all(x, "clo", split_axis=0, concat_axis=1, tiled=True)

    groups = 2 if heads_p % 2 == 0 else 1
    hg = heads_p // groups
    dkv_parts = []
    for g in range(groups):
        off = g * hg

        def gcol(extra, off=off):
            return pl.BlockSpec((TILE, HEAD_DIM), lambda i, h: (i, h + off + extra))

        def gwin(j, extra, off=off):
            return pl.BlockSpec((TILE, HEAD_DIM), lambda i, h: (i + j, h + off + extra))

        def gld(j, off=off):
            return pl.BlockSpec((None, 2, TILE), lambda i, h: (h + off, 0, i + j))

        dkv_g = pl.pallas_call(
            _key_side_kernel(nblk, scale),
            out_shape=jax.ShapeDtypeStruct((plane, 2 * hg * HEAD_DIM), jnp.bfloat16),
            grid=(n_tiles, hg),
            in_specs=[gcol(0), gcol(heads_p)] + [gwin(j, 0) for j in range(nblk)]
            + [gwin(j, heads_p) for j in range(nblk)] + [gld(j) for j in range(nblk)] + [bias_spec],
            out_specs=pl.BlockSpec((TILE, 2 * HEAD_DIM), lambda i, h: (i, h)),
            compiler_params=params,
            name="attn_key_side",
        )(kv, kv, *([qd_win] * (2 * nblk)), *([ld_win] * nblk), k_bias)
        dkv_parts.append(from_plane(dkv_g).reshape(-1, clo_n, 1, hg, 2, HEAD_DIM))

    dkv = jnp.concatenate(dkv_parts, axis=2)
    rows = dkv.shape[0]
    attn_dk = dkv[:, :, :, :, 0, :].reshape(rows, clo_n * width)
    attn_dv = dkv[:, :, :, :, 1, :].reshape(rows, clo_n * width)
    return (from_plane(dq), attn_dk, attn_dv)


def solution(mesh):
    ctx_n, head_n = mesh.devices.shape
    def fn(attn_q, attn_k, attn_v, attn_dout, doc_ids):
        tok_in = attn_q.shape[0] // (ctx_n * head_n)
        clo_n = _plan(tok_in, ctx_n, head_n)
        chi_n = ctx_n // clo_n
        sub = Mesh(np.asarray(mesh.devices).reshape(chi_n, clo_n, head_n), ("chi", "clo", "head"))
        inner = jax.shard_map(
            lambda *a: _per_device(clo_n, *a),
            mesh=sub,
            in_specs=(
                P(("chi", "clo", "head"), None),
                P(("chi", "clo", "head"), None),
                P(("chi", "clo", "head"), None),
                P(("chi", "clo", "head"), None),
                P(),
            ),
            out_specs=(P(("chi", "clo"), "head"), P(("chi", "clo"), "head"), P(("chi", "clo"), "head")),
            check_vma=False,
        )
        return inner(attn_q, attn_k, attn_v, attn_dout, doc_ids)
    return fn
```

```python
import jax
import jax.numpy as jnp
import numpy as np
from jax import lax
from jax.experimental import pallas as pl
from jax.experimental.pallas import tpu as pltpu
from jax.sharding import Mesh
from jax.sharding import PartitionSpec as P

HEAD_DIM = 128
MAX_DOC = 1024
PLANE_TOKENS = 1024
TILE = 256

masked_value = -1e30


def shifted(value, axis, steps):
    count = lax.axis_size(axis)
    leading, last = (max(0, -steps), min(count, count - steps))
    return lax.ppermute(value, axis, [(source, source + steps) for source in range(leading, last)])


def _row(col, tok):
    return jnp.transpose(jnp.broadcast_to(col, (tok, 128)))[0:1, :]


def _query_side_kernel(nblk, scale):
    def kernel(*refs):
        q_ref, d_ref = refs[0], refs[1]
        k_refs = refs[2:2 + nblk]
        v_refs = refs[2 + nblk:2 + 2 * nblk]
        bias_ref = refs[2 + 2 * nblk]
        dq_ref, ld_ref = refs[3 + 2 * nblk], refs[4 + 2 * nblk]
        q = q_ref[...]
        d = d_ref[...]
        logits = []
        for j in range(nblk):
            raw = lax.dot_general(q, k_refs[j][...], (((1,), (1,)), ((), ())),
                                  preferred_element_type=jnp.float32)
            logits.append(raw * scale + bias_ref[:, j * TILE:(j + 1) * TILE])
        top = logits[0].max(axis=1, keepdims=True)
        for j in range(1, nblk):
            top = jnp.maximum(top, logits[j].max(axis=1, keepdims=True))
        denom = jnp.exp(logits[0] - top).sum(axis=1, keepdims=True)
        for j in range(1, nblk):
            denom = denom + jnp.exp(logits[j] - top).sum(axis=1, keepdims=True)
        lse = top + jnp.log(denom)
        probs = [jnp.exp(item - lse) for item in logits]
        out = None
        for j in range(nblk):
            part = jnp.dot(probs[j].astype(jnp.bfloat16), v_refs[j][...],
                           preferred_element_type=jnp.float32)
            out = part if out is None else out + part
        delta = (d.astype(jnp.float32) * out).sum(axis=1, keepdims=True)
        dq = None
        for j in range(nblk):
            dprobs = lax.dot_general(d, v_refs[j][...], (((1,), (1,)), ((), ())),
                                     preferred_element_type=jnp.float32)
            dscores = (probs[j] * (dprobs - delta)).astype(jnp.bfloat16)
            part = jnp.dot(dscores, k_refs[j][...], preferred_element_type=jnp.float32)
            dq = part if dq is None else dq + part
        dq_ref[...] = (dq * scale).astype(dq_ref.dtype)
        ld_ref[0:1, :] = _row(lse, TILE)
        ld_ref[1:2, :] = _row(delta, TILE)

    return kernel


def _key_side_kernel(nblk, scale):
    def kernel(*refs):
        k_ref, v_ref = refs[0], refs[1]
        q_refs = refs[2:2 + nblk]
        d_refs = refs[2 + nblk:2 + 2 * nblk]
        ld_refs = refs[2 + 2 * nblk:2 + 3 * nblk]
        bias_ref = refs[2 + 3 * nblk]
        out_ref = refs[3 + 3 * nblk]
        k = k_ref[...]
        v = v_ref[...]
        dk = None
        dv = None
        for j in range(nblk):
            q = q_refs[j][...]
            d = d_refs[j][...]
            lse = ld_refs[j][0:1, :]
            delta = ld_refs[j][1:2, :]
            raw = lax.dot_general(k, q, (((1,), (1,)), ((), ())),
                                  preferred_element_type=jnp.float32)
            logit = raw * scale + bias_ref[:, j * TILE:(j + 1) * TILE]
            prob = jnp.exp(logit - lse)
            dprobs = lax.dot_general(v, d, (((1,), (1,)), ((), ())),
                                     preferred_element_type=jnp.float32)
            dscores = (prob * (dprobs - delta)).astype(jnp.bfloat16)
            part_k = jnp.dot(dscores, q, preferred_element_type=jnp.float32)
            part_v = jnp.dot(prob.astype(jnp.bfloat16), d, preferred_element_type=jnp.float32)
            dk = part_k if dk is None else dk + part_k
            dv = part_v if dv is None else dv + part_v
        out_ref[:, 0:HEAD_DIM] = (dk * scale).astype(out_ref.dtype)
        out_ref[:, HEAD_DIM:2 * HEAD_DIM] = dv.astype(out_ref.dtype)

    return kernel


def _plan(tok_in, ctx_n, head_n):
    clo_n = 1
    while (clo_n * 2 <= ctx_n and ctx_n % (clo_n * 2) == 0
           and tok_in * clo_n * head_n < PLANE_TOKENS):
        clo_n *= 2
    return clo_n


def _per_device(clo_n, attn_q, attn_k, attn_v, attn_dout, doc_ids):
    tok_in, full_width = attn_q.shape
    head_n = lax.axis_size("head")
    chi_n = lax.axis_size("chi")
    group = clo_n * head_n
    width = full_width // group
    heads_p = width // HEAD_DIM
    plane = tok_in * group
    n_tok = doc_ids.shape[0]
    scale = HEAD_DIM ** (-0.5)
    reach = min(-(-(MAX_DOC - 1) // plane), chi_n - 1)
    tile_reach = -(-(MAX_DOC - 1) // TILE)
    nblk = tile_reach + 1
    n_tiles = plane // TILE
    chi = lax.axis_index("chi")
    plane_start = chi * plane

    def to_plane(a, b):
        a = a.reshape(tok_in, head_n, clo_n, 1, width)
        b = b.reshape(tok_in, head_n, clo_n, 1, width)
        x = jnp.concatenate([a, b], axis=3).transpose(0, 2, 1, 3, 4).reshape(tok_in, 2 * full_width)
        return lax.all_to_all(x, ("clo", "head"), split_axis=1, concat_axis=0, tiled=True)

    kv = to_plane(attn_k, attn_v)
    split = reach == 1 and tile_reach * TILE == plane and n_tiles % 2 == 0
    if split:
        half = plane // 2
        prev_late = shifted(kv[half:], "chi", 1)
        early_src, prev_late = lax.optimization_barrier((kv[:half], prev_late))
        prev_early = shifted(early_src, "chi", 1)
    else:
        kv_win = jnp.concatenate([shifted(kv, "chi", shift) for shift in range(reach, 0, -1)] + [kv], axis=0)
    qd = to_plane(attn_q, attn_dout)
    qd_win = jnp.concatenate([qd] + [shifted(qd, "chi", -shift) for shift in range(1, reach + 1)], axis=0)

    pad = (reach + 1) * plane
    docs_pad = jnp.concatenate([
        jnp.full((pad,), -1, jnp.int32), doc_ids.astype(jnp.int32), jnp.full((pad,), -1, jnp.int32)])
    span = nblk * TILE
    cols = jnp.arange(span, dtype=jnp.int32)
    rows = jnp.arange(TILE, dtype=jnp.int32)
    q_bias, k_bias = [], []
    for i in range(n_tiles):
        t_start = plane_start + i * TILE
        own_doc = lax.dynamic_slice_in_dim(docs_pad, t_start + pad, TILE)
        own_pos = t_start + rows
        k_start = t_start - tile_reach * TILE
        k_doc = lax.dynamic_slice_in_dim(docs_pad, k_start + pad, span)
        k_pos = k_start + cols
        mask = (k_pos[None, :] <= own_pos[:, None]) & (k_doc[None, :] == own_doc[:, None])
        q_bias.append(jnp.where(mask, 0.0, masked_value).astype(jnp.float32))
        q_doc = lax.dynamic_slice_in_dim(docs_pad, t_start + pad, span)
        q_pos = t_start + cols
        mask = (own_pos[:, None] <= q_pos[None, :]) & (own_doc[:, None] == q_doc[None, :])
        k_bias.append(jnp.where(mask, 0.0, masked_value).astype(jnp.float32))
    q_bias = jnp.concatenate(q_bias, axis=0)
    k_bias = jnp.concatenate(k_bias, axis=0)

    own_spec = pl.BlockSpec((TILE, HEAD_DIM), lambda i, h: (i, h))
    base = reach * n_tiles - tile_reach

    def col_spec(off):
        return pl.BlockSpec((TILE, HEAD_DIM), lambda i, h: (i, h + off))

    def kwin_spec(j, off):
        return pl.BlockSpec((TILE, HEAD_DIM), lambda i, h: (base + i + j, h + off))

    def qwin_spec(j, off):
        return pl.BlockSpec((TILE, HEAD_DIM), lambda i, h: (i + j, h + off))

    def ldwin_spec(j):
        return pl.BlockSpec((None, 2, TILE), lambda i, h: (h, 0, i + j))

    bias_spec = pl.BlockSpec((TILE, span), lambda i, h: (i, 0))
    ld_spec = pl.BlockSpec((None, 2, TILE), lambda i, h: (h, 0, i))
    params = pltpu.CompilerParams(dimension_semantics=("arbitrary", "arbitrary"))
    grid = (n_tiles, heads_p)

    def query_side(window, i_off, count, w_base):
        def gcol(extra):
            return pl.BlockSpec((TILE, HEAD_DIM), lambda i, h: (i + i_off, h + extra))

        def gwin(j, extra):
            return pl.BlockSpec((TILE, HEAD_DIM), lambda i, h: (w_base + i + j, h + extra))

        return pl.pallas_call(
            _query_side_kernel(nblk, scale),
            out_shape=(
                jax.ShapeDtypeStruct((count * TILE, width), jnp.bfloat16),
                jax.ShapeDtypeStruct((heads_p, 2, count * TILE), jnp.float32),
            ),
            grid=(count, heads_p),
            in_specs=[gcol(0), gcol(heads_p)] + [gwin(j, 0) for j in range(nblk)]
            + [gwin(j, heads_p) for j in range(nblk)]
            + [pl.BlockSpec((TILE, span), lambda i, h: (i + i_off, 0))],
            out_specs=(own_spec, ld_spec),
            compiler_params=params,
            name="attn_query_side",
        )(qd, qd, *([window] * (2 * nblk)), q_bias)

    if split:
        late = n_tiles // 2
        dq_late, ld_late = query_side(jnp.concatenate([prev_late, kv], axis=0), late, n_tiles - late, 0)
        dq_late, ld_late, prev_early = lax.optimization_barrier((dq_late, ld_late, prev_early))
        dq_early, ld_early = query_side(
            jnp.concatenate([prev_early, prev_late, kv[:half]], axis=0), 0, late, 0)
        dq = jnp.concatenate([dq_early, dq_late], axis=0)
        ld = jnp.concatenate([ld_early, ld_late], axis=2)
    else:
        dq, ld = query_side(kv_win, 0, n_tiles, base)

    ld_parts = [ld]
    for shift in range(1, reach + 1):
        ld_parts.append(shifted(ld, "chi", -shift))
    ld_win = jnp.concatenate(ld_parts, axis=2)

    def from_plane(x):
        return lax.all_to_all(x, "clo", split_axis=0, concat_axis=1, tiled=True)

    groups = 2 if heads_p % 2 == 0 else 1
    hg = heads_p // groups
    dkv_parts = []
    for g in range(groups):
        off = g * hg

        def gcol(extra, off=off):
            return pl.BlockSpec((TILE, HEAD_DIM), lambda i, h: (i, h + off + extra))

        def gwin(j, extra, off=off):
            return pl.BlockSpec((TILE, HEAD_DIM), lambda i, h: (i + j, h + off + extra))

        def gld(j, off=off):
            return pl.BlockSpec((None, 2, TILE), lambda i, h: (h + off, 0, i + j))

        dkv_g = pl.pallas_call(
            _key_side_kernel(nblk, scale),
            out_shape=jax.ShapeDtypeStruct((plane, 2 * hg * HEAD_DIM), jnp.bfloat16),
            grid=(n_tiles, hg),
            in_specs=[gcol(0), gcol(heads_p)] + [gwin(j, 0) for j in range(nblk)]
            + [gwin(j, heads_p) for j in range(nblk)] + [gld(j) for j in range(nblk)] + [bias_spec],
            out_specs=pl.BlockSpec((TILE, 2 * HEAD_DIM), lambda i, h: (i, h)),
            compiler_params=params,
            name="attn_key_side",
        )(kv, kv, *([qd_win] * (2 * nblk)), *([ld_win] * nblk), k_bias)
        dkv_parts.append(from_plane(dkv_g).reshape(-1, clo_n, 1, hg, 2, HEAD_DIM))

    dkv = jnp.concatenate(dkv_parts, axis=2)
    rows = dkv.shape[0]
    attn_dk = dkv[:, :, :, :, 0, :].reshape(rows, clo_n * width)
    attn_dv = dkv[:, :, :, :, 1, :].reshape(rows, clo_n * width)
    return (from_plane(dq), attn_dk, attn_dv)


def solution(mesh):
    ctx_n, head_n = mesh.devices.shape
    def fn(attn_q, attn_k, attn_v, attn_dout, doc_ids):
        tok_in = attn_q.shape[0] // (ctx_n * head_n)
        clo_n = _plan(tok_in, ctx_n, head_n)
        chi_n = ctx_n // clo_n
        sub = Mesh(np.asarray(mesh.devices).reshape(chi_n, clo_n, head_n), ("chi", "clo", "head"))
        inner = jax.shard_map(
            lambda *a: _per_device(clo_n, *a),
            mesh=sub,
            in_specs=(
                P(("chi", "clo", "head"), None),
                P(("chi", "clo", "head"), None),
                P(("chi", "clo", "head"), None),
                P(("chi", "clo", "head"), None),
                P(),
            ),
            out_specs=(P(("chi", "clo"), "head"), P(("chi", "clo"), "head"), P(("chi", "clo"), "head")),
            check_vma=False,
        )
        return inner(attn_q, attn_k, attn_v, attn_dout, doc_ids)
    return fn
```

```python
import jax
import jax.numpy as jnp
import numpy as np
from jax import lax
from jax.experimental import pallas as pl
from jax.experimental.pallas import tpu as pltpu
from jax.sharding import Mesh
from jax.sharding import PartitionSpec as P

HEAD_DIM = 128
MAX_DOC = 1024
PLANE_TOKENS = 1024
TILE = 256

masked_value = -1e30


def shifted(value, axis, steps):
    count = lax.axis_size(axis)
    leading, last = (max(0, -steps), min(count, count - steps))
    return lax.ppermute(value, axis, [(source, source + steps) for source in range(leading, last)])


def _row(col, tok):
    return jnp.transpose(jnp.broadcast_to(col, (tok, 128)))[0:1, :]


def _query_side_kernel(nblk, scale):
    def kernel(*refs):
        q_ref, d_ref = refs[0], refs[1]
        k_refs = refs[2:2 + nblk]
        v_refs = refs[2 + nblk:2 + 2 * nblk]
        bias_ref = refs[2 + 2 * nblk]
        dq_ref, ld_ref = refs[3 + 2 * nblk], refs[4 + 2 * nblk]
        q = q_ref[...]
        d = d_ref[...]
        logits = []
        for j in range(nblk):
            raw = lax.dot_general(q, k_refs[j][...], (((1,), (1,)), ((), ())),
                                  preferred_element_type=jnp.float32)
            logits.append(raw * scale + bias_ref[:, j * TILE:(j + 1) * TILE])
        top = logits[0].max(axis=1, keepdims=True)
        for j in range(1, nblk):
            top = jnp.maximum(top, logits[j].max(axis=1, keepdims=True))
        denom = jnp.exp(logits[0] - top).sum(axis=1, keepdims=True)
        for j in range(1, nblk):
            denom = denom + jnp.exp(logits[j] - top).sum(axis=1, keepdims=True)
        lse = top + jnp.log(denom)
        probs = [jnp.exp(item - lse) for item in logits]
        out = None
        for j in range(nblk):
            part = jnp.dot(probs[j].astype(jnp.bfloat16), v_refs[j][...],
                           preferred_element_type=jnp.float32)
            out = part if out is None else out + part
        delta = (d.astype(jnp.float32) * out).sum(axis=1, keepdims=True)
        dq = None
        for j in range(nblk):
            dprobs = lax.dot_general(d, v_refs[j][...], (((1,), (1,)), ((), ())),
                                     preferred_element_type=jnp.float32)
            dscores = (probs[j] * (dprobs - delta)).astype(jnp.bfloat16)
            part = jnp.dot(dscores, k_refs[j][...], preferred_element_type=jnp.float32)
            dq = part if dq is None else dq + part
        dq_ref[...] = (dq * scale).astype(dq_ref.dtype)
        ld_ref[0:1, :] = _row(lse, TILE)
        ld_ref[1:2, :] = _row(delta, TILE)

    return kernel


def _key_side_kernel(nblk, scale):
    def kernel(*refs):
        k_ref, v_ref = refs[0], refs[1]
        q_refs = refs[2:2 + nblk]
        d_refs = refs[2 + nblk:2 + 2 * nblk]
        ld_refs = refs[2 + 2 * nblk:2 + 3 * nblk]
        bias_ref = refs[2 + 3 * nblk]
        out_ref = refs[3 + 3 * nblk]
        k = k_ref[...]
        v = v_ref[...]
        dk = None
        dv = None
        for j in range(nblk):
            q = q_refs[j][...]
            d = d_refs[j][...]
            lse = ld_refs[j][0:1, :]
            delta = ld_refs[j][1:2, :]
            raw = lax.dot_general(k, q, (((1,), (1,)), ((), ())),
                                  preferred_element_type=jnp.float32)
            logit = raw * scale + bias_ref[:, j * TILE:(j + 1) * TILE]
            prob = jnp.exp(logit - lse)
            dprobs = lax.dot_general(v, d, (((1,), (1,)), ((), ())),
                                     preferred_element_type=jnp.float32)
            dscores = (prob * (dprobs - delta)).astype(jnp.bfloat16)
            part_k = jnp.dot(dscores, q, preferred_element_type=jnp.float32)
            part_v = jnp.dot(prob.astype(jnp.bfloat16), d, preferred_element_type=jnp.float32)
            dk = part_k if dk is None else dk + part_k
            dv = part_v if dv is None else dv + part_v
        out_ref[:, 0:HEAD_DIM] = (dk * scale).astype(out_ref.dtype)
        out_ref[:, HEAD_DIM:2 * HEAD_DIM] = dv.astype(out_ref.dtype)

    return kernel


def _plan(tok_in, ctx_n, head_n):
    clo_n = 1
    while (clo_n * 2 <= ctx_n and ctx_n % (clo_n * 2) == 0
           and tok_in * clo_n * head_n < PLANE_TOKENS):
        clo_n *= 2
    return clo_n


def _per_device(clo_n, attn_q, attn_k, attn_v, attn_dout, doc_ids):
    tok_in, full_width = attn_q.shape
    head_n = lax.axis_size("head")
    chi_n = lax.axis_size("chi")
    group = clo_n * head_n
    width = full_width // group
    heads_p = width // HEAD_DIM
    plane = tok_in * group
    n_tok = doc_ids.shape[0]
    scale = HEAD_DIM ** (-0.5)
    reach = min(-(-(MAX_DOC - 1) // plane), chi_n - 1)
    tile_reach = -(-(MAX_DOC - 1) // TILE)
    nblk = tile_reach + 1
    n_tiles = plane // TILE
    chi = lax.axis_index("chi")
    plane_start = chi * plane

    def to_plane(a, b):
        a = a.reshape(tok_in, head_n, clo_n, 1, width)
        b = b.reshape(tok_in, head_n, clo_n, 1, width)
        x = jnp.concatenate([a, b], axis=3).transpose(0, 2, 1, 3, 4).reshape(tok_in, 2 * full_width)
        return lax.all_to_all(x, ("clo", "head"), split_axis=1, concat_axis=0, tiled=True)

    kv = to_plane(attn_k, attn_v)
    split = reach == 1 and tile_reach * TILE == plane and n_tiles % 2 == 0
    if split:
        half = plane // 2
        prev_late = shifted(kv[half:], "chi", 1)
        early_src, prev_late = lax.optimization_barrier((kv[:half], prev_late))
        prev_early = shifted(early_src, "chi", 1)
    else:
        kv_win = jnp.concatenate([shifted(kv, "chi", shift) for shift in range(reach, 0, -1)] + [kv], axis=0)
    pad = (reach + 1) * plane
    docs_pad = jnp.concatenate([
        jnp.full((pad,), -1, jnp.int32), doc_ids.astype(jnp.int32), jnp.full((pad,), -1, jnp.int32)])
    span = nblk * TILE
    cols = jnp.arange(span, dtype=jnp.int32)
    rows = jnp.arange(TILE, dtype=jnp.int32)
    q_bias, k_bias = [], []
    for i in range(n_tiles):
        t_start = plane_start + i * TILE
        own_doc = lax.dynamic_slice_in_dim(docs_pad, t_start + pad, TILE)
        own_pos = t_start + rows
        k_start = t_start - tile_reach * TILE
        k_doc = lax.dynamic_slice_in_dim(docs_pad, k_start + pad, span)
        k_pos = k_start + cols
        mask = (k_pos[None, :] <= own_pos[:, None]) & (k_doc[None, :] == own_doc[:, None])
        q_bias.append(jnp.where(mask, 0.0, masked_value).astype(jnp.float32))
        q_doc = lax.dynamic_slice_in_dim(docs_pad, t_start + pad, span)
        q_pos = t_start + cols
        mask = (own_pos[:, None] <= q_pos[None, :]) & (own_doc[:, None] == q_doc[None, :])
        k_bias.append(jnp.where(mask, 0.0, masked_value).astype(jnp.float32))
    q_bias = jnp.concatenate(q_bias, axis=0)
    k_bias = jnp.concatenate(k_bias, axis=0)
    attn_q, attn_dout, q_bias, k_bias, kv = lax.optimization_barrier((attn_q, attn_dout, q_bias, k_bias, kv))
    qd = to_plane(attn_q, attn_dout)
    qd_win = jnp.concatenate([qd] + [shifted(qd, "chi", -shift) for shift in range(1, reach + 1)], axis=0)


    own_spec = pl.BlockSpec((TILE, HEAD_DIM), lambda i, h: (i, h))
    base = reach * n_tiles - tile_reach

    def col_spec(off):
        return pl.BlockSpec((TILE, HEAD_DIM), lambda i, h: (i, h + off))

    def kwin_spec(j, off):
        return pl.BlockSpec((TILE, HEAD_DIM), lambda i, h: (base + i + j, h + off))

    def qwin_spec(j, off):
        return pl.BlockSpec((TILE, HEAD_DIM), lambda i, h: (i + j, h + off))

    def ldwin_spec(j):
        return pl.BlockSpec((None, 2, TILE), lambda i, h: (h, 0, i + j))

    bias_spec = pl.BlockSpec((TILE, span), lambda i, h: (i, 0))
    ld_spec = pl.BlockSpec((None, 2, TILE), lambda i, h: (h, 0, i))
    params = pltpu.CompilerParams(dimension_semantics=("arbitrary", "arbitrary"))
    grid = (n_tiles, heads_p)

    def query_side(window, i_off, count, w_base):
        def gcol(extra):
            return pl.BlockSpec((TILE, HEAD_DIM), lambda i, h: (i + i_off, h + extra))

        def gwin(j, extra):
            return pl.BlockSpec((TILE, HEAD_DIM), lambda i, h: (w_base + i + j, h + extra))

        return pl.pallas_call(
            _query_side_kernel(nblk, scale),
            out_shape=(
                jax.ShapeDtypeStruct((count * TILE, width), jnp.bfloat16),
                jax.ShapeDtypeStruct((heads_p, 2, count * TILE), jnp.float32),
            ),
            grid=(count, heads_p),
            in_specs=[gcol(0), gcol(heads_p)] + [gwin(j, 0) for j in range(nblk)]
            + [gwin(j, heads_p) for j in range(nblk)]
            + [pl.BlockSpec((TILE, span), lambda i, h: (i + i_off, 0))],
            out_specs=(own_spec, ld_spec),
            compiler_params=params,
            name="attn_query_side",
        )(qd, qd, *([window] * (2 * nblk)), q_bias)

    if split:
        late = n_tiles // 2
        dq_late, ld_late = query_side(jnp.concatenate([prev_late, kv], axis=0), late, n_tiles - late, 0)
        dq_late, ld_late, prev_early = lax.optimization_barrier((dq_late, ld_late, prev_early))
        dq_early, ld_early = query_side(
            jnp.concatenate([prev_early, prev_late, kv[:half]], axis=0), 0, late, 0)
        dq = jnp.concatenate([dq_early, dq_late], axis=0)
        ld = jnp.concatenate([ld_early, ld_late], axis=2)
    else:
        dq, ld = query_side(kv_win, 0, n_tiles, base)

    ld_parts = [ld]
    for shift in range(1, reach + 1):
        ld_parts.append(shifted(ld, "chi", -shift))
    ld_win = jnp.concatenate(ld_parts, axis=2)

    def from_plane(x):
        return lax.all_to_all(x, "clo", split_axis=0, concat_axis=1, tiled=True)

    groups = 2 if heads_p % 2 == 0 else 1
    hg = heads_p // groups
    dkv_parts = []
    for g in range(groups):
        off = g * hg

        def gcol(extra, off=off):
            return pl.BlockSpec((TILE, HEAD_DIM), lambda i, h: (i, h + off + extra))

        def gwin(j, extra, off=off):
            return pl.BlockSpec((TILE, HEAD_DIM), lambda i, h: (i + j, h + off + extra))

        def gld(j, off=off):
            return pl.BlockSpec((None, 2, TILE), lambda i, h: (h + off, 0, i + j))

        dkv_g = pl.pallas_call(
            _key_side_kernel(nblk, scale),
            out_shape=jax.ShapeDtypeStruct((plane, 2 * hg * HEAD_DIM), jnp.bfloat16),
            grid=(n_tiles, hg),
            in_specs=[gcol(0), gcol(heads_p)] + [gwin(j, 0) for j in range(nblk)]
            + [gwin(j, heads_p) for j in range(nblk)] + [gld(j) for j in range(nblk)] + [bias_spec],
            out_specs=pl.BlockSpec((TILE, 2 * HEAD_DIM), lambda i, h: (i, h)),
            compiler_params=params,
            name="attn_key_side",
        )(kv, kv, *([qd_win] * (2 * nblk)), *([ld_win] * nblk), k_bias)
        dkv_parts.append(from_plane(dkv_g).reshape(-1, clo_n, 1, hg, 2, HEAD_DIM))

    dkv = jnp.concatenate(dkv_parts, axis=2)
    rows = dkv.shape[0]
    attn_dk = dkv[:, :, :, :, 0, :].reshape(rows, clo_n * width)
    attn_dv = dkv[:, :, :, :, 1, :].reshape(rows, clo_n * width)
    return (from_plane(dq), attn_dk, attn_dv)


def solution(mesh):
    ctx_n, head_n = mesh.devices.shape
    def fn(attn_q, attn_k, attn_v, attn_dout, doc_ids):
        tok_in = attn_q.shape[0] // (ctx_n * head_n)
        clo_n = _plan(tok_in, ctx_n, head_n)
        chi_n = ctx_n // clo_n
        sub = Mesh(np.asarray(mesh.devices).reshape(chi_n, clo_n, head_n), ("chi", "clo", "head"))
        inner = jax.shard_map(
            lambda *a: _per_device(clo_n, *a),
            mesh=sub,
            in_specs=(
                P(("chi", "clo", "head"), None),
                P(("chi", "clo", "head"), None),
                P(("chi", "clo", "head"), None),
                P(("chi", "clo", "head"), None),
                P(),
            ),
            out_specs=(P(("chi", "clo"), "head"), P(("chi", "clo"), "head"), P(("chi", "clo"), "head")),
            check_vma=False,
        )
        return inner(attn_q, attn_k, attn_v, attn_dout, doc_ids)
    return fn
```

```python
import jax
import jax.numpy as jnp
import numpy as np
from jax import lax
from jax.experimental import pallas as pl
from jax.experimental.pallas import tpu as pltpu
from jax.sharding import Mesh
from jax.sharding import PartitionSpec as P

HEAD_DIM = 128
MAX_DOC = 1024
PLANE_TOKENS = 1024
TILE = 256

masked_value = -1e30


def shifted(value, axis, steps):
    count = lax.axis_size(axis)
    leading, last = (max(0, -steps), min(count, count - steps))
    return lax.ppermute(value, axis, [(source, source + steps) for source in range(leading, last)])


def _row(col, tok):
    return jnp.transpose(jnp.broadcast_to(col, (tok, 128)))[0:1, :]


def _query_side_kernel(nblk, scale):
    def kernel(*refs):
        q_ref, d_ref = refs[0], refs[1]
        k_refs = refs[2:2 + nblk]
        v_refs = refs[2 + nblk:2 + 2 * nblk]
        bias_ref = refs[2 + 2 * nblk]
        dq_ref, ld_ref = refs[3 + 2 * nblk], refs[4 + 2 * nblk]
        q = q_ref[...]
        d = d_ref[...]
        logits = []
        for j in range(nblk):
            raw = lax.dot_general(q, k_refs[j][...], (((1,), (1,)), ((), ())),
                                  preferred_element_type=jnp.float32)
            logits.append(raw * scale + bias_ref[:, j * TILE:(j + 1) * TILE])
        top = logits[0].max(axis=1, keepdims=True)
        for j in range(1, nblk):
            top = jnp.maximum(top, logits[j].max(axis=1, keepdims=True))
        denom = jnp.exp(logits[0] - top).sum(axis=1, keepdims=True)
        for j in range(1, nblk):
            denom = denom + jnp.exp(logits[j] - top).sum(axis=1, keepdims=True)
        lse = top + jnp.log(denom)
        probs = [jnp.exp(item - lse) for item in logits]
        out = None
        for j in range(nblk):
            part = jnp.dot(probs[j].astype(jnp.bfloat16), v_refs[j][...],
                           preferred_element_type=jnp.float32)
            out = part if out is None else out + part
        delta = (d.astype(jnp.float32) * out).sum(axis=1, keepdims=True)
        dq = None
        for j in range(nblk):
            dprobs = lax.dot_general(d, v_refs[j][...], (((1,), (1,)), ((), ())),
                                     preferred_element_type=jnp.float32)
            dscores = (probs[j] * (dprobs - delta)).astype(jnp.bfloat16)
            part = jnp.dot(dscores, k_refs[j][...], preferred_element_type=jnp.float32)
            dq = part if dq is None else dq + part
        dq_ref[...] = (dq * scale).astype(dq_ref.dtype)
        ld_ref[0:1, :] = _row(lse, TILE)
        ld_ref[1:2, :] = _row(delta, TILE)

    return kernel


def _key_side_kernel(nblk, scale):
    def kernel(*refs):
        k_ref, v_ref = refs[0], refs[1]
        q_refs = refs[2:2 + nblk]
        d_refs = refs[2 + nblk:2 + 2 * nblk]
        ld_refs = refs[2 + 2 * nblk:2 + 3 * nblk]
        bias_ref = refs[2 + 3 * nblk]
        out_ref = refs[3 + 3 * nblk]
        k = k_ref[...]
        v = v_ref[...]
        dk = None
        dv = None
        for j in range(nblk):
            q = q_refs[j][...]
            d = d_refs[j][...]
            lse = ld_refs[j][0:1, :]
            delta = ld_refs[j][1:2, :]
            raw = lax.dot_general(k, q, (((1,), (1,)), ((), ())),
                                  preferred_element_type=jnp.float32)
            logit = raw * scale + bias_ref[:, j * TILE:(j + 1) * TILE]
            prob = jnp.exp(logit - lse)
            dprobs = lax.dot_general(v, d, (((1,), (1,)), ((), ())),
                                     preferred_element_type=jnp.float32)
            dscores = (prob * (dprobs - delta)).astype(jnp.bfloat16)
            part_k = jnp.dot(dscores, q, preferred_element_type=jnp.float32)
            part_v = jnp.dot(prob.astype(jnp.bfloat16), d, preferred_element_type=jnp.float32)
            dk = part_k if dk is None else dk + part_k
            dv = part_v if dv is None else dv + part_v
        out_ref[:, 0:HEAD_DIM] = (dk * scale).astype(out_ref.dtype)
        out_ref[:, HEAD_DIM:2 * HEAD_DIM] = dv.astype(out_ref.dtype)

    return kernel


def _plan(tok_in, ctx_n, head_n):
    clo_n = 1
    while (clo_n * 2 <= ctx_n and ctx_n % (clo_n * 2) == 0
           and tok_in * clo_n * head_n < PLANE_TOKENS):
        clo_n *= 2
    return clo_n


def _per_device(clo_n, attn_q, attn_k, attn_v, attn_dout, doc_ids):
    tok_in, full_width = attn_q.shape
    head_n = lax.axis_size("head")
    chi_n = lax.axis_size("chi")
    group = clo_n * head_n
    width = full_width // group
    heads_p = width // HEAD_DIM
    plane = tok_in * group
    n_tok = doc_ids.shape[0]
    scale = HEAD_DIM ** (-0.5)
    reach = min(-(-(MAX_DOC - 1) // plane), chi_n - 1)
    tile_reach = -(-(MAX_DOC - 1) // TILE)
    nblk = tile_reach + 1
    n_tiles = plane // TILE
    chi = lax.axis_index("chi")
    plane_start = chi * plane

    def to_plane(a, b, tied=None):
        a = a.reshape(tok_in, head_n, clo_n, 1, width)
        b = b.reshape(tok_in, head_n, clo_n, 1, width)
        x = jnp.concatenate([a, b], axis=3).transpose(0, 2, 1, 3, 4).reshape(tok_in, 2 * full_width)
        if tied is not None:
            x, tied = lax.optimization_barrier((x, tied))
        return lax.all_to_all(x, ("clo", "head"), split_axis=1, concat_axis=0, tiled=True), tied

    kv, _ = to_plane(attn_k, attn_v)
    split = reach == 1 and tile_reach * TILE == plane and n_tiles % 2 == 0
    if split:
        half = plane // 2
        prev_late = shifted(kv[half:], "chi", 1)
        early_src, prev_late = lax.optimization_barrier((kv[:half], prev_late))
        prev_early = shifted(early_src, "chi", 1)
    else:
        kv_win = jnp.concatenate([shifted(kv, "chi", shift) for shift in range(reach, 0, -1)] + [kv], axis=0)
    pad = (reach + 1) * plane
    docs_pad = jnp.concatenate([
        jnp.full((pad,), -1, jnp.int32), doc_ids.astype(jnp.int32), jnp.full((pad,), -1, jnp.int32)])
    span = nblk * TILE
    cols = jnp.arange(span, dtype=jnp.int32)
    rows = jnp.arange(TILE, dtype=jnp.int32)
    q_bias, k_bias = [], []
    for i in range(n_tiles):
        t_start = plane_start + i * TILE
        own_doc = lax.dynamic_slice_in_dim(docs_pad, t_start + pad, TILE)
        own_pos = t_start + rows
        k_start = t_start - tile_reach * TILE
        k_doc = lax.dynamic_slice_in_dim(docs_pad, k_start + pad, span)
        k_pos = k_start + cols
        mask = (k_pos[None, :] <= own_pos[:, None]) & (k_doc[None, :] == own_doc[:, None])
        q_bias.append(jnp.where(mask, 0.0, masked_value).astype(jnp.float32))
        q_doc = lax.dynamic_slice_in_dim(docs_pad, t_start + pad, span)
        q_pos = t_start + cols
        mask = (own_pos[:, None] <= q_pos[None, :]) & (own_doc[:, None] == q_doc[None, :])
        k_bias.append(jnp.where(mask, 0.0, masked_value).astype(jnp.float32))
    q_bias = jnp.concatenate(q_bias, axis=0)
    k_bias = jnp.concatenate(k_bias, axis=0)
    qd, (q_bias, k_bias) = to_plane(attn_q, attn_dout, (q_bias, k_bias))
    qd_win = jnp.concatenate([qd] + [shifted(qd, "chi", -shift) for shift in range(1, reach + 1)], axis=0)


    own_spec = pl.BlockSpec((TILE, HEAD_DIM), lambda i, h: (i, h))
    base = reach * n_tiles - tile_reach

    def col_spec(off):
        return pl.BlockSpec((TILE, HEAD_DIM), lambda i, h: (i, h + off))

    def kwin_spec(j, off):
        return pl.BlockSpec((TILE, HEAD_DIM), lambda i, h: (base + i + j, h + off))

    def qwin_spec(j, off):
        return pl.BlockSpec((TILE, HEAD_DIM), lambda i, h: (i + j, h + off))

    def ldwin_spec(j):
        return pl.BlockSpec((None, 2, TILE), lambda i, h: (h, 0, i + j))

    bias_spec = pl.BlockSpec((TILE, span), lambda i, h: (i, 0))
    ld_spec = pl.BlockSpec((None, 2, TILE), lambda i, h: (h, 0, i))
    params = pltpu.CompilerParams(dimension_semantics=("arbitrary", "arbitrary"))
    grid = (n_tiles, heads_p)

    def query_side(window, i_off, count, w_base):
        def gcol(extra):
            return pl.BlockSpec((TILE, HEAD_DIM), lambda i, h: (i + i_off, h + extra))

        def gwin(j, extra):
            return pl.BlockSpec((TILE, HEAD_DIM), lambda i, h: (w_base + i + j, h + extra))

        return pl.pallas_call(
            _query_side_kernel(nblk, scale),
            out_shape=(
                jax.ShapeDtypeStruct((count * TILE, width), jnp.bfloat16),
                jax.ShapeDtypeStruct((heads_p, 2, count * TILE), jnp.float32),
            ),
            grid=(count, heads_p),
            in_specs=[gcol(0), gcol(heads_p)] + [gwin(j, 0) for j in range(nblk)]
            + [gwin(j, heads_p) for j in range(nblk)]
            + [pl.BlockSpec((TILE, span), lambda i, h: (i + i_off, 0))],
            out_specs=(own_spec, ld_spec),
            compiler_params=params,
            name="attn_query_side",
        )(qd, qd, *([window] * (2 * nblk)), q_bias)

    if split:
        late = n_tiles // 2
        dq_late, ld_late = query_side(jnp.concatenate([prev_late, kv], axis=0), late, n_tiles - late, 0)
        dq_late, ld_late, prev_early = lax.optimization_barrier((dq_late, ld_late, prev_early))
        dq_early, ld_early = query_side(
            jnp.concatenate([prev_early, prev_late, kv[:half]], axis=0), 0, late, 0)
        dq = jnp.concatenate([dq_early, dq_late], axis=0)
        ld = jnp.concatenate([ld_early, ld_late], axis=2)
    else:
        dq, ld = query_side(kv_win, 0, n_tiles, base)

    ld_parts = [ld]
    for shift in range(1, reach + 1):
        ld_parts.append(shifted(ld, "chi", -shift))
    ld_win = jnp.concatenate(ld_parts, axis=2)

    def from_plane(x):
        return lax.all_to_all(x, "clo", split_axis=0, concat_axis=1, tiled=True)

    groups = 2 if heads_p % 2 == 0 else 1
    hg = heads_p // groups
    dkv_parts = []
    for g in range(groups):
        off = g * hg

        def gcol(extra, off=off):
            return pl.BlockSpec((TILE, HEAD_DIM), lambda i, h: (i, h + off + extra))

        def gwin(j, extra, off=off):
            return pl.BlockSpec((TILE, HEAD_DIM), lambda i, h: (i + j, h + off + extra))

        def gld(j, off=off):
            return pl.BlockSpec((None, 2, TILE), lambda i, h: (h + off, 0, i + j))

        dkv_g = pl.pallas_call(
            _key_side_kernel(nblk, scale),
            out_shape=jax.ShapeDtypeStruct((plane, 2 * hg * HEAD_DIM), jnp.bfloat16),
            grid=(n_tiles, hg),
            in_specs=[gcol(0), gcol(heads_p)] + [gwin(j, 0) for j in range(nblk)]
            + [gwin(j, heads_p) for j in range(nblk)] + [gld(j) for j in range(nblk)] + [bias_spec],
            out_specs=pl.BlockSpec((TILE, 2 * HEAD_DIM), lambda i, h: (i, h)),
            compiler_params=params,
            name="attn_key_side",
        )(kv, kv, *([qd_win] * (2 * nblk)), *([ld_win] * nblk), k_bias)
        dkv_parts.append(from_plane(dkv_g).reshape(-1, clo_n, 1, hg, 2, HEAD_DIM))

    dkv = jnp.concatenate(dkv_parts, axis=2)
    rows = dkv.shape[0]
    attn_dk = dkv[:, :, :, :, 0, :].reshape(rows, clo_n * width)
    attn_dv = dkv[:, :, :, :, 1, :].reshape(rows, clo_n * width)
    return (from_plane(dq), attn_dk, attn_dv)


def solution(mesh):
    ctx_n, head_n = mesh.devices.shape
    def fn(attn_q, attn_k, attn_v, attn_dout, doc_ids):
        tok_in = attn_q.shape[0] // (ctx_n * head_n)
        clo_n = _plan(tok_in, ctx_n, head_n)
        chi_n = ctx_n // clo_n
        sub = Mesh(np.asarray(mesh.devices).reshape(chi_n, clo_n, head_n), ("chi", "clo", "head"))
        inner = jax.shard_map(
            lambda *a: _per_device(clo_n, *a),
            mesh=sub,
            in_specs=(
                P(("chi", "clo", "head"), None),
                P(("chi", "clo", "head"), None),
                P(("chi", "clo", "head"), None),
                P(("chi", "clo", "head"), None),
                P(),
            ),
            out_specs=(P(("chi", "clo"), "head"), P(("chi", "clo"), "head"), P(("chi", "clo"), "head")),
            check_vma=False,
        )
        return inner(attn_q, attn_k, attn_v, attn_dout, doc_ids)
    return fn
```

```python
import jax
import jax.numpy as jnp
import numpy as np
from jax import lax
from jax.experimental import pallas as pl
from jax.experimental.pallas import tpu as pltpu
from jax.sharding import Mesh
from jax.sharding import PartitionSpec as P

HEAD_DIM = 128
MAX_DOC = 1024
PLANE_TOKENS = 1024
TILE = 256

masked_value = -1e30


def shifted(value, axis, steps):
    count = lax.axis_size(axis)
    leading, last = (max(0, -steps), min(count, count - steps))
    return lax.ppermute(value, axis, [(source, source + steps) for source in range(leading, last)])


def _row(col, tok):
    return jnp.transpose(jnp.broadcast_to(col, (tok, 128)))[0:1, :]


def _query_side_kernel(nblk, scale):
    def kernel(*refs):
        q_ref, d_ref = refs[0], refs[1]
        k_refs = refs[2:2 + nblk]
        v_refs = refs[2 + nblk:2 + 2 * nblk]
        bias_ref = refs[2 + 2 * nblk]
        dq_ref, ld_ref = refs[3 + 2 * nblk], refs[4 + 2 * nblk]
        q = q_ref[...]
        d = d_ref[...]
        logits = []
        for j in range(nblk):
            raw = lax.dot_general(q, k_refs[j][...], (((1,), (1,)), ((), ())),
                                  preferred_element_type=jnp.float32)
            logits.append(raw * scale + bias_ref[:, j * TILE:(j + 1) * TILE])
        top = logits[0].max(axis=1, keepdims=True)
        for j in range(1, nblk):
            top = jnp.maximum(top, logits[j].max(axis=1, keepdims=True))
        expd = [jnp.exp(item - top) for item in logits]
        denom = expd[0].sum(axis=1, keepdims=True)
        for j in range(1, nblk):
            denom = denom + expd[j].sum(axis=1, keepdims=True)
        lse = top + jnp.log(denom)
        inv = 1.0 / denom
        probs = [item * inv for item in expd]
        out = None
        for j in range(nblk):
            part = jnp.dot(probs[j].astype(jnp.bfloat16), v_refs[j][...],
                           preferred_element_type=jnp.float32)
            out = part if out is None else out + part
        delta = (d.astype(jnp.float32) * out).sum(axis=1, keepdims=True)
        dq = None
        for j in range(nblk):
            dprobs = lax.dot_general(d, v_refs[j][...], (((1,), (1,)), ((), ())),
                                     preferred_element_type=jnp.float32)
            dscores = (probs[j] * (dprobs - delta)).astype(jnp.bfloat16)
            part = jnp.dot(dscores, k_refs[j][...], preferred_element_type=jnp.float32)
            dq = part if dq is None else dq + part
        dq_ref[...] = (dq * scale).astype(dq_ref.dtype)
        ld_ref[0:1, :] = _row(lse, TILE)
        ld_ref[1:2, :] = _row(delta, TILE)

    return kernel


def _key_side_kernel(nblk, scale):
    def kernel(*refs):
        k_ref, v_ref = refs[0], refs[1]
        q_refs = refs[2:2 + nblk]
        d_refs = refs[2 + nblk:2 + 2 * nblk]
        ld_refs = refs[2 + 2 * nblk:2 + 3 * nblk]
        bias_ref = refs[2 + 3 * nblk]
        out_ref = refs[3 + 3 * nblk]
        k = k_ref[...]
        v = v_ref[...]
        dk = None
        dv = None
        for j in range(nblk):
            q = q_refs[j][...]
            d = d_refs[j][...]
            lse = ld_refs[j][0:1, :]
            delta = ld_refs[j][1:2, :]
            raw = lax.dot_general(k, q, (((1,), (1,)), ((), ())),
                                  preferred_element_type=jnp.float32)
            logit = raw * scale + bias_ref[:, j * TILE:(j + 1) * TILE]
            prob = jnp.exp(logit - lse)
            dprobs = lax.dot_general(v, d, (((1,), (1,)), ((), ())),
                                     preferred_element_type=jnp.float32)
            dscores = (prob * (dprobs - delta)).astype(jnp.bfloat16)
            part_k = jnp.dot(dscores, q, preferred_element_type=jnp.float32)
            part_v = jnp.dot(prob.astype(jnp.bfloat16), d, preferred_element_type=jnp.float32)
            dk = part_k if dk is None else dk + part_k
            dv = part_v if dv is None else dv + part_v
        out_ref[:, 0:HEAD_DIM] = (dk * scale).astype(out_ref.dtype)
        out_ref[:, HEAD_DIM:2 * HEAD_DIM] = dv.astype(out_ref.dtype)

    return kernel


def _plan(tok_in, ctx_n, head_n):
    clo_n = 1
    while (clo_n * 2 <= ctx_n and ctx_n % (clo_n * 2) == 0
           and tok_in * clo_n * head_n < PLANE_TOKENS):
        clo_n *= 2
    return clo_n


def _per_device(clo_n, attn_q, attn_k, attn_v, attn_dout, doc_ids):
    tok_in, full_width = attn_q.shape
    head_n = lax.axis_size("head")
    chi_n = lax.axis_size("chi")
    group = clo_n * head_n
    width = full_width // group
    heads_p = width // HEAD_DIM
    plane = tok_in * group
    n_tok = doc_ids.shape[0]
    scale = HEAD_DIM ** (-0.5)
    reach = min(-(-(MAX_DOC - 1) // plane), chi_n - 1)
    tile_reach = -(-(MAX_DOC - 1) // TILE)
    nblk = tile_reach + 1
    n_tiles = plane // TILE
    chi = lax.axis_index("chi")
    plane_start = chi * plane

    def to_plane(a, b, tied=None):
        a = a.reshape(tok_in, head_n, clo_n, 1, width)
        b = b.reshape(tok_in, head_n, clo_n, 1, width)
        x = jnp.concatenate([a, b], axis=3).transpose(0, 2, 1, 3, 4).reshape(tok_in, 2 * full_width)
        if tied is not None:
            x, tied = lax.optimization_barrier((x, tied))
        return lax.all_to_all(x, ("clo", "head"), split_axis=1, concat_axis=0, tiled=True), tied

    kv, _ = to_plane(attn_k, attn_v)
    split = reach == 1 and tile_reach * TILE == plane and n_tiles % 2 == 0
    if split:
        half = plane // 2
        prev_late = shifted(kv[half:], "chi", 1)
        early_src, prev_late = lax.optimization_barrier((kv[:half], prev_late))
        prev_early = shifted(early_src, "chi", 1)
    else:
        kv_win = jnp.concatenate([shifted(kv, "chi", shift) for shift in range(reach, 0, -1)] + [kv], axis=0)
    pad = (reach + 1) * plane
    docs_pad = jnp.concatenate([
        jnp.full((pad,), -1, jnp.int32), doc_ids.astype(jnp.int32), jnp.full((pad,), -1, jnp.int32)])
    span = nblk * TILE
    cols = jnp.arange(span, dtype=jnp.int32)
    rows = jnp.arange(TILE, dtype=jnp.int32)
    q_bias, k_bias = [], []
    for i in range(n_tiles):
        t_start = plane_start + i * TILE
        own_doc = lax.dynamic_slice_in_dim(docs_pad, t_start + pad, TILE)
        own_pos = t_start + rows
        k_start = t_start - tile_reach * TILE
        k_doc = lax.dynamic_slice_in_dim(docs_pad, k_start + pad, span)
        k_pos = k_start + cols
        mask = (k_pos[None, :] <= own_pos[:, None]) & (k_doc[None, :] == own_doc[:, None])
        q_bias.append(jnp.where(mask, 0.0, masked_value).astype(jnp.float32))
        q_doc = lax.dynamic_slice_in_dim(docs_pad, t_start + pad, span)
        q_pos = t_start + cols
        mask = (own_pos[:, None] <= q_pos[None, :]) & (own_doc[:, None] == q_doc[None, :])
        k_bias.append(jnp.where(mask, 0.0, masked_value).astype(jnp.float32))
    q_bias = jnp.concatenate(q_bias, axis=0)
    k_bias = jnp.concatenate(k_bias, axis=0)
    qd, (q_bias, k_bias) = to_plane(attn_q, attn_dout, (q_bias, k_bias))
    qd_win = jnp.concatenate([qd] + [shifted(qd, "chi", -shift) for shift in range(1, reach + 1)], axis=0)


    own_spec = pl.BlockSpec((TILE, HEAD_DIM), lambda i, h: (i, h))
    base = reach * n_tiles - tile_reach

    def col_spec(off):
        return pl.BlockSpec((TILE, HEAD_DIM), lambda i, h: (i, h + off))

    def kwin_spec(j, off):
        return pl.BlockSpec((TILE, HEAD_DIM), lambda i, h: (base + i + j, h + off))

    def qwin_spec(j, off):
        return pl.BlockSpec((TILE, HEAD_DIM), lambda i, h: (i + j, h + off))

    def ldwin_spec(j):
        return pl.BlockSpec((None, 2, TILE), lambda i, h: (h, 0, i + j))

    bias_spec = pl.BlockSpec((TILE, span), lambda i, h: (i, 0))
    ld_spec = pl.BlockSpec((None, 2, TILE), lambda i, h: (h, 0, i))
    params = pltpu.CompilerParams(dimension_semantics=("arbitrary", "arbitrary"))
    grid = (n_tiles, heads_p)

    def query_side(window, i_off, count, w_base):
        def gcol(extra):
            return pl.BlockSpec((TILE, HEAD_DIM), lambda i, h: (i + i_off, h + extra))

        def gwin(j, extra):
            return pl.BlockSpec((TILE, HEAD_DIM), lambda i, h: (w_base + i + j, h + extra))

        return pl.pallas_call(
            _query_side_kernel(nblk, scale),
            out_shape=(
                jax.ShapeDtypeStruct((count * TILE, width), jnp.bfloat16),
                jax.ShapeDtypeStruct((heads_p, 2, count * TILE), jnp.float32),
            ),
            grid=(count, heads_p),
            in_specs=[gcol(0), gcol(heads_p)] + [gwin(j, 0) for j in range(nblk)]
            + [gwin(j, heads_p) for j in range(nblk)]
            + [pl.BlockSpec((TILE, span), lambda i, h: (i + i_off, 0))],
            out_specs=(own_spec, ld_spec),
            compiler_params=params,
            name="attn_query_side",
        )(qd, qd, *([window] * (2 * nblk)), q_bias)

    if split:
        late = n_tiles // 2
        dq_late, ld_late = query_side(jnp.concatenate([prev_late, kv], axis=0), late, n_tiles - late, 0)
        dq_late, ld_late, prev_early = lax.optimization_barrier((dq_late, ld_late, prev_early))
        dq_early, ld_early = query_side(
            jnp.concatenate([prev_early, prev_late, kv[:half]], axis=0), 0, late, 0)
        dq = jnp.concatenate([dq_early, dq_late], axis=0)
        ld = jnp.concatenate([ld_early, ld_late], axis=2)
    else:
        dq, ld = query_side(kv_win, 0, n_tiles, base)

    ld_parts = [ld]
    for shift in range(1, reach + 1):
        ld_parts.append(shifted(ld, "chi", -shift))
    ld_win = jnp.concatenate(ld_parts, axis=2)

    def from_plane(x):
        return lax.all_to_all(x, "clo", split_axis=0, concat_axis=1, tiled=True)

    groups = 2 if heads_p % 2 == 0 else 1
    hg = heads_p // groups
    dkv_parts = []
    for g in range(groups):
        off = g * hg

        def gcol(extra, off=off):
            return pl.BlockSpec((TILE, HEAD_DIM), lambda i, h: (i, h + off + extra))

        def gwin(j, extra, off=off):
            return pl.BlockSpec((TILE, HEAD_DIM), lambda i, h: (i + j, h + off + extra))

        def gld(j, off=off):
            return pl.BlockSpec((None, 2, TILE), lambda i, h: (h + off, 0, i + j))

        dkv_g = pl.pallas_call(
            _key_side_kernel(nblk, scale),
            out_shape=jax.ShapeDtypeStruct((plane, 2 * hg * HEAD_DIM), jnp.bfloat16),
            grid=(n_tiles, hg),
            in_specs=[gcol(0), gcol(heads_p)] + [gwin(j, 0) for j in range(nblk)]
            + [gwin(j, heads_p) for j in range(nblk)] + [gld(j) for j in range(nblk)] + [bias_spec],
            out_specs=pl.BlockSpec((TILE, 2 * HEAD_DIM), lambda i, h: (i, h)),
            compiler_params=params,
            name="attn_key_side",
        )(kv, kv, *([qd_win] * (2 * nblk)), *([ld_win] * nblk), k_bias)
        dkv_parts.append(from_plane(dkv_g).reshape(-1, clo_n, 1, hg, 2, HEAD_DIM))

    dkv = jnp.concatenate(dkv_parts, axis=2)
    rows = dkv.shape[0]
    attn_dk = dkv[:, :, :, :, 0, :].reshape(rows, clo_n * width)
    attn_dv = dkv[:, :, :, :, 1, :].reshape(rows, clo_n * width)
    return (from_plane(dq), attn_dk, attn_dv)


def solution(mesh):
    ctx_n, head_n = mesh.devices.shape
    def fn(attn_q, attn_k, attn_v, attn_dout, doc_ids):
        tok_in = attn_q.shape[0] // (ctx_n * head_n)
        clo_n = _plan(tok_in, ctx_n, head_n)
        chi_n = ctx_n // clo_n
        sub = Mesh(np.asarray(mesh.devices).reshape(chi_n, clo_n, head_n), ("chi", "clo", "head"))
        inner = jax.shard_map(
            lambda *a: _per_device(clo_n, *a),
            mesh=sub,
            in_specs=(
                P(("chi", "clo", "head"), None),
                P(("chi", "clo", "head"), None),
                P(("chi", "clo", "head"), None),
                P(("chi", "clo", "head"), None),
                P(),
            ),
            out_specs=(P(("chi", "clo"), "head"), P(("chi", "clo"), "head"), P(("chi", "clo"), "head")),
            check_vma=False,
        )
        return inner(attn_q, attn_k, attn_v, attn_dout, doc_ids)
    return fn
```

```python
import jax
import jax.numpy as jnp
import numpy as np
from jax import lax
from jax.experimental import pallas as pl
from jax.experimental.pallas import tpu as pltpu
from jax.sharding import Mesh
from jax.sharding import PartitionSpec as P

HEAD_DIM = 128
MAX_DOC = 1024
PLANE_TOKENS = 1024
TILE = 256

masked_value = -1e30


def shifted(value, axis, steps):
    count = lax.axis_size(axis)
    leading, last = (max(0, -steps), min(count, count - steps))
    return lax.ppermute(value, axis, [(source, source + steps) for source in range(leading, last)])


def _row(col, tok):
    return jnp.transpose(jnp.broadcast_to(col, (tok, 128)))[0:1, :]


def _query_side_kernel(nblk, scale):
    def kernel(*refs):
        q_ref, d_ref = refs[0], refs[1]
        k_refs = refs[2:2 + nblk]
        v_refs = refs[2 + nblk:2 + 2 * nblk]
        bias_ref = refs[2 + 2 * nblk]
        dq_ref, ld_ref = refs[3 + 2 * nblk], refs[4 + 2 * nblk]
        q = q_ref[...]
        d = d_ref[...]
        logits = []
        for j in range(nblk):
            raw = lax.dot_general(q, k_refs[j][...], (((1,), (1,)), ((), ())),
                                  preferred_element_type=jnp.float32)
            logits.append(raw * scale + bias_ref[:, j * TILE:(j + 1) * TILE])
        top = logits[0].max(axis=1, keepdims=True)
        for j in range(1, nblk):
            top = jnp.maximum(top, logits[j].max(axis=1, keepdims=True))
        expd = [jnp.exp(item - top) for item in logits]
        denom = expd[0].sum(axis=1, keepdims=True)
        for j in range(1, nblk):
            denom = denom + expd[j].sum(axis=1, keepdims=True)
        lse = top + jnp.log(denom)
        inv = 1.0 / denom
        probs = [item * inv for item in expd]
        out = None
        for j in range(nblk):
            part = jnp.dot(probs[j].astype(jnp.bfloat16), v_refs[j][...],
                           preferred_element_type=jnp.float32)
            out = part if out is None else out + part
        delta = (d.astype(jnp.float32) * out).sum(axis=1, keepdims=True)
        dq = None
        for j in range(nblk):
            dprobs = lax.dot_general(d, v_refs[j][...], (((1,), (1,)), ((), ())),
                                     preferred_element_type=jnp.float32)
            dscores = (probs[j] * (dprobs - delta)).astype(jnp.bfloat16)
            part = jnp.dot(dscores, k_refs[j][...], preferred_element_type=jnp.float32)
            dq = part if dq is None else dq + part
        dq_ref[...] = (dq * scale).astype(dq_ref.dtype)
        ld_ref[0:1, :] = _row(lse, TILE)
        ld_ref[1:2, :] = _row(delta, TILE)

    return kernel


def _key_side_kernel(nblk, scale):
    def kernel(*refs):
        k_ref, v_ref = refs[0], refs[1]
        q_refs = refs[2:2 + nblk]
        d_refs = refs[2 + nblk:2 + 2 * nblk]
        ld_refs = refs[2 + 2 * nblk:2 + 3 * nblk]
        bias_ref = refs[2 + 3 * nblk]
        out_ref = refs[3 + 3 * nblk]
        k = k_ref[...]
        v = v_ref[...]
        dk = None
        dv = None
        for j in range(nblk):
            q = q_refs[j][...]
            d = d_refs[j][...]
            lse = ld_refs[j][0:1, :]
            delta = ld_refs[j][1:2, :]
            raw = lax.dot_general(k, q, (((1,), (1,)), ((), ())),
                                  preferred_element_type=jnp.float32)
            logit = raw * scale + bias_ref[:, j * TILE:(j + 1) * TILE]
            prob = jnp.exp(logit - lse)
            dprobs = lax.dot_general(v, d, (((1,), (1,)), ((), ())),
                                     preferred_element_type=jnp.float32)
            dscores = (prob * (dprobs - delta)).astype(jnp.bfloat16)
            part_k = jnp.dot(dscores, q, preferred_element_type=jnp.float32)
            part_v = jnp.dot(prob.astype(jnp.bfloat16), d, preferred_element_type=jnp.float32)
            dk = part_k if dk is None else dk + part_k
            dv = part_v if dv is None else dv + part_v
        out_ref[:, 0:HEAD_DIM] = (dk * scale).astype(out_ref.dtype)
        out_ref[:, HEAD_DIM:2 * HEAD_DIM] = dv.astype(out_ref.dtype)

    return kernel


def _plan(tok_in, ctx_n, head_n):
    clo_n = 1
    while (clo_n * 2 <= ctx_n and ctx_n % (clo_n * 2) == 0
           and tok_in * clo_n * head_n < PLANE_TOKENS):
        clo_n *= 2
    return clo_n


def _per_device(clo_n, attn_q, attn_k, attn_v, attn_dout, doc_ids):
    tok_in, full_width = attn_q.shape
    head_n = lax.axis_size("head")
    chi_n = lax.axis_size("chi")
    group = clo_n * head_n
    width = full_width // group
    heads_p = width // HEAD_DIM
    plane = tok_in * group
    n_tok = doc_ids.shape[0]
    scale = HEAD_DIM ** (-0.5)
    reach = min(-(-(MAX_DOC - 1) // plane), chi_n - 1)
    tile_reach = -(-(MAX_DOC - 1) // TILE)
    nblk = tile_reach + 1
    n_tiles = plane // TILE
    chi = lax.axis_index("chi")
    plane_start = chi * plane

    def to_plane(a, b, tied=None):
        a = a.reshape(tok_in, head_n, clo_n, 1, width)
        b = b.reshape(tok_in, head_n, clo_n, 1, width)
        x = jnp.concatenate([a, b], axis=3).transpose(0, 2, 1, 3, 4).reshape(tok_in, 2 * full_width)
        if tied is not None:
            x, tied = lax.optimization_barrier((x, tied))
        return lax.all_to_all(x, ("clo", "head"), split_axis=1, concat_axis=0, tiled=True), tied

    kv, _ = to_plane(attn_k, attn_v)
    split = reach == 1 and tile_reach * TILE == plane and n_tiles % 2 == 0
    if split:
        half = plane // 2
        prev_late = shifted(kv[half:], "chi", 1)
        early_src, prev_late = lax.optimization_barrier((kv[:half], prev_late))
        prev_early = shifted(early_src, "chi", 1)
    else:
        kv_win = jnp.concatenate([shifted(kv, "chi", shift) for shift in range(reach, 0, -1)] + [kv], axis=0)
    pad = (reach + 1) * plane
    docs_pad = jnp.concatenate([
        jnp.full((pad,), -1, jnp.int32), doc_ids.astype(jnp.int32), jnp.full((pad,), -1, jnp.int32)])
    span = nblk * TILE
    cols = jnp.arange(span, dtype=jnp.int32)
    rows = jnp.arange(TILE, dtype=jnp.int32)
    q_bias, k_bias = [], []
    for i in range(n_tiles):
        t_start = plane_start + i * TILE
        own_doc = lax.dynamic_slice_in_dim(docs_pad, t_start + pad, TILE)
        own_pos = t_start + rows
        k_start = t_start - tile_reach * TILE
        k_doc = lax.dynamic_slice_in_dim(docs_pad, k_start + pad, span)
        k_pos = k_start + cols
        mask = (k_pos[None, :] <= own_pos[:, None]) & (k_doc[None, :] == own_doc[:, None])
        q_bias.append(jnp.where(mask, 0.0, masked_value).astype(jnp.float32))
        q_doc = lax.dynamic_slice_in_dim(docs_pad, t_start + pad, span)
        q_pos = t_start + cols
        mask = (own_pos[:, None] <= q_pos[None, :]) & (own_doc[:, None] == q_doc[None, :])
        k_bias.append(jnp.where(mask, 0.0, masked_value).astype(jnp.float32))
    q_bias = jnp.concatenate(q_bias, axis=0)
    k_bias = jnp.concatenate(k_bias, axis=0)
    qd, (q_bias, k_bias) = to_plane(attn_q, attn_dout, (q_bias, k_bias))
    qd_win = jnp.concatenate([qd] + [shifted(qd, "chi", -shift) for shift in range(1, reach + 1)], axis=0)


    own_spec = pl.BlockSpec((TILE, HEAD_DIM), lambda i, h: (i, h))
    base = reach * n_tiles - tile_reach

    def col_spec(off):
        return pl.BlockSpec((TILE, HEAD_DIM), lambda i, h: (i, h + off))

    def kwin_spec(j, off):
        return pl.BlockSpec((TILE, HEAD_DIM), lambda i, h: (base + i + j, h + off))

    def qwin_spec(j, off):
        return pl.BlockSpec((TILE, HEAD_DIM), lambda i, h: (i + j, h + off))

    def ldwin_spec(j):
        return pl.BlockSpec((None, 2, TILE), lambda i, h: (h, 0, i + j))

    bias_spec = pl.BlockSpec((TILE, span), lambda i, h: (i, 0))
    ld_spec = pl.BlockSpec((None, 2, TILE), lambda i, h: (h, 0, i))
    params = pltpu.CompilerParams(dimension_semantics=("arbitrary", "arbitrary"))
    grid = (n_tiles, heads_p)

    def query_side(window, i_off, count, w_base):
        def gcol(extra):
            return pl.BlockSpec((TILE, HEAD_DIM), lambda i, h: (i + i_off, h + extra))

        def gwin(j, extra):
            return pl.BlockSpec((TILE, HEAD_DIM), lambda i, h: (w_base + i + j, h + extra))

        return pl.pallas_call(
            _query_side_kernel(nblk, scale),
            out_shape=(
                jax.ShapeDtypeStruct((count * TILE, width), jnp.bfloat16),
                jax.ShapeDtypeStruct((heads_p, 2, count * TILE), jnp.float32),
            ),
            grid=(count, heads_p),
            in_specs=[gcol(0), gcol(heads_p)] + [gwin(j, 0) for j in range(nblk)]
            + [gwin(j, heads_p) for j in range(nblk)]
            + [pl.BlockSpec((TILE, span), lambda i, h: (i + i_off, 0))],
            out_specs=(own_spec, ld_spec),
            compiler_params=params,
            name="attn_query_side",
        )(qd, qd, *([window] * (2 * nblk)), q_bias)

    if split:
        late = n_tiles // 2
        dq_late, ld_late = query_side(jnp.concatenate([prev_late, kv], axis=0), late, n_tiles - late, 0)
        dq_late, ld_late, prev_early = lax.optimization_barrier((dq_late, ld_late, prev_early))
        dq_early, ld_early = query_side(
            jnp.concatenate([prev_early, prev_late, kv[:half]], axis=0), 0, late, 0)
        dq = jnp.concatenate([dq_early, dq_late], axis=0)
        ld = jnp.concatenate([ld_early, ld_late], axis=2)
    else:
        dq, ld = query_side(kv_win, 0, n_tiles, base)

    ld_parts = [ld]
    for shift in range(1, reach + 1):
        ld_parts.append(shifted(ld, "chi", -shift))
    ld_win = jnp.concatenate(ld_parts, axis=2)

    def from_plane(x):
        return lax.all_to_all(x, "clo", split_axis=0, concat_axis=1, tiled=True)

    groups = 2 if heads_p % 2 == 0 else 1
    hg = heads_p // groups
    dkv_parts = []
    for g in range(groups):
        off = g * hg

        def gcol(extra, off=off):
            return pl.BlockSpec((TILE, HEAD_DIM), lambda i, h: (i, h + off + extra))

        def gwin(j, extra, off=off):
            return pl.BlockSpec((TILE, HEAD_DIM), lambda i, h: (i + j, h + off + extra))

        def gld(j, off=off):
            return pl.BlockSpec((None, 2, TILE), lambda i, h: (h + off, 0, i + j))

        dkv_g = pl.pallas_call(
            _key_side_kernel(nblk, scale),
            out_shape=jax.ShapeDtypeStruct((plane, 2 * hg * HEAD_DIM), jnp.bfloat16),
            grid=(n_tiles, hg),
            in_specs=[gcol(0), gcol(heads_p)] + [gwin(j, 0) for j in range(nblk)]
            + [gwin(j, heads_p) for j in range(nblk)] + [gld(j) for j in range(nblk)] + [bias_spec],
            out_specs=pl.BlockSpec((TILE, 2 * HEAD_DIM), lambda i, h: (i, h)),
            compiler_params=params,
            name="attn_key_side",
        )(kv, kv, *([qd_win] * (2 * nblk)), *([ld_win] * nblk), k_bias)
        dkv_parts.append(from_plane(dkv_g).reshape(-1, clo_n, hg, 2, HEAD_DIM))

    rows = dkv_parts[0].shape[0]
    attn_dk = jnp.zeros((rows, clo_n, groups, hg, HEAD_DIM), jnp.bfloat16)
    attn_dv = jnp.zeros((rows, clo_n, groups, hg, HEAD_DIM), jnp.bfloat16)
    for g, part in enumerate(dkv_parts):
        attn_dk = attn_dk.at[:, :, g].set(part[:, :, :, 0, :])
        attn_dv = attn_dv.at[:, :, g].set(part[:, :, :, 1, :])
    return (from_plane(dq), attn_dk.reshape(rows, clo_n * width), attn_dv.reshape(rows, clo_n * width))


def solution(mesh):
    ctx_n, head_n = mesh.devices.shape
    def fn(attn_q, attn_k, attn_v, attn_dout, doc_ids):
        tok_in = attn_q.shape[0] // (ctx_n * head_n)
        clo_n = _plan(tok_in, ctx_n, head_n)
        chi_n = ctx_n // clo_n
        sub = Mesh(np.asarray(mesh.devices).reshape(chi_n, clo_n, head_n), ("chi", "clo", "head"))
        inner = jax.shard_map(
            lambda *a: _per_device(clo_n, *a),
            mesh=sub,
            in_specs=(
                P(("chi", "clo", "head"), None),
                P(("chi", "clo", "head"), None),
                P(("chi", "clo", "head"), None),
                P(("chi", "clo", "head"), None),
                P(),
            ),
            out_specs=(P(("chi", "clo"), "head"), P(("chi", "clo"), "head"), P(("chi", "clo"), "head")),
            check_vma=False,
        )
        return inner(attn_q, attn_k, attn_v, attn_dout, doc_ids)
    return fn
```

```python
import jax
import jax.numpy as jnp
import numpy as np
from jax import lax
from jax.experimental import pallas as pl
from jax.experimental.pallas import tpu as pltpu
from jax.sharding import Mesh
from jax.sharding import PartitionSpec as P

HEAD_DIM = 128
MAX_DOC = 1024
PLANE_TOKENS = 1024
TILE = 256

masked_value = -1e30


def shifted(value, axis, steps):
    count = lax.axis_size(axis)
    leading, last = (max(0, -steps), min(count, count - steps))
    return lax.ppermute(value, axis, [(source, source + steps) for source in range(leading, last)])


def _row(col, tok):
    return jnp.transpose(jnp.broadcast_to(col, (tok, 128)))[0:1, :]


def _query_side_kernel(nblk, scale):
    def kernel(*refs):
        q_ref, d_ref = refs[0], refs[1]
        k_refs = refs[2:2 + nblk]
        v_refs = refs[2 + nblk:2 + 2 * nblk]
        bias_ref = refs[2 + 2 * nblk]
        dq_ref, ld_ref = refs[3 + 2 * nblk], refs[4 + 2 * nblk]
        q = q_ref[...]
        d = d_ref[...]
        logits = []
        for j in range(nblk):
            raw = lax.dot_general(q, k_refs[j][...], (((1,), (1,)), ((), ())),
                                  preferred_element_type=jnp.float32)
            logits.append(raw * scale + bias_ref[:, j * TILE:(j + 1) * TILE])
        top = logits[0].max(axis=1, keepdims=True)
        for j in range(1, nblk):
            top = jnp.maximum(top, logits[j].max(axis=1, keepdims=True))
        expd = [jnp.exp(item - top) for item in logits]
        denom = expd[0].sum(axis=1, keepdims=True)
        for j in range(1, nblk):
            denom = denom + expd[j].sum(axis=1, keepdims=True)
        lse = top + jnp.log(denom)
        inv = 1.0 / denom
        probs = [item * inv for item in expd]
        out = None
        for j in range(nblk):
            part = jnp.dot(probs[j].astype(jnp.bfloat16), v_refs[j][...],
                           preferred_element_type=jnp.float32)
            out = part if out is None else out + part
        delta = (d.astype(jnp.float32) * out).sum(axis=1, keepdims=True)
        dq = None
        for j in range(nblk):
            dprobs = lax.dot_general(d, v_refs[j][...], (((1,), (1,)), ((), ())),
                                     preferred_element_type=jnp.float32)
            dscores = (probs[j] * (dprobs - delta)).astype(jnp.bfloat16)
            part = jnp.dot(dscores, k_refs[j][...], preferred_element_type=jnp.float32)
            dq = part if dq is None else dq + part
        dq_ref[...] = (dq * scale).astype(dq_ref.dtype)
        ld_ref[0:1, :] = _row(lse, TILE)
        ld_ref[1:2, :] = _row(delta, TILE)

    return kernel


def _key_side_kernel(nblk, scale):
    def kernel(*refs):
        k_ref, v_ref = refs[0], refs[1]
        q_refs = refs[2:2 + nblk]
        d_refs = refs[2 + nblk:2 + 2 * nblk]
        ld_refs = refs[2 + 2 * nblk:2 + 3 * nblk]
        bias_ref = refs[2 + 3 * nblk]
        out_ref = refs[3 + 3 * nblk]
        k = k_ref[...]
        v = v_ref[...]
        dk = None
        dv = None
        for j in range(nblk):
            q = q_refs[j][...]
            d = d_refs[j][...]
            lse = ld_refs[j][0:1, :]
            delta = ld_refs[j][1:2, :]
            raw = lax.dot_general(k, q, (((1,), (1,)), ((), ())),
                                  preferred_element_type=jnp.float32)
            logit = raw * scale + bias_ref[:, j * TILE:(j + 1) * TILE]
            prob = jnp.exp(logit - lse)
            dprobs = lax.dot_general(v, d, (((1,), (1,)), ((), ())),
                                     preferred_element_type=jnp.float32)
            dscores = (prob * (dprobs - delta)).astype(jnp.bfloat16)
            part_k = jnp.dot(dscores, q, preferred_element_type=jnp.float32)
            part_v = jnp.dot(prob.astype(jnp.bfloat16), d, preferred_element_type=jnp.float32)
            dk = part_k if dk is None else dk + part_k
            dv = part_v if dv is None else dv + part_v
        out_ref[:, 0:HEAD_DIM] = (dk * scale).astype(out_ref.dtype)
        out_ref[:, HEAD_DIM:2 * HEAD_DIM] = dv.astype(out_ref.dtype)

    return kernel


def _plan(tok_in, ctx_n, head_n):
    clo_n = 1
    while (clo_n * 2 <= ctx_n and ctx_n % (clo_n * 2) == 0
           and tok_in * clo_n * head_n < PLANE_TOKENS):
        clo_n *= 2
    return clo_n


def _per_device(clo_n, attn_q, attn_k, attn_v, attn_dout, doc_ids):
    tok_in, full_width = attn_q.shape
    head_n = lax.axis_size("head")
    chi_n = lax.axis_size("chi")
    group = clo_n * head_n
    width = full_width // group
    heads_p = width // HEAD_DIM
    plane = tok_in * group
    n_tok = doc_ids.shape[0]
    scale = HEAD_DIM ** (-0.5)
    reach = min(-(-(MAX_DOC - 1) // plane), chi_n - 1)
    tile_reach = -(-(MAX_DOC - 1) // TILE)
    nblk = tile_reach + 1
    n_tiles = plane // TILE
    chi = lax.axis_index("chi")
    plane_start = chi * plane

    def to_plane(a, b, tied=None):
        a = a.reshape(tok_in, head_n, clo_n, 1, width)
        b = b.reshape(tok_in, head_n, clo_n, 1, width)
        x = jnp.concatenate([a, b], axis=3).transpose(0, 2, 1, 3, 4).reshape(tok_in, 2 * full_width)
        if tied is not None:
            x, tied = lax.optimization_barrier((x, tied))
        return lax.all_to_all(x, ("clo", "head"), split_axis=1, concat_axis=0, tiled=True), tied

    kv, _ = to_plane(attn_k, attn_v)
    split = reach == 1 and tile_reach * TILE == plane and n_tiles % 2 == 0
    if split:
        half = plane // 2
        prev_late = shifted(kv[half:], "chi", 1)
        early_src, prev_late = lax.optimization_barrier((kv[:half], prev_late))
        prev_early = shifted(early_src, "chi", 1)
    else:
        kv_win = jnp.concatenate([shifted(kv, "chi", shift) for shift in range(reach, 0, -1)] + [kv], axis=0)
    pad = (reach + 1) * plane
    docs_pad = jnp.concatenate([
        jnp.full((pad,), -1, jnp.int32), doc_ids.astype(jnp.int32), jnp.full((pad,), -1, jnp.int32)])
    span = nblk * TILE
    cols = jnp.arange(span, dtype=jnp.int32)
    rows = jnp.arange(TILE, dtype=jnp.int32)
    q_bias, k_bias = [], []
    for i in range(n_tiles):
        t_start = plane_start + i * TILE
        own_doc = lax.dynamic_slice_in_dim(docs_pad, t_start + pad, TILE)
        own_pos = t_start + rows
        k_start = t_start - tile_reach * TILE
        k_doc = lax.dynamic_slice_in_dim(docs_pad, k_start + pad, span)
        k_pos = k_start + cols
        mask = (k_pos[None, :] <= own_pos[:, None]) & (k_doc[None, :] == own_doc[:, None])
        q_bias.append(jnp.where(mask, 0.0, masked_value).astype(jnp.float32))
        q_doc = lax.dynamic_slice_in_dim(docs_pad, t_start + pad, span)
        q_pos = t_start + cols
        mask = (own_pos[:, None] <= q_pos[None, :]) & (own_doc[:, None] == q_doc[None, :])
        k_bias.append(jnp.where(mask, 0.0, masked_value).astype(jnp.float32))
    q_bias = jnp.concatenate(q_bias, axis=0)
    k_bias = jnp.concatenate(k_bias, axis=0)
    qd, (q_bias, k_bias) = to_plane(attn_q, attn_dout, (q_bias, k_bias))
    qd_win = jnp.concatenate([qd] + [shifted(qd, "chi", -shift) for shift in range(1, reach + 1)], axis=0)


    own_spec = pl.BlockSpec((TILE, HEAD_DIM), lambda i, h: (i, h))
    base = reach * n_tiles - tile_reach

    def col_spec(off):
        return pl.BlockSpec((TILE, HEAD_DIM), lambda i, h: (i, h + off))

    def kwin_spec(j, off):
        return pl.BlockSpec((TILE, HEAD_DIM), lambda i, h: (base + i + j, h + off))

    def qwin_spec(j, off):
        return pl.BlockSpec((TILE, HEAD_DIM), lambda i, h: (i + j, h + off))

    def ldwin_spec(j):
        return pl.BlockSpec((None, 2, TILE), lambda i, h: (h, 0, i + j))

    bias_spec = pl.BlockSpec((TILE, span), lambda i, h: (i, 0))
    ld_spec = pl.BlockSpec((None, 2, TILE), lambda i, h: (h, 0, i))
    params = pltpu.CompilerParams(dimension_semantics=("arbitrary", "arbitrary"))
    grid = (n_tiles, heads_p)

    def query_side(window, i_off, count, w_base):
        def gcol(extra):
            return pl.BlockSpec((TILE, HEAD_DIM), lambda i, h: (i + i_off, h + extra))

        def gwin(j, extra):
            return pl.BlockSpec((TILE, HEAD_DIM), lambda i, h: (w_base + i + j, h + extra))

        return pl.pallas_call(
            _query_side_kernel(nblk, scale),
            out_shape=(
                jax.ShapeDtypeStruct((count * TILE, width), jnp.bfloat16),
                jax.ShapeDtypeStruct((heads_p, 2, count * TILE), jnp.float32),
            ),
            grid=(count, heads_p),
            in_specs=[gcol(0), gcol(heads_p)] + [gwin(j, 0) for j in range(nblk)]
            + [gwin(j, heads_p) for j in range(nblk)]
            + [pl.BlockSpec((TILE, span), lambda i, h: (i + i_off, 0))],
            out_specs=(own_spec, ld_spec),
            compiler_params=params,
            name="attn_query_side",
        )(qd, qd, *([window] * (2 * nblk)), q_bias)

    if split:
        late = n_tiles // 2
        dq_late, ld_late = query_side(jnp.concatenate([prev_late, kv], axis=0), late, n_tiles - late, 0)
        dq_late, ld_late, prev_early = lax.optimization_barrier((dq_late, ld_late, prev_early))
        dq_early, ld_early = query_side(
            jnp.concatenate([prev_early, prev_late, kv[:half]], axis=0), 0, late, 0)
        dq = jnp.concatenate([dq_early, dq_late], axis=0)
        ld = jnp.concatenate([ld_early, ld_late], axis=2)
    else:
        dq, ld = query_side(kv_win, 0, n_tiles, base)

    ld_parts = [ld]
    for shift in range(1, reach + 1):
        ld_parts.append(shifted(ld, "chi", -shift))
    ld_win = jnp.concatenate(ld_parts, axis=2)

    def from_plane(x):
        return lax.all_to_all(x, "clo", split_axis=0, concat_axis=1, tiled=True)

    groups = 4 if heads_p % 4 == 0 else (2 if heads_p % 2 == 0 else 1)
    hg = heads_p // groups
    dkv_parts = []
    for g in range(groups):
        off = g * hg

        def gcol(extra, off=off):
            return pl.BlockSpec((TILE, HEAD_DIM), lambda i, h: (i, h + off + extra))

        def gwin(j, extra, off=off):
            return pl.BlockSpec((TILE, HEAD_DIM), lambda i, h: (i + j, h + off + extra))

        def gld(j, off=off):
            return pl.BlockSpec((None, 2, TILE), lambda i, h: (h + off, 0, i + j))

        dkv_g = pl.pallas_call(
            _key_side_kernel(nblk, scale),
            out_shape=jax.ShapeDtypeStruct((plane, 2 * hg * HEAD_DIM), jnp.bfloat16),
            grid=(n_tiles, hg),
            in_specs=[gcol(0), gcol(heads_p)] + [gwin(j, 0) for j in range(nblk)]
            + [gwin(j, heads_p) for j in range(nblk)] + [gld(j) for j in range(nblk)] + [bias_spec],
            out_specs=pl.BlockSpec((TILE, 2 * HEAD_DIM), lambda i, h: (i, h)),
            compiler_params=params,
            name="attn_key_side",
        )(kv, kv, *([qd_win] * (2 * nblk)), *([ld_win] * nblk), k_bias)
        dkv_parts.append(from_plane(dkv_g).reshape(-1, clo_n, hg, 2, HEAD_DIM))

    rows = dkv_parts[0].shape[0]
    attn_dk = jnp.zeros((rows, clo_n, groups, hg, HEAD_DIM), jnp.bfloat16)
    attn_dv = jnp.zeros((rows, clo_n, groups, hg, HEAD_DIM), jnp.bfloat16)
    for g, part in enumerate(dkv_parts):
        attn_dk = attn_dk.at[:, :, g].set(part[:, :, :, 0, :])
        attn_dv = attn_dv.at[:, :, g].set(part[:, :, :, 1, :])
    return (from_plane(dq), attn_dk.reshape(rows, clo_n * width), attn_dv.reshape(rows, clo_n * width))


def solution(mesh):
    ctx_n, head_n = mesh.devices.shape
    def fn(attn_q, attn_k, attn_v, attn_dout, doc_ids):
        tok_in = attn_q.shape[0] // (ctx_n * head_n)
        clo_n = _plan(tok_in, ctx_n, head_n)
        chi_n = ctx_n // clo_n
        sub = Mesh(np.asarray(mesh.devices).reshape(chi_n, clo_n, head_n), ("chi", "clo", "head"))
        inner = jax.shard_map(
            lambda *a: _per_device(clo_n, *a),
            mesh=sub,
            in_specs=(
                P(("chi", "clo", "head"), None),
                P(("chi", "clo", "head"), None),
                P(("chi", "clo", "head"), None),
                P(("chi", "clo", "head"), None),
                P(),
            ),
            out_specs=(P(("chi", "clo"), "head"), P(("chi", "clo"), "head"), P(("chi", "clo"), "head")),
            check_vma=False,
        )
        return inner(attn_q, attn_k, attn_v, attn_dout, doc_ids)
    return fn
```

```python
import jax
import jax.numpy as jnp
import numpy as np
from jax import lax
from jax.experimental import pallas as pl
from jax.experimental.pallas import tpu as pltpu
from jax.sharding import Mesh
from jax.sharding import PartitionSpec as P

HEAD_DIM = 128
MAX_DOC = 1024
PLANE_TOKENS = 1024
TILE = 256

masked_value = -1e30


def shifted(value, axis, steps):
    count = lax.axis_size(axis)
    leading, last = (max(0, -steps), min(count, count - steps))
    return lax.ppermute(value, axis, [(source, source + steps) for source in range(leading, last)])


def _row(col, tok):
    return jnp.transpose(jnp.broadcast_to(col, (tok, 128)))[0:1, :]


class _Picked:
    def __init__(self, refs, starts, tile):
        self.refs, self.starts, self.tile = refs, starts, tile

    def __getitem__(self, idx):
        value = self.refs[-1][idx]
        for p in range(len(self.refs) - 2, -1, -1):
            value = jnp.where(self.tile < self.starts[p + 1], self.refs[p][idx], value)
        return value


def _query_side_kernel(nblk, scale, layout=None):
    def kernel(*refs):
        q_ref, d_ref = refs[0], refs[1]
        if layout is None:
            k_refs = refs[2:2 + nblk]
            v_refs = refs[2 + nblk:2 + 2 * nblk]
            rest = refs[2 + 2 * nblk:]
        else:
            tile = pl.program_id(0)
            at = 2
            k_refs, v_refs = [], []
            for group in (k_refs, v_refs):
                for j, starts in enumerate(layout):
                    group.append(_Picked(refs[at:at + len(starts)], starts, tile + j))
                    at += len(starts)
            rest = refs[at:]
        bias_ref, dq_ref, ld_ref = rest
        q = q_ref[...]
        d = d_ref[...]
        logits = []
        for j in range(nblk):
            raw = lax.dot_general(q, k_refs[j][...], (((1,), (1,)), ((), ())),
                                  preferred_element_type=jnp.float32)
            logits.append(raw * scale + bias_ref[:, j * TILE:(j + 1) * TILE])
        top = logits[0].max(axis=1, keepdims=True)
        for j in range(1, nblk):
            top = jnp.maximum(top, logits[j].max(axis=1, keepdims=True))
        denom = jnp.exp(logits[0] - top).sum(axis=1, keepdims=True)
        for j in range(1, nblk):
            denom = denom + jnp.exp(logits[j] - top).sum(axis=1, keepdims=True)
        lse = top + jnp.log(denom)
        probs = [jnp.exp(item - lse) for item in logits]
        out = None
        for j in range(nblk):
            part = jnp.dot(probs[j].astype(jnp.bfloat16), v_refs[j][...],
                           preferred_element_type=jnp.float32)
            out = part if out is None else out + part
        delta = (d.astype(jnp.float32) * out).sum(axis=1, keepdims=True)
        dq = None
        for j in range(nblk):
            dprobs = lax.dot_general(d, v_refs[j][...], (((1,), (1,)), ((), ())),
                                     preferred_element_type=jnp.float32)
            dscores = (probs[j] * (dprobs - delta)).astype(jnp.bfloat16)
            part = jnp.dot(dscores, k_refs[j][...], preferred_element_type=jnp.float32)
            dq = part if dq is None else dq + part
        dq_ref[...] = (dq * scale).astype(dq_ref.dtype)
        ld_ref[0:1, :] = _row(lse, TILE)
        ld_ref[1:2, :] = _row(delta, TILE)

    return kernel


def _key_side_kernel(nblk, scale):
    def kernel(*refs):
        k_ref, v_ref = refs[0], refs[1]
        q_refs = refs[2:2 + nblk]
        d_refs = refs[2 + nblk:2 + 2 * nblk]
        ld_refs = refs[2 + 2 * nblk:2 + 3 * nblk]
        bias_ref = refs[2 + 3 * nblk]
        out_ref = refs[3 + 3 * nblk]
        k = k_ref[...]
        v = v_ref[...]
        dk = None
        dv = None
        for j in range(nblk):
            q = q_refs[j][...]
            d = d_refs[j][...]
            lse = ld_refs[j][0:1, :]
            delta = ld_refs[j][1:2, :]
            raw = lax.dot_general(k, q, (((1,), (1,)), ((), ())),
                                  preferred_element_type=jnp.float32)
            logit = raw * scale + bias_ref[:, j * TILE:(j + 1) * TILE]
            prob = jnp.exp(logit - lse)
            dprobs = lax.dot_general(v, d, (((1,), (1,)), ((), ())),
                                     preferred_element_type=jnp.float32)
            dscores = (prob * (dprobs - delta)).astype(jnp.bfloat16)
            part_k = jnp.dot(dscores, q, preferred_element_type=jnp.float32)
            part_v = jnp.dot(prob.astype(jnp.bfloat16), d, preferred_element_type=jnp.float32)
            dk = part_k if dk is None else dk + part_k
            dv = part_v if dv is None else dv + part_v
        out_ref[:, 0:HEAD_DIM] = (dk * scale).astype(out_ref.dtype)
        out_ref[:, HEAD_DIM:2 * HEAD_DIM] = dv.astype(out_ref.dtype)

    return kernel


def _plan(tok_in, ctx_n, head_n):
    clo_n = 1
    while (clo_n * 2 <= ctx_n and ctx_n % (clo_n * 2) == 0
           and tok_in * clo_n * head_n < PLANE_TOKENS):
        clo_n *= 2
    return clo_n


def _per_device(clo_n, attn_q, attn_k, attn_v, attn_dout, doc_ids):
    tok_in, full_width = attn_q.shape
    head_n = lax.axis_size("head")
    chi_n = lax.axis_size("chi")
    group = clo_n * head_n
    width = full_width // group
    heads_p = width // HEAD_DIM
    plane = tok_in * group
    n_tok = doc_ids.shape[0]
    scale = HEAD_DIM ** (-0.5)
    reach = min(-(-(MAX_DOC - 1) // plane), chi_n - 1)
    tile_reach = -(-(MAX_DOC - 1) // TILE)
    nblk = tile_reach + 1
    n_tiles = plane // TILE
    chi = lax.axis_index("chi")
    plane_start = chi * plane

    def to_plane(a, b, tied=None):
        a = a.reshape(tok_in, head_n, clo_n, 1, width)
        b = b.reshape(tok_in, head_n, clo_n, 1, width)
        x = jnp.concatenate([a, b], axis=3).transpose(0, 2, 1, 3, 4).reshape(tok_in, 2 * full_width)
        if tied is not None:
            x, tied = lax.optimization_barrier((x, tied))
        return lax.all_to_all(x, ("clo", "head"), split_axis=1, concat_axis=0, tiled=True), tied

    kv, _ = to_plane(attn_k, attn_v)
    split = reach == 1 and tile_reach * TILE == plane and n_tiles % 2 == 0
    if split:
        half = plane // 2
        prev_late = shifted(kv[half:], "chi", 1)
        early_src, prev_late = lax.optimization_barrier((kv[:half], prev_late))
        prev_early = shifted(early_src, "chi", 1)
    else:
        kv_win = jnp.concatenate([shifted(kv, "chi", shift) for shift in range(reach, 0, -1)] + [kv], axis=0)
    pad = (reach + 1) * plane
    docs_pad = jnp.concatenate([
        jnp.full((pad,), -1, jnp.int32), doc_ids.astype(jnp.int32), jnp.full((pad,), -1, jnp.int32)])
    span = nblk * TILE
    cols = jnp.arange(span, dtype=jnp.int32)
    rows = jnp.arange(TILE, dtype=jnp.int32)
    q_bias, k_bias = [], []
    for i in range(n_tiles):
        t_start = plane_start + i * TILE
        own_doc = lax.dynamic_slice_in_dim(docs_pad, t_start + pad, TILE)
        own_pos = t_start + rows
        k_start = t_start - tile_reach * TILE
        k_doc = lax.dynamic_slice_in_dim(docs_pad, k_start + pad, span)
        k_pos = k_start + cols
        mask = (k_pos[None, :] <= own_pos[:, None]) & (k_doc[None, :] == own_doc[:, None])
        q_bias.append(jnp.where(mask, 0.0, masked_value).astype(jnp.float32))
        q_doc = lax.dynamic_slice_in_dim(docs_pad, t_start + pad, span)
        q_pos = t_start + cols
        mask = (own_pos[:, None] <= q_pos[None, :]) & (own_doc[:, None] == q_doc[None, :])
        k_bias.append(jnp.where(mask, 0.0, masked_value).astype(jnp.float32))
    q_bias = jnp.concatenate(q_bias, axis=0)
    k_bias = jnp.concatenate(k_bias, axis=0)
    qd, (q_bias, k_bias) = to_plane(attn_q, attn_dout, (q_bias, k_bias))
    qd_win = jnp.concatenate([qd] + [shifted(qd, "chi", -shift) for shift in range(1, reach + 1)], axis=0)


    own_spec = pl.BlockSpec((TILE, HEAD_DIM), lambda i, h: (i, h))
    base = reach * n_tiles - tile_reach

    def col_spec(off):
        return pl.BlockSpec((TILE, HEAD_DIM), lambda i, h: (i, h + off))

    def kwin_spec(j, off):
        return pl.BlockSpec((TILE, HEAD_DIM), lambda i, h: (base + i + j, h + off))

    def qwin_spec(j, off):
        return pl.BlockSpec((TILE, HEAD_DIM), lambda i, h: (i + j, h + off))

    def ldwin_spec(j):
        return pl.BlockSpec((None, 2, TILE), lambda i, h: (h, 0, i + j))

    bias_spec = pl.BlockSpec((TILE, span), lambda i, h: (i, 0))
    ld_spec = pl.BlockSpec((None, 2, TILE), lambda i, h: (h, 0, i))
    params = pltpu.CompilerParams(dimension_semantics=("arbitrary", "arbitrary"))
    grid = (n_tiles, heads_p)

    def query_side(window, i_off, count, w_base):
        def gcol(extra):
            return pl.BlockSpec((TILE, HEAD_DIM), lambda i, h: (i + i_off, h + extra))

        def gwin(j, extra):
            return pl.BlockSpec((TILE, HEAD_DIM), lambda i, h: (w_base + i + j, h + extra))

        return pl.pallas_call(
            _query_side_kernel(nblk, scale),
            out_shape=(
                jax.ShapeDtypeStruct((count * TILE, width), jnp.bfloat16),
                jax.ShapeDtypeStruct((heads_p, 2, count * TILE), jnp.float32),
            ),
            grid=(count, heads_p),
            in_specs=[gcol(0), gcol(heads_p)] + [gwin(j, 0) for j in range(nblk)]
            + [gwin(j, heads_p) for j in range(nblk)]
            + [pl.BlockSpec((TILE, span), lambda i, h: (i + i_off, 0))],
            out_specs=(own_spec, ld_spec),
            compiler_params=params,
            name="attn_query_side",
        )(qd, qd, *([window] * (2 * nblk)), q_bias)

    def query_side_pieces(pieces, i_off, count):
        layout, specs, args = [], [], []
        for extra in (0, heads_p):
            for j in range(nblk):
                starts = []
                for arr, first, n in pieces:
                    if first <= j + count - 1 and j <= first + n - 1:
                        starts.append(first)
                        specs.append(pl.BlockSpec(
                            (TILE, HEAD_DIM),
                            lambda i, h, j=j, first=first, n=n, extra=extra:
                                (jnp.clip(i + j - first, 0, n - 1), h + extra)))
                        args.append(arr)
                if extra == 0:
                    layout.append(starts)
        return pl.pallas_call(
            _query_side_kernel(nblk, scale, layout),
            out_shape=(
                jax.ShapeDtypeStruct((count * TILE, width), jnp.bfloat16),
                jax.ShapeDtypeStruct((heads_p, 2, count * TILE), jnp.float32),
            ),
            grid=(count, heads_p),
            in_specs=[pl.BlockSpec((TILE, HEAD_DIM), lambda i, h: (i + i_off, h)),
                      pl.BlockSpec((TILE, HEAD_DIM), lambda i, h: (i + i_off, h + heads_p))]
            + specs + [pl.BlockSpec((TILE, span), lambda i, h: (i + i_off, 0))],
            out_specs=(own_spec, ld_spec),
            compiler_params=params,
            name="attn_query_side",
        )(qd, qd, *args, q_bias)

    if split:
        late = n_tiles // 2
        h_t = half // TILE
        dq_late, ld_late = query_side_pieces([(prev_late, 0, h_t), (kv, h_t, n_tiles)], late, n_tiles - late)
        dq_late, ld_late, prev_early = lax.optimization_barrier((dq_late, ld_late, prev_early))
        dq_early, ld_early = query_side_pieces(
            [(prev_early, 0, h_t), (prev_late, h_t, h_t), (kv, 2 * h_t, n_tiles)], 0, late)
        dq = jnp.concatenate([dq_early, dq_late], axis=0)
        ld = jnp.concatenate([ld_early, ld_late], axis=2)
    else:
        dq, ld = query_side(kv_win, 0, n_tiles, base)

    ld_parts = [ld]
    for shift in range(1, reach + 1):
        ld_parts.append(shifted(ld, "chi", -shift))
    ld_win = jnp.concatenate(ld_parts, axis=2)

    def from_plane(x):
        return lax.all_to_all(x, "clo", split_axis=0, concat_axis=1, tiled=True)

    groups = 2 if heads_p % 2 == 0 else 1
    hg = heads_p // groups
    dkv_parts = []
    for g in range(groups):
        off = g * hg

        def gcol(extra, off=off):
            return pl.BlockSpec((TILE, HEAD_DIM), lambda i, h: (i, h + off + extra))

        def gwin(j, extra, off=off):
            return pl.BlockSpec((TILE, HEAD_DIM), lambda i, h: (i + j, h + off + extra))

        def gld(j, off=off):
            return pl.BlockSpec((None, 2, TILE), lambda i, h: (h + off, 0, i + j))

        dkv_g = pl.pallas_call(
            _key_side_kernel(nblk, scale),
            out_shape=jax.ShapeDtypeStruct((plane, 2 * hg * HEAD_DIM), jnp.bfloat16),
            grid=(n_tiles, hg),
            in_specs=[gcol(0), gcol(heads_p)] + [gwin(j, 0) for j in range(nblk)]
            + [gwin(j, heads_p) for j in range(nblk)] + [gld(j) for j in range(nblk)] + [bias_spec],
            out_specs=pl.BlockSpec((TILE, 2 * HEAD_DIM), lambda i, h: (i, h)),
            compiler_params=params,
            name="attn_key_side",
        )(kv, kv, *([qd_win] * (2 * nblk)), *([ld_win] * nblk), k_bias)
        dkv_parts.append(from_plane(dkv_g).reshape(-1, clo_n, 1, hg, 2, HEAD_DIM))

    dkv = jnp.concatenate(dkv_parts, axis=2)
    rows = dkv.shape[0]
    attn_dk = dkv[:, :, :, :, 0, :].reshape(rows, clo_n * width)
    attn_dv = dkv[:, :, :, :, 1, :].reshape(rows, clo_n * width)
    return (from_plane(dq), attn_dk, attn_dv)


def solution(mesh):
    ctx_n, head_n = mesh.devices.shape
    def fn(attn_q, attn_k, attn_v, attn_dout, doc_ids):
        tok_in = attn_q.shape[0] // (ctx_n * head_n)
        clo_n = _plan(tok_in, ctx_n, head_n)
        chi_n = ctx_n // clo_n
        sub = Mesh(np.asarray(mesh.devices).reshape(chi_n, clo_n, head_n), ("chi", "clo", "head"))
        inner = jax.shard_map(
            lambda *a: _per_device(clo_n, *a),
            mesh=sub,
            in_specs=(
                P(("chi", "clo", "head"), None),
                P(("chi", "clo", "head"), None),
                P(("chi", "clo", "head"), None),
                P(("chi", "clo", "head"), None),
                P(),
            ),
            out_specs=(P(("chi", "clo"), "head"), P(("chi", "clo"), "head"), P(("chi", "clo"), "head")),
            check_vma=False,
        )
        return inner(attn_q, attn_k, attn_v, attn_dout, doc_ids)
    return fn
```

```python
import jax
import jax.numpy as jnp
import numpy as np
from jax import lax
from jax.experimental import pallas as pl
from jax.experimental.pallas import tpu as pltpu
from jax.sharding import Mesh
from jax.sharding import PartitionSpec as P

HEAD_DIM = 128
MAX_DOC = 1024
PLANE_TOKENS = 1024
TILE = 256

masked_value = -1e30


def shifted(value, axis, steps):
    count = lax.axis_size(axis)
    leading, last = (max(0, -steps), min(count, count - steps))
    return lax.ppermute(value, axis, [(source, source + steps) for source in range(leading, last)])


def _row(col, tok):
    return jnp.transpose(jnp.broadcast_to(col, (tok, 128)))[0:1, :]


class _Picked:
    def __init__(self, refs, starts, tile):
        self.refs, self.starts, self.tile = refs, starts, tile

    def __getitem__(self, idx):
        value = self.refs[-1][idx]
        for p in range(len(self.refs) - 2, -1, -1):
            value = jnp.where(self.tile < self.starts[p + 1], self.refs[p][idx], value)
        return value


def _query_side_kernel(nblk, scale, layout=None):
    def kernel(*refs):
        q_ref, d_ref = refs[0], refs[1]
        if layout is None:
            k_refs = refs[2:2 + nblk]
            v_refs = refs[2 + nblk:2 + 2 * nblk]
            rest = refs[2 + 2 * nblk:]
        else:
            tile = pl.program_id(0)
            at = 2
            k_refs, v_refs = [], []
            for group in (k_refs, v_refs):
                for j, starts in enumerate(layout):
                    group.append(_Picked(refs[at:at + len(starts)], starts, tile + j))
                    at += len(starts)
            rest = refs[at:]
        bias_ref, dq_ref, ld_ref = rest
        q = q_ref[...]
        d = d_ref[...]
        logits = []
        for j in range(nblk):
            raw = lax.dot_general(q, k_refs[j][...], (((1,), (1,)), ((), ())),
                                  preferred_element_type=jnp.float32)
            logits.append(raw * scale + bias_ref[:, j * TILE:(j + 1) * TILE])
        top = logits[0].max(axis=1, keepdims=True)
        for j in range(1, nblk):
            top = jnp.maximum(top, logits[j].max(axis=1, keepdims=True))
        denom = jnp.exp(logits[0] - top).sum(axis=1, keepdims=True)
        for j in range(1, nblk):
            denom = denom + jnp.exp(logits[j] - top).sum(axis=1, keepdims=True)
        lse = top + jnp.log(denom)
        probs = [jnp.exp(item - lse) for item in logits]
        out = None
        for j in range(nblk):
            part = jnp.dot(probs[j].astype(jnp.bfloat16), v_refs[j][...],
                           preferred_element_type=jnp.float32)
            out = part if out is None else out + part
        delta = (d.astype(jnp.float32) * out).sum(axis=1, keepdims=True)
        dq = None
        for j in range(nblk):
            dprobs = lax.dot_general(d, v_refs[j][...], (((1,), (1,)), ((), ())),
                                     preferred_element_type=jnp.float32)
            dscores = (probs[j] * (dprobs - delta)).astype(jnp.bfloat16)
            part = jnp.dot(dscores, k_refs[j][...], preferred_element_type=jnp.float32)
            dq = part if dq is None else dq + part
        dq_ref[...] = (dq * scale).astype(dq_ref.dtype)
        ld_ref[0:1, :] = _row(lse, TILE)
        ld_ref[1:2, :] = _row(delta, TILE)

    return kernel


def _key_side_kernel(nblk, scale, layout=None):
    def kernel(*refs):
        k_ref, v_ref = refs[0], refs[1]
        if layout is None:
            q_refs = refs[2:2 + nblk]
            d_refs = refs[2 + nblk:2 + 2 * nblk]
            rest = refs[2 + 2 * nblk:]
        else:
            tile = pl.program_id(0)
            at = 2
            q_refs, d_refs = [], []
            for group in (q_refs, d_refs):
                for j, starts in enumerate(layout):
                    group.append(_Picked(refs[at:at + len(starts)], starts, tile + j))
                    at += len(starts)
            rest = refs[at:]
        ld_refs = rest[:nblk]
        bias_ref, out_ref = rest[nblk:]
        k = k_ref[...]
        v = v_ref[...]
        dk = None
        dv = None
        for j in range(nblk):
            q = q_refs[j][...]
            d = d_refs[j][...]
            lse = ld_refs[j][0:1, :]
            delta = ld_refs[j][1:2, :]
            raw = lax.dot_general(k, q, (((1,), (1,)), ((), ())),
                                  preferred_element_type=jnp.float32)
            logit = raw * scale + bias_ref[:, j * TILE:(j + 1) * TILE]
            prob = jnp.exp(logit - lse)
            dprobs = lax.dot_general(v, d, (((1,), (1,)), ((), ())),
                                     preferred_element_type=jnp.float32)
            dscores = (prob * (dprobs - delta)).astype(jnp.bfloat16)
            part_k = jnp.dot(dscores, q, preferred_element_type=jnp.float32)
            part_v = jnp.dot(prob.astype(jnp.bfloat16), d, preferred_element_type=jnp.float32)
            dk = part_k if dk is None else dk + part_k
            dv = part_v if dv is None else dv + part_v
        out_ref[:, 0:HEAD_DIM] = (dk * scale).astype(out_ref.dtype)
        out_ref[:, HEAD_DIM:2 * HEAD_DIM] = dv.astype(out_ref.dtype)

    return kernel


def _plan(tok_in, ctx_n, head_n):
    clo_n = 1
    while (clo_n * 2 <= ctx_n and ctx_n % (clo_n * 2) == 0
           and tok_in * clo_n * head_n < PLANE_TOKENS):
        clo_n *= 2
    return clo_n


def _per_device(clo_n, attn_q, attn_k, attn_v, attn_dout, doc_ids):
    tok_in, full_width = attn_q.shape
    head_n = lax.axis_size("head")
    chi_n = lax.axis_size("chi")
    group = clo_n * head_n
    width = full_width // group
    heads_p = width // HEAD_DIM
    plane = tok_in * group
    n_tok = doc_ids.shape[0]
    scale = HEAD_DIM ** (-0.5)
    reach = min(-(-(MAX_DOC - 1) // plane), chi_n - 1)
    tile_reach = -(-(MAX_DOC - 1) // TILE)
    nblk = tile_reach + 1
    n_tiles = plane // TILE
    chi = lax.axis_index("chi")
    plane_start = chi * plane

    def to_plane(a, b, tied=None):
        a = a.reshape(tok_in, head_n, clo_n, 1, width)
        b = b.reshape(tok_in, head_n, clo_n, 1, width)
        x = jnp.concatenate([a, b], axis=3).transpose(0, 2, 1, 3, 4).reshape(tok_in, 2 * full_width)
        if tied is not None:
            x, tied = lax.optimization_barrier((x, tied))
        return lax.all_to_all(x, ("clo", "head"), split_axis=1, concat_axis=0, tiled=True), tied

    kv, _ = to_plane(attn_k, attn_v)
    split = reach == 1 and tile_reach * TILE == plane and n_tiles % 2 == 0
    if split:
        half = plane // 2
        prev_late = shifted(kv[half:], "chi", 1)
        early_src, prev_late = lax.optimization_barrier((kv[:half], prev_late))
        prev_early = shifted(early_src, "chi", 1)
    else:
        kv_win = jnp.concatenate([shifted(kv, "chi", shift) for shift in range(reach, 0, -1)] + [kv], axis=0)
    pad = (reach + 1) * plane
    docs_pad = jnp.concatenate([
        jnp.full((pad,), -1, jnp.int32), doc_ids.astype(jnp.int32), jnp.full((pad,), -1, jnp.int32)])
    span = nblk * TILE
    cols = jnp.arange(span, dtype=jnp.int32)
    rows = jnp.arange(TILE, dtype=jnp.int32)
    q_bias, k_bias = [], []
    for i in range(n_tiles):
        t_start = plane_start + i * TILE
        own_doc = lax.dynamic_slice_in_dim(docs_pad, t_start + pad, TILE)
        own_pos = t_start + rows
        k_start = t_start - tile_reach * TILE
        k_doc = lax.dynamic_slice_in_dim(docs_pad, k_start + pad, span)
        k_pos = k_start + cols
        mask = (k_pos[None, :] <= own_pos[:, None]) & (k_doc[None, :] == own_doc[:, None])
        q_bias.append(jnp.where(mask, 0.0, masked_value).astype(jnp.float32))
        q_doc = lax.dynamic_slice_in_dim(docs_pad, t_start + pad, span)
        q_pos = t_start + cols
        mask = (own_pos[:, None] <= q_pos[None, :]) & (own_doc[:, None] == q_doc[None, :])
        k_bias.append(jnp.where(mask, 0.0, masked_value).astype(jnp.float32))
    q_bias = jnp.concatenate(q_bias, axis=0)
    k_bias = jnp.concatenate(k_bias, axis=0)
    qd, (q_bias, k_bias) = to_plane(attn_q, attn_dout, (q_bias, k_bias))
    qd_parts = [qd] + [shifted(qd, "chi", -shift) for shift in range(1, reach + 1)]


    own_spec = pl.BlockSpec((TILE, HEAD_DIM), lambda i, h: (i, h))
    base = reach * n_tiles - tile_reach

    def col_spec(off):
        return pl.BlockSpec((TILE, HEAD_DIM), lambda i, h: (i, h + off))

    def kwin_spec(j, off):
        return pl.BlockSpec((TILE, HEAD_DIM), lambda i, h: (base + i + j, h + off))

    def qwin_spec(j, off):
        return pl.BlockSpec((TILE, HEAD_DIM), lambda i, h: (i + j, h + off))

    def ldwin_spec(j):
        return pl.BlockSpec((None, 2, TILE), lambda i, h: (h, 0, i + j))

    bias_spec = pl.BlockSpec((TILE, span), lambda i, h: (i, 0))
    ld_spec = pl.BlockSpec((None, 2, TILE), lambda i, h: (h, 0, i))
    params = pltpu.CompilerParams(dimension_semantics=("arbitrary", "arbitrary"))
    grid = (n_tiles, heads_p)

    def query_side(window, i_off, count, w_base):
        def gcol(extra):
            return pl.BlockSpec((TILE, HEAD_DIM), lambda i, h: (i + i_off, h + extra))

        def gwin(j, extra):
            return pl.BlockSpec((TILE, HEAD_DIM), lambda i, h: (w_base + i + j, h + extra))

        return pl.pallas_call(
            _query_side_kernel(nblk, scale),
            out_shape=(
                jax.ShapeDtypeStruct((count * TILE, width), jnp.bfloat16),
                jax.ShapeDtypeStruct((heads_p, 2, count * TILE), jnp.float32),
            ),
            grid=(count, heads_p),
            in_specs=[gcol(0), gcol(heads_p)] + [gwin(j, 0) for j in range(nblk)]
            + [gwin(j, heads_p) for j in range(nblk)]
            + [pl.BlockSpec((TILE, span), lambda i, h: (i + i_off, 0))],
            out_specs=(own_spec, ld_spec),
            compiler_params=params,
            name="attn_query_side",
        )(qd, qd, *([window] * (2 * nblk)), q_bias)

    def query_side_pieces(pieces, i_off, count):
        layout, specs, args = [], [], []
        for extra in (0, heads_p):
            for j in range(nblk):
                starts = []
                for arr, first, n in pieces:
                    if first <= j + count - 1 and j <= first + n - 1:
                        starts.append(first)
                        specs.append(pl.BlockSpec(
                            (TILE, HEAD_DIM),
                            lambda i, h, j=j, first=first, n=n, extra=extra:
                                (jnp.clip(i + j - first, 0, n - 1), h + extra)))
                        args.append(arr)
                if extra == 0:
                    layout.append(starts)
        return pl.pallas_call(
            _query_side_kernel(nblk, scale, layout),
            out_shape=(
                jax.ShapeDtypeStruct((count * TILE, width), jnp.bfloat16),
                jax.ShapeDtypeStruct((heads_p, 2, count * TILE), jnp.float32),
            ),
            grid=(count, heads_p),
            in_specs=[pl.BlockSpec((TILE, HEAD_DIM), lambda i, h: (i + i_off, h)),
                      pl.BlockSpec((TILE, HEAD_DIM), lambda i, h: (i + i_off, h + heads_p))]
            + specs + [pl.BlockSpec((TILE, span), lambda i, h: (i + i_off, 0))],
            out_specs=(own_spec, ld_spec),
            compiler_params=params,
            name="attn_query_side",
        )(qd, qd, *args, q_bias)

    if split:
        late = n_tiles // 2
        h_t = half // TILE
        dq_late, ld_late = query_side_pieces([(prev_late, 0, h_t), (kv, h_t, n_tiles)], late, n_tiles - late)
        dq_late, ld_late, prev_early = lax.optimization_barrier((dq_late, ld_late, prev_early))
        dq_early, ld_early = query_side_pieces(
            [(prev_early, 0, h_t), (prev_late, h_t, h_t), (kv, 2 * h_t, n_tiles)], 0, late)
        dq = jnp.concatenate([dq_early, dq_late], axis=0)
        ld = jnp.concatenate([ld_early, ld_late], axis=2)
    else:
        dq, ld = query_side(kv_win, 0, n_tiles, base)

    ld_parts = [ld]
    for shift in range(1, reach + 1):
        ld_parts.append(shifted(ld, "chi", -shift))
    ld_win = jnp.concatenate(ld_parts, axis=2)

    def from_plane(x):
        return lax.all_to_all(x, "clo", split_axis=0, concat_axis=1, tiled=True)

    groups = 2 if heads_p % 2 == 0 else 1
    hg = heads_p // groups
    dkv_parts = []
    for g in range(groups):
        off = g * hg

        def gcol(extra, off=off):
            return pl.BlockSpec((TILE, HEAD_DIM), lambda i, h: (i, h + off + extra))

        def gwin(j, extra, off=off):
            return pl.BlockSpec((TILE, HEAD_DIM), lambda i, h: (i + j, h + off + extra))

        def gld(j, off=off):
            return pl.BlockSpec((None, 2, TILE), lambda i, h: (h + off, 0, i + j))

        layout, q_specs, q_args = [], [], []
        for extra in (0, heads_p):
            for j in range(nblk):
                starts = []
                for p, arr in enumerate(qd_parts):
                    first = p * n_tiles
                    if first <= j + n_tiles - 1 and j <= first + n_tiles - 1:
                        starts.append(first)
                        q_specs.append(pl.BlockSpec(
                            (TILE, HEAD_DIM),
                            lambda i, h, j=j, first=first, extra=extra, off=off:
                                (jnp.clip(i + j - first, 0, n_tiles - 1), h + off + extra)))
                        q_args.append(arr)
                if extra == 0:
                    layout.append(starts)

        dkv_g = pl.pallas_call(
            _key_side_kernel(nblk, scale, layout),
            out_shape=jax.ShapeDtypeStruct((plane, 2 * hg * HEAD_DIM), jnp.bfloat16),
            grid=(n_tiles, hg),
            in_specs=[gcol(0), gcol(heads_p)] + q_specs + [gld(j) for j in range(nblk)] + [bias_spec],
            out_specs=pl.BlockSpec((TILE, 2 * HEAD_DIM), lambda i, h: (i, h)),
            compiler_params=params,
            name="attn_key_side",
        )(kv, kv, *q_args, *([ld_win] * nblk), k_bias)
        dkv_parts.append(from_plane(dkv_g).reshape(-1, clo_n, 1, hg, 2, HEAD_DIM))

    dkv = jnp.concatenate(dkv_parts, axis=2)
    rows = dkv.shape[0]
    attn_dk = dkv[:, :, :, :, 0, :].reshape(rows, clo_n * width)
    attn_dv = dkv[:, :, :, :, 1, :].reshape(rows, clo_n * width)
    return (from_plane(dq), attn_dk, attn_dv)


def solution(mesh):
    ctx_n, head_n = mesh.devices.shape
    def fn(attn_q, attn_k, attn_v, attn_dout, doc_ids):
        tok_in = attn_q.shape[0] // (ctx_n * head_n)
        clo_n = _plan(tok_in, ctx_n, head_n)
        chi_n = ctx_n // clo_n
        sub = Mesh(np.asarray(mesh.devices).reshape(chi_n, clo_n, head_n), ("chi", "clo", "head"))
        inner = jax.shard_map(
            lambda *a: _per_device(clo_n, *a),
            mesh=sub,
            in_specs=(
                P(("chi", "clo", "head"), None),
                P(("chi", "clo", "head"), None),
                P(("chi", "clo", "head"), None),
                P(("chi", "clo", "head"), None),
                P(),
            ),
            out_specs=(P(("chi", "clo"), "head"), P(("chi", "clo"), "head"), P(("chi", "clo"), "head")),
            check_vma=False,
        )
        return inner(attn_q, attn_k, attn_v, attn_dout, doc_ids)
    return fn
```

```python
import jax
import jax.numpy as jnp
import numpy as np
from jax import lax
from jax.experimental import pallas as pl
from jax.experimental.pallas import tpu as pltpu
from jax.sharding import Mesh
from jax.sharding import PartitionSpec as P

HEAD_DIM = 128
MAX_DOC = 1024
PLANE_TOKENS = 1024
TILE = 256

masked_value = -1e30


def shifted(value, axis, steps):
    count = lax.axis_size(axis)
    leading, last = (max(0, -steps), min(count, count - steps))
    return lax.ppermute(value, axis, [(source, source + steps) for source in range(leading, last)])


def _row(col, tok):
    return jnp.transpose(jnp.broadcast_to(col, (tok, 128)))[0:1, :]


class _Picked:
    def __init__(self, refs, starts, tile):
        self.refs, self.starts, self.tile = refs, starts, tile

    def __getitem__(self, idx):
        value = self.refs[-1][idx]
        for p in range(len(self.refs) - 2, -1, -1):
            value = jnp.where(self.tile < self.starts[p + 1], self.refs[p][idx], value)
        return value


def _query_side_kernel(nblk, scale, layout=None):
    def kernel(*refs):
        q_ref, d_ref = refs[0], refs[1]
        if layout is None:
            k_refs = refs[2:2 + nblk]
            v_refs = refs[2 + nblk:2 + 2 * nblk]
            rest = refs[2 + 2 * nblk:]
        else:
            tile = pl.program_id(0)
            at = 2
            k_refs, v_refs = [], []
            for group in (k_refs, v_refs):
                for j, starts in enumerate(layout):
                    group.append(_Picked(refs[at:at + len(starts)], starts, tile + j))
                    at += len(starts)
            rest = refs[at:]
        bias_ref, dq_ref, ld_ref = rest
        q = q_ref[...]
        d = d_ref[...]
        logits = []
        for j in range(nblk):
            raw = lax.dot_general(q, k_refs[j][...], (((1,), (1,)), ((), ())),
                                  preferred_element_type=jnp.float32)
            logits.append(raw * scale + bias_ref[:, j * TILE:(j + 1) * TILE])
        top = logits[0].max(axis=1, keepdims=True)
        for j in range(1, nblk):
            top = jnp.maximum(top, logits[j].max(axis=1, keepdims=True))
        denom = jnp.exp(logits[0] - top).sum(axis=1, keepdims=True)
        for j in range(1, nblk):
            denom = denom + jnp.exp(logits[j] - top).sum(axis=1, keepdims=True)
        lse = top + jnp.log(denom)
        probs = [jnp.exp(item - lse) for item in logits]
        out = None
        for j in range(nblk):
            part = jnp.dot(probs[j].astype(jnp.bfloat16), v_refs[j][...],
                           preferred_element_type=jnp.float32)
            out = part if out is None else out + part
        delta = (d.astype(jnp.float32) * out).sum(axis=1, keepdims=True)
        dq = None
        for j in range(nblk):
            dprobs = lax.dot_general(d, v_refs[j][...], (((1,), (1,)), ((), ())),
                                     preferred_element_type=jnp.float32)
            dscores = (probs[j] * (dprobs - delta)).astype(jnp.bfloat16)
            part = jnp.dot(dscores, k_refs[j][...], preferred_element_type=jnp.float32)
            dq = part if dq is None else dq + part
        dq_ref[...] = (dq * scale).astype(dq_ref.dtype)
        ld_ref[0:1, :] = _row(lse, TILE)
        ld_ref[1:2, :] = _row(delta, TILE)

    return kernel


def _key_side_kernel(nblk, scale, layout=None):
    def kernel(*refs):
        k_ref, v_ref = refs[0], refs[1]
        if layout is None:
            q_refs = refs[2:2 + nblk]
            d_refs = refs[2 + nblk:2 + 2 * nblk]
            rest = refs[2 + 2 * nblk:]
        else:
            tile = pl.program_id(0)
            at = 2
            q_refs, d_refs = [], []
            for group in (q_refs, d_refs):
                for j, starts in enumerate(layout):
                    group.append(_Picked(refs[at:at + len(starts)], starts, tile + j))
                    at += len(starts)
            rest = refs[at:]
        if layout is None:
            ld_refs = rest[:nblk]
            rest = rest[nblk:]
        else:
            ld_refs = []
            for j, starts in enumerate(layout):
                ld_refs.append(_Picked(rest[:len(starts)], starts, tile + j))
                rest = rest[len(starts):]
        bias_ref, out_ref = rest
        k = k_ref[...]
        v = v_ref[...]
        dk = None
        dv = None
        for j in range(nblk):
            q = q_refs[j][...]
            d = d_refs[j][...]
            lse = ld_refs[j][0:1, :]
            delta = ld_refs[j][1:2, :]
            raw = lax.dot_general(k, q, (((1,), (1,)), ((), ())),
                                  preferred_element_type=jnp.float32)
            logit = raw * scale + bias_ref[:, j * TILE:(j + 1) * TILE]
            prob = jnp.exp(logit - lse)
            dprobs = lax.dot_general(v, d, (((1,), (1,)), ((), ())),
                                     preferred_element_type=jnp.float32)
            dscores = (prob * (dprobs - delta)).astype(jnp.bfloat16)
            part_k = jnp.dot(dscores, q, preferred_element_type=jnp.float32)
            part_v = jnp.dot(prob.astype(jnp.bfloat16), d, preferred_element_type=jnp.float32)
            dk = part_k if dk is None else dk + part_k
            dv = part_v if dv is None else dv + part_v
        out_ref[:, 0:HEAD_DIM] = (dk * scale).astype(out_ref.dtype)
        out_ref[:, HEAD_DIM:2 * HEAD_DIM] = dv.astype(out_ref.dtype)

    return kernel


def _plan(tok_in, ctx_n, head_n):
    clo_n = 1
    while (clo_n * 2 <= ctx_n and ctx_n % (clo_n * 2) == 0
           and tok_in * clo_n * head_n < PLANE_TOKENS):
        clo_n *= 2
    return clo_n


def _per_device(clo_n, attn_q, attn_k, attn_v, attn_dout, doc_ids):
    tok_in, full_width = attn_q.shape
    head_n = lax.axis_size("head")
    chi_n = lax.axis_size("chi")
    group = clo_n * head_n
    width = full_width // group
    heads_p = width // HEAD_DIM
    plane = tok_in * group
    n_tok = doc_ids.shape[0]
    scale = HEAD_DIM ** (-0.5)
    reach = min(-(-(MAX_DOC - 1) // plane), chi_n - 1)
    tile_reach = -(-(MAX_DOC - 1) // TILE)
    nblk = tile_reach + 1
    n_tiles = plane // TILE
    chi = lax.axis_index("chi")
    plane_start = chi * plane

    def to_plane(a, b, tied=None):
        a = a.reshape(tok_in, head_n, clo_n, 1, width)
        b = b.reshape(tok_in, head_n, clo_n, 1, width)
        x = jnp.concatenate([a, b], axis=3).transpose(0, 2, 1, 3, 4).reshape(tok_in, 2 * full_width)
        if tied is not None:
            x, tied = lax.optimization_barrier((x, tied))
        return lax.all_to_all(x, ("clo", "head"), split_axis=1, concat_axis=0, tiled=True), tied

    kv, _ = to_plane(attn_k, attn_v)
    split = reach == 1 and tile_reach * TILE == plane and n_tiles % 2 == 0
    if split:
        half = plane // 2
        prev_late = shifted(kv[half:], "chi", 1)
        early_src, prev_late = lax.optimization_barrier((kv[:half], prev_late))
        prev_early = shifted(early_src, "chi", 1)
    else:
        kv_win = jnp.concatenate([shifted(kv, "chi", shift) for shift in range(reach, 0, -1)] + [kv], axis=0)
    pad = (reach + 1) * plane
    docs_pad = jnp.concatenate([
        jnp.full((pad,), -1, jnp.int32), doc_ids.astype(jnp.int32), jnp.full((pad,), -1, jnp.int32)])
    span = nblk * TILE
    cols = jnp.arange(span, dtype=jnp.int32)
    rows = jnp.arange(TILE, dtype=jnp.int32)
    q_bias, k_bias = [], []
    for i in range(n_tiles):
        t_start = plane_start + i * TILE
        own_doc = lax.dynamic_slice_in_dim(docs_pad, t_start + pad, TILE)
        own_pos = t_start + rows
        k_start = t_start - tile_reach * TILE
        k_doc = lax.dynamic_slice_in_dim(docs_pad, k_start + pad, span)
        k_pos = k_start + cols
        mask = (k_pos[None, :] <= own_pos[:, None]) & (k_doc[None, :] == own_doc[:, None])
        q_bias.append(jnp.where(mask, 0.0, masked_value).astype(jnp.float32))
        q_doc = lax.dynamic_slice_in_dim(docs_pad, t_start + pad, span)
        q_pos = t_start + cols
        mask = (own_pos[:, None] <= q_pos[None, :]) & (own_doc[:, None] == q_doc[None, :])
        k_bias.append(jnp.where(mask, 0.0, masked_value).astype(jnp.float32))
    q_bias = jnp.concatenate(q_bias, axis=0)
    k_bias = jnp.concatenate(k_bias, axis=0)
    qd, (q_bias, k_bias) = to_plane(attn_q, attn_dout, (q_bias, k_bias))
    qd_parts = [qd] + [shifted(qd, "chi", -shift) for shift in range(1, reach + 1)]


    own_spec = pl.BlockSpec((TILE, HEAD_DIM), lambda i, h: (i, h))
    base = reach * n_tiles - tile_reach

    def col_spec(off):
        return pl.BlockSpec((TILE, HEAD_DIM), lambda i, h: (i, h + off))

    def kwin_spec(j, off):
        return pl.BlockSpec((TILE, HEAD_DIM), lambda i, h: (base + i + j, h + off))

    def qwin_spec(j, off):
        return pl.BlockSpec((TILE, HEAD_DIM), lambda i, h: (i + j, h + off))

    def ldwin_spec(j):
        return pl.BlockSpec((None, 2, TILE), lambda i, h: (h, 0, i + j))

    bias_spec = pl.BlockSpec((TILE, span), lambda i, h: (i, 0))
    ld_spec = pl.BlockSpec((None, 2, TILE), lambda i, h: (h, 0, i))
    params = pltpu.CompilerParams(dimension_semantics=("arbitrary", "arbitrary"))
    grid = (n_tiles, heads_p)

    def query_side(window, i_off, count, w_base):
        def gcol(extra):
            return pl.BlockSpec((TILE, HEAD_DIM), lambda i, h: (i + i_off, h + extra))

        def gwin(j, extra):
            return pl.BlockSpec((TILE, HEAD_DIM), lambda i, h: (w_base + i + j, h + extra))

        return pl.pallas_call(
            _query_side_kernel(nblk, scale),
            out_shape=(
                jax.ShapeDtypeStruct((count * TILE, width), jnp.bfloat16),
                jax.ShapeDtypeStruct((heads_p, 2, count * TILE), jnp.float32),
            ),
            grid=(count, heads_p),
            in_specs=[gcol(0), gcol(heads_p)] + [gwin(j, 0) for j in range(nblk)]
            + [gwin(j, heads_p) for j in range(nblk)]
            + [pl.BlockSpec((TILE, span), lambda i, h: (i + i_off, 0))],
            out_specs=(own_spec, ld_spec),
            compiler_params=params,
            name="attn_query_side",
        )(qd, qd, *([window] * (2 * nblk)), q_bias)

    def query_side_pieces(pieces, i_off, count):
        layout, specs, args = [], [], []
        for extra in (0, heads_p):
            for j in range(nblk):
                starts = []
                for arr, first, n in pieces:
                    if first <= j + count - 1 and j <= first + n - 1:
                        starts.append(first)
                        specs.append(pl.BlockSpec(
                            (TILE, HEAD_DIM),
                            lambda i, h, j=j, first=first, n=n, extra=extra:
                                (jnp.clip(i + j - first, 0, n - 1), h + extra)))
                        args.append(arr)
                if extra == 0:
                    layout.append(starts)
        return pl.pallas_call(
            _query_side_kernel(nblk, scale, layout),
            out_shape=(
                jax.ShapeDtypeStruct((count * TILE, width), jnp.bfloat16),
                jax.ShapeDtypeStruct((heads_p, 2, count * TILE), jnp.float32),
            ),
            grid=(count, heads_p),
            in_specs=[pl.BlockSpec((TILE, HEAD_DIM), lambda i, h: (i + i_off, h)),
                      pl.BlockSpec((TILE, HEAD_DIM), lambda i, h: (i + i_off, h + heads_p))]
            + specs + [pl.BlockSpec((TILE, span), lambda i, h: (i + i_off, 0))],
            out_specs=(own_spec, ld_spec),
            compiler_params=params,
            name="attn_query_side",
        )(qd, qd, *args, q_bias)

    if split:
        late = n_tiles // 2
        h_t = half // TILE
        dq_late, ld_late = query_side_pieces([(prev_late, 0, h_t), (kv, h_t, n_tiles)], late, n_tiles - late)
        dq_late, ld_late, prev_early = lax.optimization_barrier((dq_late, ld_late, prev_early))
        dq_early, ld_early = query_side_pieces(
            [(prev_early, 0, h_t), (prev_late, h_t, h_t), (kv, 2 * h_t, n_tiles)], 0, late)
        dq = jnp.concatenate([dq_early, dq_late], axis=0)
        ld = jnp.concatenate([ld_early, ld_late], axis=2)
    else:
        dq, ld = query_side(kv_win, 0, n_tiles, base)

    ld_parts = [ld]
    for shift in range(1, reach + 1):
        ld_parts.append(shifted(ld, "chi", -shift))
    ld_win = jnp.concatenate(ld_parts, axis=2)

    def from_plane(x):
        return lax.all_to_all(x, "clo", split_axis=0, concat_axis=1, tiled=True)

    groups = 2 if heads_p % 2 == 0 else 1
    hg = heads_p // groups
    dkv_parts = []
    for g in range(groups):
        off = g * hg

        def gcol(extra, off=off):
            return pl.BlockSpec((TILE, HEAD_DIM), lambda i, h: (i, h + off + extra))

        def gwin(j, extra, off=off):
            return pl.BlockSpec((TILE, HEAD_DIM), lambda i, h: (i + j, h + off + extra))

        def gld(j, off=off):
            return pl.BlockSpec((None, 2, TILE), lambda i, h: (h + off, 0, i + j))

        layout, q_specs, q_args = [], [], []
        for extra in (0, heads_p):
            for j in range(nblk):
                starts = []
                for p, arr in enumerate(qd_parts):
                    first = p * n_tiles
                    if first <= j + n_tiles - 1 and j <= first + n_tiles - 1:
                        starts.append(first)
                        q_specs.append(pl.BlockSpec(
                            (TILE, HEAD_DIM),
                            lambda i, h, j=j, first=first, extra=extra, off=off:
                                (jnp.clip(i + j - first, 0, n_tiles - 1), h + off + extra)))
                        q_args.append(arr)
                if extra == 0:
                    layout.append(starts)
        ld_specs, ld_args = [], []
        for j in range(nblk):
            for p, arr in enumerate(ld_parts):
                first = p * n_tiles
                if first <= j + n_tiles - 1 and j <= first + n_tiles - 1:
                    ld_specs.append(pl.BlockSpec(
                        (None, 2, TILE),
                        lambda i, h, j=j, first=first, off=off:
                            (h + off, 0, jnp.clip(i + j - first, 0, n_tiles - 1))))
                    ld_args.append(arr)

        dkv_g = pl.pallas_call(
            _key_side_kernel(nblk, scale, layout),
            out_shape=jax.ShapeDtypeStruct((plane, 2 * hg * HEAD_DIM), jnp.bfloat16),
            grid=(n_tiles, hg),
            in_specs=[gcol(0), gcol(heads_p)] + q_specs + ld_specs + [bias_spec],
            out_specs=pl.BlockSpec((TILE, 2 * HEAD_DIM), lambda i, h: (i, h)),
            compiler_params=params,
            name="attn_key_side",
        )(kv, kv, *q_args, *ld_args, k_bias)
        dkv_parts.append(from_plane(dkv_g).reshape(-1, clo_n, 1, hg, 2, HEAD_DIM))

    dkv = jnp.concatenate(dkv_parts, axis=2)
    rows = dkv.shape[0]
    attn_dk = dkv[:, :, :, :, 0, :].reshape(rows, clo_n * width)
    attn_dv = dkv[:, :, :, :, 1, :].reshape(rows, clo_n * width)
    return (from_plane(dq), attn_dk, attn_dv)


def solution(mesh):
    ctx_n, head_n = mesh.devices.shape
    def fn(attn_q, attn_k, attn_v, attn_dout, doc_ids):
        tok_in = attn_q.shape[0] // (ctx_n * head_n)
        clo_n = _plan(tok_in, ctx_n, head_n)
        chi_n = ctx_n // clo_n
        sub = Mesh(np.asarray(mesh.devices).reshape(chi_n, clo_n, head_n), ("chi", "clo", "head"))
        inner = jax.shard_map(
            lambda *a: _per_device(clo_n, *a),
            mesh=sub,
            in_specs=(
                P(("chi", "clo", "head"), None),
                P(("chi", "clo", "head"), None),
                P(("chi", "clo", "head"), None),
                P(("chi", "clo", "head"), None),
                P(),
            ),
            out_specs=(P(("chi", "clo"), "head"), P(("chi", "clo"), "head"), P(("chi", "clo"), "head")),
            check_vma=False,
        )
        return inner(attn_q, attn_k, attn_v, attn_dout, doc_ids)
    return fn
```

```python
import jax
import jax.numpy as jnp
import numpy as np
from jax import lax
from jax.experimental import pallas as pl
from jax.experimental.pallas import tpu as pltpu
from jax.sharding import Mesh
from jax.sharding import PartitionSpec as P

HEAD_DIM = 128
MAX_DOC = 1024
PLANE_TOKENS = 1024
TILE = 256

masked_value = -1e30


def shifted(value, axis, steps):
    count = lax.axis_size(axis)
    leading, last = (max(0, -steps), min(count, count - steps))
    return lax.ppermute(value, axis, [(source, source + steps) for source in range(leading, last)])


def _row(col, tok):
    return jnp.transpose(jnp.broadcast_to(col, (tok, 128)))[0:1, :]


class _Picked:
    def __init__(self, refs, starts, tile):
        self.refs, self.starts, self.tile = refs, starts, tile

    def __getitem__(self, idx):
        value = self.refs[-1][idx]
        for p in range(len(self.refs) - 2, -1, -1):
            value = jnp.where(self.tile < self.starts[p + 1], self.refs[p][idx], value)
        return value


def _query_side_kernel(nblk, scale, layout=None):
    def kernel(*refs):
        q_ref, d_ref = refs[0], refs[1]
        if layout is None:
            k_refs = refs[2:2 + nblk]
            v_refs = refs[2 + nblk:2 + 2 * nblk]
            rest = refs[2 + 2 * nblk:]
        else:
            tile = pl.program_id(0)
            at = 2
            k_refs, v_refs = [], []
            for group in (k_refs, v_refs):
                for j, starts in enumerate(layout):
                    group.append(_Picked(refs[at:at + len(starts)], starts, tile + j))
                    at += len(starts)
            rest = refs[at:]
        bias_ref, dq_ref, ld_ref = rest
        q = q_ref[...]
        d = d_ref[...]
        logits = []
        for j in range(nblk):
            raw = lax.dot_general(q, k_refs[j][...], (((1,), (1,)), ((), ())),
                                  preferred_element_type=jnp.float32)
            logits.append(raw * scale + bias_ref[:, j * TILE:(j + 1) * TILE])
        top = logits[0].max(axis=1, keepdims=True)
        for j in range(1, nblk):
            top = jnp.maximum(top, logits[j].max(axis=1, keepdims=True))
        denom = jnp.exp(logits[0] - top).sum(axis=1, keepdims=True)
        for j in range(1, nblk):
            denom = denom + jnp.exp(logits[j] - top).sum(axis=1, keepdims=True)
        lse = top + jnp.log(denom)
        probs = [jnp.exp(item - lse) for item in logits]
        out = None
        for j in range(nblk):
            part = jnp.dot(probs[j].astype(jnp.bfloat16), v_refs[j][...],
                           preferred_element_type=jnp.float32)
            out = part if out is None else out + part
        delta = (d.astype(jnp.float32) * out).sum(axis=1, keepdims=True)
        dq = None
        for j in range(nblk):
            dprobs = lax.dot_general(d, v_refs[j][...], (((1,), (1,)), ((), ())),
                                     preferred_element_type=jnp.float32)
            dscores = (probs[j] * (dprobs - delta)).astype(jnp.bfloat16)
            part = jnp.dot(dscores, k_refs[j][...], preferred_element_type=jnp.float32)
            dq = part if dq is None else dq + part
        dq_ref[...] = (dq * scale).astype(dq_ref.dtype)
        ld_ref[0:1, :] = _row(lse, TILE)
        ld_ref[1:2, :] = _row(delta, TILE)

    return kernel


def _key_side_kernel(nblk, scale, layout=None):
    def kernel(*refs):
        k_ref, v_ref = refs[0], refs[1]
        if layout is None:
            q_refs = refs[2:2 + nblk]
            d_refs = refs[2 + nblk:2 + 2 * nblk]
            rest = refs[2 + 2 * nblk:]
        else:
            tile = pl.program_id(0)
            at = 2
            q_refs, d_refs = [], []
            for group in (q_refs, d_refs):
                for j, starts in enumerate(layout):
                    group.append(_Picked(refs[at:at + len(starts)], starts, tile + j))
                    at += len(starts)
            rest = refs[at:]
        if layout is None:
            ld_refs = rest[:nblk]
            rest = rest[nblk:]
        else:
            ld_refs = []
            for j, starts in enumerate(layout):
                ld_refs.append(_Picked(rest[:len(starts)], starts, tile + j))
                rest = rest[len(starts):]
        bias_ref, out_ref = rest
        k = k_ref[...]
        v = v_ref[...]
        dk = None
        dv = None
        for j in range(nblk):
            q = q_refs[j][...]
            d = d_refs[j][...]
            lse = ld_refs[j][0:1, :]
            delta = ld_refs[j][1:2, :]
            raw = lax.dot_general(k, q, (((1,), (1,)), ((), ())),
                                  preferred_element_type=jnp.float32)
            logit = raw * scale + bias_ref[:, j * TILE:(j + 1) * TILE]
            prob = jnp.exp(logit - lse)
            dprobs = lax.dot_general(v, d, (((1,), (1,)), ((), ())),
                                     preferred_element_type=jnp.float32)
            dscores = (prob * (dprobs - delta)).astype(jnp.bfloat16)
            part_k = jnp.dot(dscores, q, preferred_element_type=jnp.float32)
            part_v = jnp.dot(prob.astype(jnp.bfloat16), d, preferred_element_type=jnp.float32)
            dk = part_k if dk is None else dk + part_k
            dv = part_v if dv is None else dv + part_v
        out_ref[:, 0:HEAD_DIM] = (dk * scale).astype(out_ref.dtype)
        out_ref[:, HEAD_DIM:2 * HEAD_DIM] = dv.astype(out_ref.dtype)

    return kernel


def _plan(tok_in, ctx_n, head_n):
    clo_n = 1
    while (clo_n * 2 <= ctx_n and ctx_n % (clo_n * 2) == 0
           and tok_in * clo_n * head_n < PLANE_TOKENS):
        clo_n *= 2
    return clo_n


def _per_device(clo_n, attn_q, attn_k, attn_v, attn_dout, doc_ids):
    tok_in, full_width = attn_q.shape
    head_n = lax.axis_size("head")
    chi_n = lax.axis_size("chi")
    group = clo_n * head_n
    width = full_width // group
    heads_p = width // HEAD_DIM
    plane = tok_in * group
    n_tok = doc_ids.shape[0]
    scale = HEAD_DIM ** (-0.5)
    reach = min(-(-(MAX_DOC - 1) // plane), chi_n - 1)
    tile_reach = -(-(MAX_DOC - 1) // TILE)
    nblk = tile_reach + 1
    n_tiles = plane // TILE
    chi = lax.axis_index("chi")
    plane_start = chi * plane

    def to_plane(a, b, tied=None):
        a = a.reshape(tok_in, head_n, clo_n, 1, width)
        b = b.reshape(tok_in, head_n, clo_n, 1, width)
        x = jnp.concatenate([a, b], axis=3).transpose(0, 2, 1, 3, 4).reshape(tok_in, 2 * full_width)
        if tied is not None:
            x, tied = lax.optimization_barrier((x, tied))
        return lax.all_to_all(x, ("clo", "head"), split_axis=1, concat_axis=0, tiled=True), tied

    kv, _ = to_plane(attn_k, attn_v)
    split = reach == 1 and tile_reach * TILE == plane and n_tiles % 2 == 0
    if split:
        half = plane // 2
        prev_late = shifted(kv[half:], "chi", 1)
        early_src, prev_late = lax.optimization_barrier((kv[:half], prev_late))
        prev_early = shifted(early_src, "chi", 1)
    else:
        kv_win = jnp.concatenate([shifted(kv, "chi", shift) for shift in range(reach, 0, -1)] + [kv], axis=0)
    pad = (reach + 1) * plane
    docs_pad = jnp.concatenate([
        jnp.full((pad,), -1, jnp.int32), doc_ids.astype(jnp.int32), jnp.full((pad,), -1, jnp.int32)])
    span = nblk * TILE
    cols = jnp.arange(span, dtype=jnp.int32)
    rows = jnp.arange(TILE, dtype=jnp.int32)
    q_bias, k_bias = [], []
    for i in range(n_tiles):
        t_start = plane_start + i * TILE
        own_doc = lax.dynamic_slice_in_dim(docs_pad, t_start + pad, TILE)
        own_pos = t_start + rows
        k_start = t_start - tile_reach * TILE
        k_doc = lax.dynamic_slice_in_dim(docs_pad, k_start + pad, span)
        k_pos = k_start + cols
        mask = (k_pos[None, :] <= own_pos[:, None]) & (k_doc[None, :] == own_doc[:, None])
        q_bias.append(jnp.where(mask, 0.0, masked_value).astype(jnp.bfloat16))
        q_doc = lax.dynamic_slice_in_dim(docs_pad, t_start + pad, span)
        q_pos = t_start + cols
        mask = (own_pos[:, None] <= q_pos[None, :]) & (own_doc[:, None] == q_doc[None, :])
        k_bias.append(jnp.where(mask, 0.0, masked_value).astype(jnp.bfloat16))
    q_bias = jnp.concatenate(q_bias, axis=0)
    k_bias = jnp.concatenate(k_bias, axis=0)
    qd, (q_bias, k_bias) = to_plane(attn_q, attn_dout, (q_bias, k_bias))
    qd_parts = [qd] + [shifted(qd, "chi", -shift) for shift in range(1, reach + 1)]


    own_spec = pl.BlockSpec((TILE, HEAD_DIM), lambda i, h: (i, h))
    base = reach * n_tiles - tile_reach

    def col_spec(off):
        return pl.BlockSpec((TILE, HEAD_DIM), lambda i, h: (i, h + off))

    def kwin_spec(j, off):
        return pl.BlockSpec((TILE, HEAD_DIM), lambda i, h: (base + i + j, h + off))

    def qwin_spec(j, off):
        return pl.BlockSpec((TILE, HEAD_DIM), lambda i, h: (i + j, h + off))

    def ldwin_spec(j):
        return pl.BlockSpec((None, 2, TILE), lambda i, h: (h, 0, i + j))

    bias_spec = pl.BlockSpec((TILE, span), lambda i, h: (i, 0))
    ld_spec = pl.BlockSpec((None, 2, TILE), lambda i, h: (h, 0, i))
    params = pltpu.CompilerParams(dimension_semantics=("arbitrary", "arbitrary"))
    grid = (n_tiles, heads_p)

    def query_side(window, i_off, count, w_base):
        def gcol(extra):
            return pl.BlockSpec((TILE, HEAD_DIM), lambda i, h: (i + i_off, h + extra))

        def gwin(j, extra):
            return pl.BlockSpec((TILE, HEAD_DIM), lambda i, h: (w_base + i + j, h + extra))

        return pl.pallas_call(
            _query_side_kernel(nblk, scale),
            out_shape=(
                jax.ShapeDtypeStruct((count * TILE, width), jnp.bfloat16),
                jax.ShapeDtypeStruct((heads_p, 2, count * TILE), jnp.float32),
            ),
            grid=(count, heads_p),
            in_specs=[gcol(0), gcol(heads_p)] + [gwin(j, 0) for j in range(nblk)]
            + [gwin(j, heads_p) for j in range(nblk)]
            + [pl.BlockSpec((TILE, span), lambda i, h: (i + i_off, 0))],
            out_specs=(own_spec, ld_spec),
            compiler_params=params,
            name="attn_query_side",
        )(qd, qd, *([window] * (2 * nblk)), q_bias)

    def query_side_pieces(pieces, i_off, count):
        layout, specs, args = [], [], []
        for extra in (0, heads_p):
            for j in range(nblk):
                starts = []
                for arr, first, n in pieces:
                    if first <= j + count - 1 and j <= first + n - 1:
                        starts.append(first)
                        specs.append(pl.BlockSpec(
                            (TILE, HEAD_DIM),
                            lambda i, h, j=j, first=first, n=n, extra=extra:
                                (jnp.clip(i + j - first, 0, n - 1), h + extra)))
                        args.append(arr)
                if extra == 0:
                    layout.append(starts)
        return pl.pallas_call(
            _query_side_kernel(nblk, scale, layout),
            out_shape=(
                jax.ShapeDtypeStruct((count * TILE, width), jnp.bfloat16),
                jax.ShapeDtypeStruct((heads_p, 2, count * TILE), jnp.float32),
            ),
            grid=(count, heads_p),
            in_specs=[pl.BlockSpec((TILE, HEAD_DIM), lambda i, h: (i + i_off, h)),
                      pl.BlockSpec((TILE, HEAD_DIM), lambda i, h: (i + i_off, h + heads_p))]
            + specs + [pl.BlockSpec((TILE, span), lambda i, h: (i + i_off, 0))],
            out_specs=(own_spec, ld_spec),
            compiler_params=params,
            name="attn_query_side",
        )(qd, qd, *args, q_bias)

    if split:
        late = n_tiles // 2
        h_t = half // TILE
        dq_late, ld_late = query_side_pieces([(prev_late, 0, h_t), (kv, h_t, n_tiles)], late, n_tiles - late)
        dq_late, ld_late, prev_early = lax.optimization_barrier((dq_late, ld_late, prev_early))
        dq_early, ld_early = query_side_pieces(
            [(prev_early, 0, h_t), (prev_late, h_t, h_t), (kv, 2 * h_t, n_tiles)], 0, late)
        dq = jnp.concatenate([dq_early, dq_late], axis=0)
        ld = jnp.concatenate([ld_early, ld_late], axis=2)
    else:
        dq, ld = query_side(kv_win, 0, n_tiles, base)

    ld_parts = [ld]
    for shift in range(1, reach + 1):
        ld_parts.append(shifted(ld, "chi", -shift))
    ld_win = jnp.concatenate(ld_parts, axis=2)

    def from_plane(x):
        return lax.all_to_all(x, "clo", split_axis=0, concat_axis=1, tiled=True)

    groups = 2 if heads_p % 2 == 0 else 1
    hg = heads_p // groups
    dkv_parts = []
    for g in range(groups):
        off = g * hg

        def gcol(extra, off=off):
            return pl.BlockSpec((TILE, HEAD_DIM), lambda i, h: (i, h + off + extra))

        def gwin(j, extra, off=off):
            return pl.BlockSpec((TILE, HEAD_DIM), lambda i, h: (i + j, h + off + extra))

        def gld(j, off=off):
            return pl.BlockSpec((None, 2, TILE), lambda i, h: (h + off, 0, i + j))

        layout, q_specs, q_args = [], [], []
        for extra in (0, heads_p):
            for j in range(nblk):
                starts = []
                for p, arr in enumerate(qd_parts):
                    first = p * n_tiles
                    if first <= j + n_tiles - 1 and j <= first + n_tiles - 1:
                        starts.append(first)
                        q_specs.append(pl.BlockSpec(
                            (TILE, HEAD_DIM),
                            lambda i, h, j=j, first=first, extra=extra, off=off:
                                (jnp.clip(i + j - first, 0, n_tiles - 1), h + off + extra)))
                        q_args.append(arr)
                if extra == 0:
                    layout.append(starts)
        ld_specs, ld_args = [], []
        for j in range(nblk):
            for p, arr in enumerate(ld_parts):
                first = p * n_tiles
                if first <= j + n_tiles - 1 and j <= first + n_tiles - 1:
                    ld_specs.append(pl.BlockSpec(
                        (None, 2, TILE),
                        lambda i, h, j=j, first=first, off=off:
                            (h + off, 0, jnp.clip(i + j - first, 0, n_tiles - 1))))
                    ld_args.append(arr)

        dkv_g = pl.pallas_call(
            _key_side_kernel(nblk, scale, layout),
            out_shape=jax.ShapeDtypeStruct((plane, 2 * hg * HEAD_DIM), jnp.bfloat16),
            grid=(n_tiles, hg),
            in_specs=[gcol(0), gcol(heads_p)] + q_specs + ld_specs + [bias_spec],
            out_specs=pl.BlockSpec((TILE, 2 * HEAD_DIM), lambda i, h: (i, h)),
            compiler_params=params,
            name="attn_key_side",
        )(kv, kv, *q_args, *ld_args, k_bias)
        dkv_parts.append(from_plane(dkv_g).reshape(-1, clo_n, 1, hg, 2, HEAD_DIM))

    dkv = jnp.concatenate(dkv_parts, axis=2)
    rows = dkv.shape[0]
    attn_dk = dkv[:, :, :, :, 0, :].reshape(rows, clo_n * width)
    attn_dv = dkv[:, :, :, :, 1, :].reshape(rows, clo_n * width)
    return (from_plane(dq), attn_dk, attn_dv)


def solution(mesh):
    ctx_n, head_n = mesh.devices.shape
    def fn(attn_q, attn_k, attn_v, attn_dout, doc_ids):
        tok_in = attn_q.shape[0] // (ctx_n * head_n)
        clo_n = _plan(tok_in, ctx_n, head_n)
        chi_n = ctx_n // clo_n
        sub = Mesh(np.asarray(mesh.devices).reshape(chi_n, clo_n, head_n), ("chi", "clo", "head"))
        inner = jax.shard_map(
            lambda *a: _per_device(clo_n, *a),
            mesh=sub,
            in_specs=(
                P(("chi", "clo", "head"), None),
                P(("chi", "clo", "head"), None),
                P(("chi", "clo", "head"), None),
                P(("chi", "clo", "head"), None),
                P(),
            ),
            out_specs=(P(("chi", "clo"), "head"), P(("chi", "clo"), "head"), P(("chi", "clo"), "head")),
            check_vma=False,
        )
        return inner(attn_q, attn_k, attn_v, attn_dout, doc_ids)
    return fn
```
